32 devices in a mesh: groups: 2 (over y), tm: 4 (over z), face: 4 (over x, core).
Axes of the slice: x: 2, y: 2, z: 4, core: 2. Of those that a mesh axis runs over, the one named last changes fastest.
Arguments:
- latents: bfloat16 [8, 4, 896, 1152], P(('groups', 'tm'), 'face'), parts along dimension 0, may hold values from -6 to 6
- modulation: float32 [6, 1152], P('groups'), parts along dimension 0, may hold values from -3 to 3
- w_qkv: bfloat16 [1152, 1728], P('face'), as said below
- w_out: bfloat16 [576, 1152], P(None, 'face'), may hold values from -0.25 to 0.25
- edge_table: int32 [4, 4, 4], replicated, may hold values from 0 to 3, as said below
- space_ramp: int32 [2], replicated, may hold values from 1 to 8, as said below
- time_ramp: int32 [4], replicated, may hold values from 1 to 8, as said below
Outputs:
- blended: bfloat16 [8, 4, 896, 1152], P(('groups', 'tm'), 'face'), parts along dimension 0
The draws below stay inside these ranges and needn't reach their ends.
There are 2 independent parts, one for each index of `groups`. The reference program is written for one: setup_inputs(seed, part) draws one part's arguments, and reference() takes and returns one part's arrays. A program takes and returns all parts, laid end to end along the dimension named above; an argument that names none is the same for every part. Nothing has to cross between parts.
Inputs may be any that keep to these rules, and one draw needn't show every extreme that they name: Row edge_table[g, e] = (p, e2, flip, route): route r in 0..3 names an offset o = 1, -1, 2, -2 with p = (g + o) mod 4; the four edges of a tile take the four routes; row edge_table[p, e2] points back to (g, e) with the same flip (0 or 1) and the route of the opposite offset. `space_ramp`: distinct positive integers, one of them 8. `time_ramp`: distinct positive integers, one of them 8. `w_qkv`: projection weights of order 1152 ** -0.5 in most heads.
All inputs are finite; a program needn't handle non-finite values.
Results may differ from the reference program's by a relative error of at most 0.0046.
Values may be sent and summed in bfloat16 or wider, within the bound.
No kernel may reach another device: no remote copies, remote signals or barrier semaphores. Data moves between devices by JAX's collectives and lax.ppermute only.
A program may use at most 64 MiB of HBM per device.

```python
import math
import jax
import jax.numpy as jnp
from jax import lax

D = 1152
HD = 72
HEADS = 8
S = 8
OVS = 2
OVT = 4
F = 14
TOK = 896
TILES = 4
SPANS = 4


def draw_w_qkv(key, part):
    key_values = jax.random.fold_in(key, 0)
    hidden_width = HEADS * HD
    values = jax.random.truncated_normal(key_values, -6.0, 6.0, (D, 3 * hidden_width), jnp.float32) * D ** (-0.5)
    return values.astype(jnp.bfloat16)


def draw_edge_table(key, part):
    key_roles, key_near, key_far = jax.random.split(key, 3)
    scores = jax.random.randint(key_roles, (TILES, 4), 0, 1 << 20) * 4 + jnp.arange(4, dtype=jnp.int32)[None, :]
    roles = jnp.argsort(scores, axis=1).astype(jnp.int32)
    flip_near = jax.random.randint(key_near, (TILES,), 0, 2)
    flip_far = jax.random.randint(key_far, (TILES,), 0, 2)
    tile_ids = jnp.arange(TILES, dtype=jnp.int32)
    offsets = jnp.array([1, -1, 2, -2], jnp.int32)
    partner_route = jnp.array([1, 0, 3, 2], jnp.int32)
    partner = (tile_ids[:, None] + offsets[None, :]) % TILES
    partner_edge = roles[partner, partner_route[None, :]]
    flips = jnp.stack([flip_near, flip_near[(tile_ids - 1) % TILES], flip_far, flip_far[(tile_ids - 2) % TILES]], axis=1)
    route_ids = jnp.broadcast_to(jnp.arange(4, dtype=jnp.int32)[None, :], (TILES, 4))
    by_route = jnp.stack([partner, partner_edge, flips, route_ids], axis=2)
    onehot = (roles[:, :, None] == jnp.arange(4, dtype=jnp.int32)[None, None, :]).astype(jnp.int32)
    table = jnp.sum(onehot[:, :, :, None] * by_route[:, :, None, :], axis=1)
    return table.astype(jnp.int32)


def distinct_ramp(key, count):
    key_pick, key_order = jax.random.split(key)
    others = jax.random.permutation(key_pick, jnp.arange(1, 8, dtype=jnp.int32))[:count - 1]
    values = jnp.concatenate([others, jnp.array([8], jnp.int32)])
    return jax.random.permutation(key_order, values).astype(jnp.int32)


def draw_space_ramp(key, part):
    return distinct_ramp(jax.random.fold_in(key, 11), OVS)


def draw_time_ramp(key, part):
    return distinct_ramp(jax.random.fold_in(key, 23), OVT)


def steps_of(rng, dims, cuts, smallest, largest):
    def one(position, shards_of):
        draws = jax.random.uniform(jax.random.fold_in(jax.random.fold_in(rng, 6), position), (shards_of,), jnp.float32, smallest / len(cuts), largest / len(cuts))
        return jnp.repeat(jnp.exp(draws), dims[position] // shards_of).reshape((-1,) + (1,) * (len(dims) - position - 1))

    loudness = one(*cuts[0])
    for cut in cuts[1:]:
        loudness = loudness * one(*cut)
    return loudness


def bell_draw(rng, dims, scale, bound, cuts=(), kind=jnp.bfloat16):
    result = jax.random.normal(rng, dims, jnp.float32) * scale
    if len(cuts) > 0:
        result = steps_of(rng, dims, cuts, -0.22, 0.18) * result
    return jnp.clip(result, min=-bound, max=bound).astype(kind)


def setup_inputs(seed: int = 0, part: int = 0) -> dict:
    streams_of = jax.random.split(jax.random.key(seed), 8)
    part_keys = jax.random.split(jax.random.fold_in(streams_of[7], part), 8)
    return {
        "latents": bell_draw(part_keys[0], (SPANS, TILES, TOK, D), 1.0, 6.0, ((0, 4), (1, 4))),
        "modulation": bell_draw(part_keys[1], (3, D), 0.5, 3.0, (), jnp.float32),
        "w_qkv": draw_w_qkv(jax.random.fold_in(streams_of[7], 71), part),
        "w_out": bell_draw(streams_of[3], (HEADS * HD, D), (HEADS * HD) ** -0.5, 0.25, ((1, 4),)),
        "edge_table": draw_edge_table(jax.random.fold_in(streams_of[7], 71), part),
        "space_ramp": draw_space_ramp(jax.random.fold_in(streams_of[7], 71), part),
        "time_ramp": draw_time_ramp(jax.random.fold_in(streams_of[7], 71), part),
    }


NORM_EPS = 1e-06

def modulate(block_in, modulation):
    values = block_in.astype(jnp.float32)
    center = lax.optimization_barrier(jnp.mean(values, axis=-1, keepdims=True))
    spread = lax.optimization_barrier(jnp.mean(jnp.square(values - center), axis=-1, keepdims=True))
    normed = (values - center) * lax.rsqrt(spread + NORM_EPS)
    return (normed * (1.0 + modulation[1]) + modulation[0]).astype(jnp.bfloat16)

def attend(qkv_all, head_count, head_size):
    tokens = qkv_all.shape[0]
    stacked = qkv_all.reshape(tokens, 3, head_count, head_size).transpose(1, 2, 0, 3)

    def one_head(operands):
        queries, keyset, valset = operands
        scores = jnp.dot(queries, keyset.T, preferred_element_type=jnp.float32) * (1.0 / math.sqrt(head_size))
        row_max = lax.optimization_barrier(jnp.max(scores, axis=-1, keepdims=True))
        weights = jnp.exp(scores - row_max)
        row_sum = lax.optimization_barrier(jnp.sum(weights, axis=-1, keepdims=True))
        probabilities = (weights / row_sum).astype(jnp.bfloat16)
        return jnp.dot(probabilities, valset, preferred_element_type=jnp.float32).astype(jnp.bfloat16)
    outputs = lax.map(one_head, (stacked[0], stacked[1], stacked[2]))
    return outputs.transpose(1, 0, 2).reshape(tokens, head_count * head_size)

def tile_block(block_in, modulation, w_qkv, w_out):
    moved = modulate(block_in, modulation)
    qkv_all = jnp.dot(moved, w_qkv, preferred_element_type=jnp.float32).astype(jnp.bfloat16)
    mixed = attend(qkv_all, HEADS, HD)
    projected = jnp.dot(mixed, w_out, preferred_element_type=jnp.float32)
    return (block_in.astype(jnp.float32) + modulation[2] * projected).astype(jnp.bfloat16)

def take_strips(block):
    extent = block.shape[1]
    middle = slice(OVS, extent - OVS)
    upper_rim = block[:, :OVS, middle]
    lower_rim = block[:, extent - OVS:, middle][:, ::-1]
    left_rim = jnp.swapaxes(block[:, middle, :OVS], 1, 2)
    right_rim = jnp.swapaxes(block[:, middle, extent - OVS:][:, :, ::-1], 1, 2)
    return jnp.stack([upper_rim, lower_rim, left_rim, right_rim])

def put_strips(block, strips):
    extent = block.shape[1]
    middle = slice(OVS, extent - OVS)
    block = block.at[:, :OVS, middle].set(strips[0])
    block = block.at[:, extent - OVS:, middle].set(strips[1][:, ::-1])
    block = block.at[:, middle, :OVS].set(jnp.swapaxes(strips[2], 1, 2))
    block = block.at[:, middle, extent - OVS:].set(jnp.swapaxes(strips[3], 1, 2)[:, :, ::-1])
    return block

def space_blend(own, incoming, flip_bits, space_ramp):
    ramp = space_ramp.astype(jnp.float32)
    weight_own = (ramp / (ramp + ramp[::-1]))[None, None, :, None, None]
    weight_far = (ramp[::-1] / (ramp + ramp[::-1]))[None, None, :, None, None]
    own_strips = take_strips(own)
    mapped = incoming.astype(jnp.float32)[:, :, ::-1]
    mapped = jnp.where(flip_bits[:, None, None, None, None] > 0, mapped[:, :, :, ::-1], mapped)
    return put_strips(own, weight_own * own_strips + weight_far * mapped)

def time_blend(own, lower, upper, has_lower, has_upper, time_ramp):
    ramp = time_ramp.astype(jnp.float32)
    shape_rim = (-1,) + (1,) * (own.ndim - 1)
    weight_own = (ramp / (ramp + ramp[::-1])).reshape(shape_rim)
    weight_far = (ramp[::-1] / (ramp + ramp[::-1])).reshape(shape_rim)
    frames = own.shape[0]
    low_mix = jnp.where(has_lower, weight_own * own[:OVT] + weight_far * lower, own[:OVT])
    high_mix = jnp.where(has_upper, weight_own[::-1] * own[frames - OVT:] + weight_far[::-1] * upper, own[frames - OVT:])
    return own.at[:OVT].set(low_mix).at[frames - OVT:].set(high_mix)

def reference(latents, modulation, w_qkv, w_out, edge_table, space_ramp, time_ramp):
    flat = latents.reshape(SPANS * TILES, TOK, D)

    def run_tile(block_in):
        return tile_block(block_in, modulation, w_qkv, w_out)
    outputs = lax.map(run_tile, flat).reshape(SPANS, TILES, F, S, S, D)
    partner_tile = edge_table[:, :, 0]
    partner_edge = edge_table[:, :, 1]
    flip_bits = edge_table[:, :, 2]

    def space_span(span):
        strips = jax.vmap(take_strips)(span)
        incoming = strips[partner_tile, partner_edge]
        mixed = jax.vmap(space_blend, in_axes=(0, 0, 0, None))(span.astype(jnp.float32), incoming, flip_bits, space_ramp)
        return mixed.astype(jnp.bfloat16)
    spaced = lax.map(space_span, outputs).astype(jnp.float32)
    zero_rim = jnp.zeros_like(spaced[:1, :, :OVT])
    lower = jnp.concatenate([zero_rim, spaced[:-1, :, F - OVT:]], axis=0)
    upper = jnp.concatenate([spaced[1:, :, :OVT], zero_rim], axis=0)
    span_ids = jnp.arange(SPANS)
    has_lower = span_ids > 0
    has_upper = span_ids < SPANS - 1
    inner_map = jax.vmap(time_blend, in_axes=(0, 0, 0, None, None, None))
    outer_map = jax.vmap(inner_map, in_axes=(0, 0, 0, 0, 0, None))
    blended = outer_map(spaced, lower, upper, has_lower, has_upper, time_ramp)
    return blended.reshape(SPANS, TILES, TOK, D).astype(jnp.bfloat16)
```

```python
import math

import jax
import jax.numpy as jnp
import numpy as np
from jax import lax
from jax.sharding import PartitionSpec as P

D = 1152
HD = 72
HEADS = 8
S = 8
OVS = 2
OVT = 4
MID = S - 2 * OVS


NORM_EPS = 1e-06
OFFSETS = (1, -1, 2, -2)
PARTNER_ROUTE = (1, 0, 3, 2)


def modulate(block_in, modulation):
    values = block_in.astype(jnp.float32)
    center = jnp.mean(values, axis=-1, keepdims=True)
    spread = jnp.mean(jnp.square(values - center), axis=-1, keepdims=True)
    normed = (values - center) * lax.rsqrt(spread + NORM_EPS)
    return (normed * (1.0 + modulation[1]) + modulation[0]).astype(jnp.bfloat16)


def attend(qkv_all, head_count, head_size):
    tokens = qkv_all.shape[0]
    stacked = qkv_all.reshape(tokens, 3, head_count, head_size).transpose(1, 2, 0, 3)

    def one_head(operands):
        queries, keyset, valset = operands
        scores = jnp.dot(queries, keyset.T, preferred_element_type=jnp.float32) * (
            1.0 / math.sqrt(head_size)
        )
        row_max = jnp.max(scores, axis=-1, keepdims=True)
        weights = jnp.exp(scores - row_max)
        row_sum = jnp.sum(weights, axis=-1, keepdims=True)
        probabilities = (weights / row_sum).astype(jnp.bfloat16)
        return jnp.dot(probabilities, valset, preferred_element_type=jnp.float32).astype(
            jnp.bfloat16
        )

    outputs = lax.map(one_head, (stacked[0], stacked[1], stacked[2]))
    return outputs.transpose(1, 0, 2).reshape(tokens, head_count * head_size)


def face_pieces(shard):
    n = lax.axis_size("face")
    me = lax.axis_index("face")

    def fetch(x, src_of):
        return lax.ppermute(x, "face", [(src_of(i), i) for i in range(n)])

    pieces = [(shard, me), (fetch(shard, lambda i: i ^ 1), me ^ 1)]
    for j in range(1, n // 2):
        far = fetch(shard, lambda i: (i + 2 * j) % n)
        pieces.append((far, (me + 2 * j) % n))
        pieces.append((fetch(far, lambda i: i ^ 1), ((me ^ 1) + 2 * j) % n))
    return pieces


def cell_token(edge, frame, depth, pos):
    row = jnp.where(edge == 0, depth, jnp.where(edge == 1, S - 1 - depth, OVS + pos))
    col = jnp.where(edge < 2, OVS + pos, jnp.where(edge == 2, depth, S - 1 - depth))
    return frame * (S * S) + row * S + col


def strip_depth(frames):
    grid = np.full((S, S), -1, np.int32)
    for d in range(OVS):
        grid[d, OVS : S - OVS] = d
        grid[S - 1 - d, OVS : S - OVS] = d
        grid[OVS : S - OVS, d] = d
        grid[OVS : S - OVS, S - 1 - d] = d
    return np.tile(grid.reshape(-1), frames)


def per_device(latents, modulation, w_qkv, w_out, edge_table, space_ramp, time_ramp):
    block_in = latents[0, 0]
    tokens = block_in.shape[0]
    frames = tokens // (S * S)
    n = lax.axis_size("face")
    rows = w_qkv.shape[0]
    moved = modulate(block_in, modulation)
    if n <= 4:
        moved_parts = moved.reshape(tokens, n, rows).transpose(1, 0, 2)
        qkv_sums = None
        for piece, index in face_pieces(w_qkv):
            part = jnp.dot(
                lax.dynamic_index_in_dim(moved_parts, index, 0, keepdims=False),
                piece,
                preferred_element_type=jnp.float32,
            )
            qkv_sums = part if qkv_sums is None else qkv_sums + part
    else:
        qkv_stack = jnp.zeros((n,) + w_qkv.shape, w_qkv.dtype)
        for piece, index in face_pieces(w_qkv):
            qkv_stack = lax.dynamic_update_index_in_dim(qkv_stack, piece, index, 0)
        w_qkv_full = qkv_stack.reshape(n * rows, w_qkv.shape[1])
        qkv_sums = jnp.dot(moved, w_qkv_full, preferred_element_type=jnp.float32)
    qkv_all = qkv_sums.astype(jnp.bfloat16)

    out_stack = jnp.zeros((n,) + w_out.shape, w_out.dtype)
    for piece, index in face_pieces(w_out):
        out_stack = lax.dynamic_update_index_in_dim(out_stack, piece, index, 0)
    w_out_full = out_stack.transpose(1, 0, 2).reshape(w_out.shape[0], n * w_out.shape[1])

    mixed = attend(qkv_all, HEADS, HD)
    projected = jnp.dot(mixed, w_out_full, preferred_element_type=jnp.float32)
    tile_out = (block_in.astype(jnp.float32) + modulation[2] * projected).astype(jnp.bfloat16)

    my_rows = lax.dynamic_index_in_dim(edge_table, lax.axis_index("face"), 0, keepdims=False)
    flips = my_rows[:, 2]
    routes = my_rows[:, 3]
    edge_ids = jnp.arange(4, dtype=jnp.int32)
    frame = jnp.arange(frames, dtype=jnp.int32)[:, None, None]
    depth = jnp.arange(OVS, dtype=jnp.int32)[None, :, None]
    pos = jnp.arange(MID, dtype=jnp.int32)[None, None, :]
    send_cells = []
    recv_cells = []
    for route_id in range(4):
        sender = jnp.sum(edge_ids * (routes == PARTNER_ROUTE[route_id]))
        flip = jnp.sum(flips * (edge_ids == sender))
        mapped_pos = jnp.where(flip > 0, MID - 1 - pos, pos)
        send_cells.append(cell_token(sender, frame, OVS - 1 - depth, mapped_pos).reshape(-1))
        target = jnp.sum(edge_ids * (routes == route_id))
        recv_cells.append(cell_token(target, frame, depth, pos).reshape(-1))
    token_ids = jnp.arange(tokens, dtype=jnp.int32)
    send_cells = jnp.concatenate(send_cells)
    recv_cells = jnp.concatenate(recv_cells)
    pick = (send_cells[:, None] == token_ids[None, :]).astype(jnp.bfloat16)
    outgoing = jnp.dot(pick, tile_out, preferred_element_type=jnp.float32).astype(jnp.bfloat16)
    strip_len = frames * OVS * MID
    arrived = []
    for route_id in range(4):
        sent = outgoing[route_id * strip_len : (route_id + 1) * strip_len]
        shift = -OFFSETS[route_id]
        arrived.append(
            lax.ppermute(sent, "face", [(i, (i + shift) % n) for i in range(n)])
        )
    arrived = jnp.concatenate(arrived, axis=0)
    place = (token_ids[:, None] == recv_cells[None, :]).astype(jnp.bfloat16)
    partner = jnp.dot(place, arrived, preferred_element_type=jnp.float32)

    ramp = space_ramp.astype(jnp.float32)
    keep = ramp / (ramp + ramp[::-1])
    take = ramp[::-1] / (ramp + ramp[::-1])
    dep = jnp.asarray(strip_depth(frames))
    in_strip = (dep >= 0)[:, None]
    dep_c = jnp.maximum(dep, 0)
    w_keep = keep[dep_c][:, None]
    w_take = take[dep_c][:, None]
    own = tile_out.astype(jnp.float32)
    spaced = jnp.where(in_strip, w_keep * own + w_take * partner, own).astype(jnp.bfloat16)

    rim = OVT * S * S
    low = spaced[:rim]
    high = spaced[tokens - rim :]
    count = lax.axis_size("tm")
    lower = lax.ppermute(high, "tm", [(i, i + 1) for i in range(count - 1)])
    upper = lax.ppermute(low, "tm", [(i + 1, i) for i in range(count - 1)])
    span_id = lax.axis_index("tm")
    has_lower = span_id > 0
    has_upper = span_id < count - 1
    tramp = time_ramp.astype(jnp.float32)
    hold = tramp / (tramp + tramp[::-1])
    pass_ = tramp[::-1] / (tramp + tramp[::-1])
    per_frame = jnp.arange(rim, dtype=jnp.int32) // (S * S)
    hold_low = hold[per_frame][:, None]
    pass_low = pass_[per_frame][:, None]
    hold_high = hold[OVT - 1 - per_frame][:, None]
    pass_high = pass_[OVT - 1 - per_frame][:, None]
    low_f = low.astype(jnp.float32)
    high_f = high.astype(jnp.float32)
    low_mix = jnp.where(has_lower, hold_low * low_f + pass_low * lower.astype(jnp.float32), low_f)
    high_mix = jnp.where(
        has_upper, hold_high * high_f + pass_high * upper.astype(jnp.float32), high_f
    )
    result = jnp.concatenate(
        [low_mix.astype(jnp.bfloat16), spaced[rim : tokens - rim], high_mix.astype(jnp.bfloat16)],
        axis=0,
    )
    return result.reshape(1, 1, tokens, D)


def solution(mesh):
    return jax.shard_map(
        per_device,
        mesh=mesh,
        in_specs=(
            P(("groups", "tm"), "face", None, None),
            P("groups", None),
            P("face", None),
            P(None, "face"),
            P(),
            P(),
            P(),
        ),
        out_specs=P(("groups", "tm"), "face", None, None),
        check_vma=False,
    )
```

```python
import math

import jax
import jax.numpy as jnp
import numpy as np
from jax import lax
from jax.sharding import PartitionSpec as P

D = 1152
HD = 72
HEADS = 8
S = 8
OVS = 2
OVT = 4
MID = S - 2 * OVS


NORM_EPS = 1e-06
OFFSETS = (1, -1, 2, -2)
PARTNER_ROUTE = (1, 0, 3, 2)


def modulate(block_in, modulation):
    values = block_in.astype(jnp.float32)
    center = jnp.mean(values, axis=-1, keepdims=True)
    spread = jnp.mean(jnp.square(values - center), axis=-1, keepdims=True)
    normed = (values - center) * lax.rsqrt(spread + NORM_EPS)
    return (normed * (1.0 + modulation[1]) + modulation[0]).astype(jnp.bfloat16)


def attend(qkv_all, head_count, head_size):
    tokens = qkv_all.shape[0]
    stacked = qkv_all.reshape(tokens, 3, head_count, head_size).transpose(1, 2, 0, 3)

    def one_head(operands):
        queries, keyset, valset = operands
        scores = jnp.dot(queries, keyset.T, preferred_element_type=jnp.float32) * (
            1.0 / math.sqrt(head_size)
        )
        row_max = jnp.max(scores, axis=-1, keepdims=True)
        weights = jnp.exp(scores - row_max)
        row_sum = jnp.sum(weights, axis=-1, keepdims=True)
        probabilities = (weights / row_sum).astype(jnp.bfloat16)
        return jnp.dot(probabilities, valset, preferred_element_type=jnp.float32).astype(
            jnp.bfloat16
        )

    outputs = lax.map(one_head, (stacked[0], stacked[1], stacked[2]))
    return outputs.transpose(1, 0, 2).reshape(tokens, head_count * head_size)


def face_pieces(shard):
    n = lax.axis_size("face")
    me = lax.axis_index("face")

    def fetch(x, src_of):
        return lax.ppermute(x, "face", [(src_of(i), i) for i in range(n)])

    pieces = [(shard, me), (fetch(shard, lambda i: i ^ 1), me ^ 1)]
    for j in range(1, n // 2):
        far = fetch(shard, lambda i: (i + 2 * j) % n)
        pieces.append((far, (me + 2 * j) % n))
        pieces.append((fetch(far, lambda i: i ^ 1), ((me ^ 1) + 2 * j) % n))
    return pieces


def strip_tables(frames):
    frame, depth, pos = np.meshgrid(
        np.arange(frames), np.arange(OVS), np.arange(MID), indexing="ij"
    )

    def token(edge, d, t):
        row = (d, S - 1 - d, OVS + t, OVS + t)[edge]
        col = (OVS + t, OVS + t, d, S - 1 - d)[edge]
        return (frame * (S * S) + row * S + col).reshape(-1)

    recv = np.stack([token(e, depth, pos) for e in range(4)])
    send = np.stack(
        [[token(e, OVS - 1 - depth, pos if flip == 0 else MID - 1 - pos) for flip in range(2)]
         for e in range(4)]
    )
    return recv.astype(np.int32), send.astype(np.int32)


def strip_depth(frames):
    grid = np.full((S, S), -1, np.int32)
    for d in range(OVS):
        grid[d, OVS : S - OVS] = d
        grid[S - 1 - d, OVS : S - OVS] = d
        grid[OVS : S - OVS, d] = d
        grid[OVS : S - OVS, S - 1 - d] = d
    return np.tile(grid.reshape(-1), frames)


def per_device(latents, modulation, w_qkv, w_out, edge_table, space_ramp, time_ramp):
    block_in = latents[0, 0]
    tokens = block_in.shape[0]
    frames = tokens // (S * S)
    n = lax.axis_size("face")
    rows = w_qkv.shape[0]
    moved = modulate(block_in, modulation)
    if n <= 4:
        moved_parts = moved.reshape(tokens, n, rows).transpose(1, 0, 2)
        qkv_sums = None
        for piece, index in face_pieces(w_qkv):
            part = jnp.dot(
                lax.dynamic_index_in_dim(moved_parts, index, 0, keepdims=False),
                piece,
                preferred_element_type=jnp.float32,
            )
            qkv_sums = part if qkv_sums is None else qkv_sums + part
    else:
        qkv_stack = jnp.zeros((n,) + w_qkv.shape, w_qkv.dtype)
        for piece, index in face_pieces(w_qkv):
            qkv_stack = lax.dynamic_update_index_in_dim(qkv_stack, piece, index, 0)
        w_qkv_full = qkv_stack.reshape(n * rows, w_qkv.shape[1])
        qkv_sums = jnp.dot(moved, w_qkv_full, preferred_element_type=jnp.float32)
    qkv_all = qkv_sums.astype(jnp.bfloat16)

    out_stack = jnp.zeros((n,) + w_out.shape, w_out.dtype)
    for piece, index in face_pieces(w_out):
        out_stack = lax.dynamic_update_index_in_dim(out_stack, piece, index, 0)
    w_out_full = out_stack.transpose(1, 0, 2).reshape(w_out.shape[0], n * w_out.shape[1])

    mixed = attend(qkv_all, HEADS, HD)
    projected = jnp.dot(mixed, w_out_full, preferred_element_type=jnp.float32)
    tile_out = (block_in.astype(jnp.float32) + modulation[2] * projected).astype(jnp.bfloat16)

    my_rows = lax.dynamic_index_in_dim(edge_table, lax.axis_index("face"), 0, keepdims=False)
    flips = my_rows[:, 2]
    routes = my_rows[:, 3]
    recv_table, send_table = strip_tables(frames)
    send_by_edge = jnp.where(flips[:, None] > 0, send_table[:, 1], send_table[:, 0])
    send_match = routes[None, :] == jnp.asarray(PARTNER_ROUTE, jnp.int32)[:, None]
    send_cells = jnp.sum(jnp.where(send_match[:, :, None], send_by_edge[None], 0), axis=1)
    recv_match = routes[None, :] == jnp.arange(4, dtype=jnp.int32)[:, None]
    recv_cells = jnp.sum(jnp.where(recv_match[:, :, None], recv_table[None], 0), axis=1)
    send_cells = send_cells.reshape(-1)
    recv_cells = recv_cells.reshape(-1)
    token_ids = jnp.arange(tokens, dtype=jnp.int32)
    pick = (send_cells[:, None] == token_ids[None, :]).astype(jnp.bfloat16)
    outgoing = jnp.dot(pick, tile_out, preferred_element_type=jnp.float32).astype(jnp.bfloat16)
    strip_len = frames * OVS * MID
    arrived = []
    for route_id in range(4):
        sent = outgoing[route_id * strip_len : (route_id + 1) * strip_len]
        shift = -OFFSETS[route_id]
        arrived.append(
            lax.ppermute(sent, "face", [(i, (i + shift) % n) for i in range(n)])
        )
    arrived = jnp.concatenate(arrived, axis=0)
    place = (token_ids[:, None] == recv_cells[None, :]).astype(jnp.bfloat16)
    partner = jnp.dot(place, arrived, preferred_element_type=jnp.float32)

    ramp = space_ramp.astype(jnp.float32)
    keep = ramp / (ramp + ramp[::-1])
    take = ramp[::-1] / (ramp + ramp[::-1])
    dep = strip_depth(frames)[:, None]
    w_keep = jnp.where(dep == 0, keep[0], keep[1])
    w_take = jnp.where(dep == 0, take[0], take[1])
    in_strip = dep >= 0
    own = tile_out.astype(jnp.float32)
    spaced = jnp.where(in_strip, w_keep * own + w_take * partner, own).astype(jnp.bfloat16)

    rim = OVT * S * S
    low = spaced[:rim]
    high = spaced[tokens - rim :]
    count = lax.axis_size("tm")
    lower = lax.ppermute(high, "tm", [(i, i + 1) for i in range(count - 1)])
    upper = lax.ppermute(low, "tm", [(i + 1, i) for i in range(count - 1)])
    span_id = lax.axis_index("tm")
    has_lower = span_id > 0
    has_upper = span_id < count - 1
    tramp = time_ramp.astype(jnp.float32)
    hold = tramp / (tramp + tramp[::-1])
    pass_ = tramp[::-1] / (tramp + tramp[::-1])
    blocks = (OVT, S * S, D)
    low_f = low.astype(jnp.float32).reshape(blocks)
    high_f = high.astype(jnp.float32).reshape(blocks)
    hold_low = hold[:, None, None]
    pass_low = pass_[:, None, None]
    hold_high = hold[::-1][:, None, None]
    pass_high = pass_[::-1][:, None, None]
    low_mix = jnp.where(
        has_lower, hold_low * low_f + pass_low * lower.astype(jnp.float32).reshape(blocks), low_f
    ).reshape(rim, D)
    high_mix = jnp.where(
        has_upper, hold_high * high_f + pass_high * upper.astype(jnp.float32).reshape(blocks), high_f
    ).reshape(rim, D)
    result = jnp.concatenate(
        [low_mix.astype(jnp.bfloat16), spaced[rim : tokens - rim], high_mix.astype(jnp.bfloat16)],
        axis=0,
    )
    return result.reshape(1, 1, tokens, D)


def solution(mesh):
    return jax.shard_map(
        per_device,
        mesh=mesh,
        in_specs=(
            P(("groups", "tm"), "face", None, None),
            P("groups", None),
            P("face", None),
            P(None, "face"),
            P(),
            P(),
            P(),
        ),
        out_specs=P(("groups", "tm"), "face", None, None),
        check_vma=False,
    )
```

```python
import math

import jax
import jax.numpy as jnp
import numpy as np
from jax import lax
from jax.sharding import PartitionSpec as P

D = 1152
HD = 72
HEADS = 8
S = 8
OVS = 2
OVT = 4
MID = S - 2 * OVS


NORM_EPS = 1e-06
OFFSETS = (1, -1, 2, -2)
PARTNER_ROUTE = (1, 0, 3, 2)


def modulate(block_in, modulation):
    values = block_in.astype(jnp.float32)
    center = jnp.mean(values, axis=-1, keepdims=True)
    spread = jnp.mean(jnp.square(values - center), axis=-1, keepdims=True)
    normed = (values - center) * lax.rsqrt(spread + NORM_EPS)
    return (normed * (1.0 + modulation[1]) + modulation[0]).astype(jnp.bfloat16)


def attend(queries_all, keys_all, values_all, head_size):
    def one_head(operands):
        queries, keyset, valset = operands
        scores = jnp.dot(queries, keyset.T, preferred_element_type=jnp.float32) * (
            1.0 / math.sqrt(head_size)
        )
        row_max = jnp.max(scores, axis=-1, keepdims=True)
        weights = jnp.exp(scores - row_max)
        row_sum = jnp.sum(weights, axis=-1, keepdims=True)
        probabilities = (weights / row_sum).astype(jnp.bfloat16)
        return jnp.dot(probabilities, valset, preferred_element_type=jnp.float32).astype(
            jnp.bfloat16
        )

    outputs = lax.map(one_head, (queries_all, keys_all, values_all))
    heads, tokens, size = outputs.shape
    return outputs.transpose(1, 0, 2).reshape(tokens, heads * size)


def face_pieces(shard):
    n = lax.axis_size("face")
    me = lax.axis_index("face")

    def fetch(x, src_of):
        return lax.ppermute(x, "face", [(src_of(i), i) for i in range(n)])

    pieces = [(shard, me), (fetch(shard, lambda i: i ^ 1), me ^ 1)]
    for j in range(1, n // 2):
        far = fetch(shard, lambda i: (i + 2 * j) % n)
        pieces.append((far, (me + 2 * j) % n))
        pieces.append((fetch(far, lambda i: i ^ 1), ((me ^ 1) + 2 * j) % n))
    return pieces


def strip_tables(frames):
    frame, depth, pos = np.meshgrid(
        np.arange(frames), np.arange(OVS), np.arange(MID), indexing="ij"
    )

    def token(edge, d, t):
        row = (d, S - 1 - d, OVS + t, OVS + t)[edge]
        col = (OVS + t, OVS + t, d, S - 1 - d)[edge]
        return (frame * (S * S) + row * S + col).reshape(-1)

    recv = np.stack([token(e, depth, pos) for e in range(4)])
    send = np.stack(
        [[token(e, OVS - 1 - depth, pos if flip == 0 else MID - 1 - pos) for flip in range(2)]
         for e in range(4)]
    )
    return recv.astype(np.int32), send.astype(np.int32)


def strip_depth(frames):
    grid = np.full((S, S), -1, np.int32)
    for d in range(OVS):
        grid[d, OVS : S - OVS] = d
        grid[S - 1 - d, OVS : S - OVS] = d
        grid[OVS : S - OVS, d] = d
        grid[OVS : S - OVS, S - 1 - d] = d
    return np.tile(grid.reshape(-1), frames)


def per_device(latents, modulation, w_qkv, w_out, edge_table, space_ramp, time_ramp):
    block_in = latents[0, 0]
    tokens = block_in.shape[0]
    frames = tokens // (S * S)
    n = lax.axis_size("face")
    rows = w_qkv.shape[0]
    moved = modulate(block_in, modulation)
    if n <= 4:
        moved_parts = moved.reshape(tokens, n, rows).transpose(1, 0, 2)
        qkv_sums = None
        for piece, index in face_pieces(w_qkv):
            part = jnp.dot(
                lax.dynamic_index_in_dim(moved_parts, index, 0, keepdims=False),
                piece,
                preferred_element_type=jnp.float32,
            )
            qkv_sums = part if qkv_sums is None else qkv_sums + part
    else:
        qkv_stack = jnp.zeros((n,) + w_qkv.shape, w_qkv.dtype)
        for piece, index in face_pieces(w_qkv):
            qkv_stack = lax.dynamic_update_index_in_dim(qkv_stack, piece, index, 0)
        w_qkv_full = qkv_stack.reshape(n * rows, w_qkv.shape[1])
        qkv_sums = jnp.dot(moved, w_qkv_full, preferred_element_type=jnp.float32)
    qkv_all = qkv_sums.astype(jnp.bfloat16)

    out_stack = jnp.zeros((n,) + w_out.shape, w_out.dtype)
    for piece, index in face_pieces(w_out):
        out_stack = lax.dynamic_update_index_in_dim(out_stack, piece, index, 0)
    w_out_full = out_stack.transpose(1, 0, 2).reshape(w_out.shape[0], n * w_out.shape[1])

    stacked = qkv_all.reshape(tokens, 3, HEADS, HD).transpose(1, 2, 0, 3)
    rim = OVT * S * S
    queries = stacked[0]
    rim_queries = jnp.concatenate([queries[:, :rim], queries[:, tokens - rim :]], axis=1)
    mid_queries = queries[:, rim : tokens - rim]
    rim_in = jnp.concatenate([block_in[:rim], block_in[tokens - rim :]], axis=0)
    mid_in = block_in[rim : tokens - rim]

    def project(mixed, part_in):
        projected = jnp.dot(mixed, w_out_full, preferred_element_type=jnp.float32)
        return (part_in.astype(jnp.float32) + modulation[2] * projected).astype(jnp.bfloat16)

    my_rows = lax.dynamic_index_in_dim(edge_table, lax.axis_index("face"), 0, keepdims=False)
    flips = my_rows[:, 2]
    routes = my_rows[:, 3]
    send_match = routes[None, :] == jnp.asarray(PARTNER_ROUTE, jnp.int32)[:, None]
    recv_match = routes[None, :] == jnp.arange(4, dtype=jnp.int32)[:, None]
    ramp = space_ramp.astype(jnp.float32)
    keep = ramp / (ramp + ramp[::-1])
    take = ramp[::-1] / (ramp + ramp[::-1])

    def strips_out(tile_out):
        part_tokens = tile_out.shape[0]
        part_frames = part_tokens // (S * S)
        recv_table, send_table = strip_tables(part_frames)
        send_by_edge = jnp.where(flips[:, None] > 0, send_table[:, 1], send_table[:, 0])
        send_cells = jnp.sum(jnp.where(send_match[:, :, None], send_by_edge[None], 0), axis=1)
        send_cells = send_cells.reshape(-1)
        token_ids = jnp.arange(part_tokens, dtype=jnp.int32)
        pick = (send_cells[:, None] == token_ids[None, :]).astype(jnp.bfloat16)
        return jnp.dot(pick, tile_out, preferred_element_type=jnp.float32).astype(jnp.bfloat16)

    def strips_in(outgoing):
        strip_len = outgoing.shape[0] // 4
        arrived = []
        for route_id in range(4):
            sent = outgoing[route_id * strip_len : (route_id + 1) * strip_len]
            shift = -OFFSETS[route_id]
            arrived.append(
                lax.ppermute(sent, "face", [(i, (i + shift) % n) for i in range(n)])
            )
        return jnp.concatenate(arrived, axis=0)

    def space_blend(tile_out, arrived):
        part_tokens = tile_out.shape[0]
        part_frames = part_tokens // (S * S)
        recv_table, _ = strip_tables(part_frames)
        recv_cells = jnp.sum(jnp.where(recv_match[:, :, None], recv_table[None], 0), axis=1)
        recv_cells = recv_cells.reshape(-1)
        token_ids = jnp.arange(part_tokens, dtype=jnp.int32)
        place = (token_ids[:, None] == recv_cells[None, :]).astype(jnp.bfloat16)
        partner = jnp.dot(place, arrived, preferred_element_type=jnp.float32)
        dep = strip_depth(part_frames)[:, None]
        w_keep = jnp.where(dep == 0, keep[0], keep[1])
        w_take = jnp.where(dep == 0, take[0], take[1])
        own = tile_out.astype(jnp.float32)
        return jnp.where(dep >= 0, w_keep * own + w_take * partner, own).astype(jnp.bfloat16)

    keys_all, values_all = stacked[1], stacked[2]
    half = HEADS // 2
    tile_rim = project(attend(rim_queries, keys_all, values_all, HD), rim_in)
    outgoing_rim = strips_out(tile_rim)
    arrived_rim = strips_in(outgoing_rim)
    mid_first, outgoing_rim = lax.optimization_barrier((mid_queries[:half], outgoing_rim))
    heads_first = attend(mid_first, keys_all[:half], values_all[:half], HD)
    arrived_rim, heads_first = lax.optimization_barrier((arrived_rim, heads_first))
    spaced_rim = space_blend(tile_rim, arrived_rim)
    low, high = lax.optimization_barrier((spaced_rim[:rim], spaced_rim[rim:]))
    count = lax.axis_size("tm")
    lower = lax.ppermute(high, "tm", [(i, i + 1) for i in range(count - 1)])
    upper = lax.ppermute(low, "tm", [(i + 1, i) for i in range(count - 1)])
    mid_second, low, high = lax.optimization_barrier((mid_queries[half:], low, high))
    heads_second = attend(mid_second, keys_all[half:], values_all[half:], HD)
    tile_mid = project(jnp.concatenate([heads_first, heads_second], axis=1), mid_in)
    spaced_mid = space_blend(tile_mid, strips_in(strips_out(tile_mid)))

    span_id = lax.axis_index("tm")
    has_lower = span_id > 0
    has_upper = span_id < count - 1
    tramp = time_ramp.astype(jnp.float32)
    hold = tramp / (tramp + tramp[::-1])
    pass_ = tramp[::-1] / (tramp + tramp[::-1])
    blocks = (OVT, S * S, D)
    low_f = low.astype(jnp.float32).reshape(blocks)
    high_f = high.astype(jnp.float32).reshape(blocks)
    hold_low = hold[:, None, None]
    pass_low = pass_[:, None, None]
    hold_high = hold[::-1][:, None, None]
    pass_high = pass_[::-1][:, None, None]
    low_mix = jnp.where(
        has_lower, hold_low * low_f + pass_low * lower.astype(jnp.float32).reshape(blocks), low_f
    ).reshape(rim, D)
    high_mix = jnp.where(
        has_upper, hold_high * high_f + pass_high * upper.astype(jnp.float32).reshape(blocks), high_f
    ).reshape(rim, D)
    result = jnp.concatenate(
        [low_mix.astype(jnp.bfloat16), spaced_mid, high_mix.astype(jnp.bfloat16)], axis=0
    )
    return result.reshape(1, 1, tokens, D)


def solution(mesh):
    return jax.shard_map(
        per_device,
        mesh=mesh,
        in_specs=(
            P(("groups", "tm"), "face", None, None),
            P("groups", None),
            P("face", None),
            P(None, "face"),
            P(),
            P(),
            P(),
        ),
        out_specs=P(("groups", "tm"), "face", None, None),
        check_vma=False,
    )
```

```python
import math

import jax
import jax.numpy as jnp
import numpy as np
from jax import lax
from jax.experimental import pallas as pl
from jax.experimental.pallas import tpu as pltpu
from jax.sharding import PartitionSpec as P

D = 1152
HD = 72
HEADS = 8
S = 8
OVS = 2
OVT = 4
MID = S - 2 * OVS


NORM_EPS = 1e-06
OFFSETS = (1, -1, 2, -2)
PARTNER_ROUTE = (1, 0, 3, 2)


def modulate(block_in, modulation):
    values = block_in.astype(jnp.float32)
    center = jnp.mean(values, axis=-1, keepdims=True)
    spread = jnp.mean(jnp.square(values - center), axis=-1, keepdims=True)
    normed = (values - center) * lax.rsqrt(spread + NORM_EPS)
    return (normed * (1.0 + modulation[1]) + modulation[0]).astype(jnp.bfloat16)


def attention_kernel(q_ref, k_ref, v_ref, w_ref, x_ref, g_ref, o_ref, acc_ref):
    head = pl.program_id(1)

    @pl.when(head == 0)
    def _():
        acc_ref[...] = jnp.zeros_like(acc_ref)

    scores = lax.dot_general(
        q_ref[0], k_ref[0], (((1,), (1,)), ((), ())), preferred_element_type=jnp.float32
    ) * (1.0 / math.sqrt(HD))
    row_max = jnp.max(scores, axis=-1, keepdims=True)
    weights = jnp.exp(scores - row_max)
    row_sum = jnp.sum(weights, axis=-1, keepdims=True)
    probabilities = (weights / row_sum).astype(jnp.bfloat16)
    mixed = jnp.dot(probabilities, v_ref[0], preferred_element_type=jnp.float32).astype(
        jnp.bfloat16
    )
    acc_ref[...] += jnp.dot(mixed, w_ref[0], preferred_element_type=jnp.float32)

    @pl.when(head == pl.num_programs(1) - 1)
    def _():
        o_ref[...] = (x_ref[...].astype(jnp.float32) + g_ref[...] * acc_ref[...]).astype(
            o_ref.dtype
        )


def attend_project(stacked, w_out_full, block_in, gate):
    heads, tokens, size = stacked.shape[1:]
    width = block_in.shape[1]
    chunk = tokens // 2
    w_heads = w_out_full.reshape(heads, size, width)
    return pl.pallas_call(
        attention_kernel,
        grid=(tokens // chunk, heads),
        in_specs=[
            pl.BlockSpec((1, chunk, size), lambda i, h: (h, i, 0)),
            pl.BlockSpec((1, tokens, size), lambda i, h: (h, 0, 0)),
            pl.BlockSpec((1, tokens, size), lambda i, h: (h, 0, 0)),
            pl.BlockSpec((1, size, width), lambda i, h: (h, 0, 0)),
            pl.BlockSpec((chunk, width), lambda i, h: (i, 0)),
            pl.BlockSpec((1, width), lambda i, h: (0, 0)),
        ],
        out_specs=pl.BlockSpec((chunk, width), lambda i, h: (i, 0)),
        out_shape=jax.ShapeDtypeStruct(block_in.shape, block_in.dtype),
        scratch_shapes=[pltpu.VMEM((chunk, width), jnp.float32)],
        compiler_params=pltpu.CompilerParams(dimension_semantics=("arbitrary", "arbitrary")),
    )(stacked[0], stacked[1], stacked[2], w_heads, block_in, gate.reshape(1, width))


def face_pieces(shard):
    n = lax.axis_size("face")
    me = lax.axis_index("face")

    def fetch(x, src_of):
        return lax.ppermute(x, "face", [(src_of(i), i) for i in range(n)])

    pieces = [(shard, me), (fetch(shard, lambda i: i ^ 1), me ^ 1)]
    for j in range(1, n // 2):
        far = fetch(shard, lambda i: (i + 2 * j) % n)
        pieces.append((far, (me + 2 * j) % n))
        pieces.append((fetch(far, lambda i: i ^ 1), ((me ^ 1) + 2 * j) % n))
    return pieces


def strip_tables(frames):
    frame, depth, pos = np.meshgrid(
        np.arange(frames), np.arange(OVS), np.arange(MID), indexing="ij"
    )

    def token(edge, d, t):
        row = (d, S - 1 - d, OVS + t, OVS + t)[edge]
        col = (OVS + t, OVS + t, d, S - 1 - d)[edge]
        return (frame * (S * S) + row * S + col).reshape(-1)

    recv = np.stack([token(e, depth, pos) for e in range(4)])
    send = np.stack(
        [[token(e, OVS - 1 - depth, pos if flip == 0 else MID - 1 - pos) for flip in range(2)]
         for e in range(4)]
    )
    return recv.astype(np.int32), send.astype(np.int32)


def strip_depth(frames):
    grid = np.full((S, S), -1, np.int32)
    for d in range(OVS):
        grid[d, OVS : S - OVS] = d
        grid[S - 1 - d, OVS : S - OVS] = d
        grid[OVS : S - OVS, d] = d
        grid[OVS : S - OVS, S - 1 - d] = d
    return np.tile(grid.reshape(-1), frames)


def per_device(latents, modulation, w_qkv, w_out, edge_table, space_ramp, time_ramp):
    block_in = latents[0, 0]
    tokens = block_in.shape[0]
    frames = tokens // (S * S)
    n = lax.axis_size("face")
    rows = w_qkv.shape[0]
    moved = modulate(block_in, modulation)
    if n <= 4:
        moved_parts = moved.reshape(tokens, n, rows).transpose(1, 0, 2)
        qkv_sums = None
        for piece, index in face_pieces(w_qkv):
            part = jnp.dot(
                lax.dynamic_index_in_dim(moved_parts, index, 0, keepdims=False),
                piece,
                preferred_element_type=jnp.float32,
            )
            qkv_sums = part if qkv_sums is None else qkv_sums + part
    else:
        qkv_stack = jnp.zeros((n,) + w_qkv.shape, w_qkv.dtype)
        for piece, index in face_pieces(w_qkv):
            qkv_stack = lax.dynamic_update_index_in_dim(qkv_stack, piece, index, 0)
        w_qkv_full = qkv_stack.reshape(n * rows, w_qkv.shape[1])
        qkv_sums = jnp.dot(moved, w_qkv_full, preferred_element_type=jnp.float32)
    qkv_all = qkv_sums.astype(jnp.bfloat16)

    out_stack = jnp.zeros((n,) + w_out.shape, w_out.dtype)
    for piece, index in face_pieces(w_out):
        out_stack = lax.dynamic_update_index_in_dim(out_stack, piece, index, 0)
    w_out_full = out_stack.transpose(1, 0, 2).reshape(w_out.shape[0], n * w_out.shape[1])

    stacked = qkv_all.reshape(tokens, 3, HEADS, HD).transpose(1, 2, 0, 3)
    tile_out = attend_project(stacked, w_out_full, block_in, modulation[2])

    my_rows = lax.dynamic_index_in_dim(edge_table, lax.axis_index("face"), 0, keepdims=False)
    flips = my_rows[:, 2]
    routes = my_rows[:, 3]
    recv_table, send_table = strip_tables(frames)
    send_by_edge = jnp.where(flips[:, None] > 0, send_table[:, 1], send_table[:, 0])
    send_match = routes[None, :] == jnp.asarray(PARTNER_ROUTE, jnp.int32)[:, None]
    send_cells = jnp.sum(jnp.where(send_match[:, :, None], send_by_edge[None], 0), axis=1)
    recv_match = routes[None, :] == jnp.arange(4, dtype=jnp.int32)[:, None]
    recv_cells = jnp.sum(jnp.where(recv_match[:, :, None], recv_table[None], 0), axis=1)
    send_cells = send_cells.reshape(-1)
    recv_cells = recv_cells.reshape(-1)
    token_ids = jnp.arange(tokens, dtype=jnp.int32)
    pick = (send_cells[:, None] == token_ids[None, :]).astype(jnp.bfloat16)
    outgoing = jnp.dot(pick, tile_out, preferred_element_type=jnp.float32).astype(jnp.bfloat16)
    strip_len = frames * OVS * MID
    arrived = []
    for route_id in range(4):
        sent = outgoing[route_id * strip_len : (route_id + 1) * strip_len]
        shift = -OFFSETS[route_id]
        arrived.append(
            lax.ppermute(sent, "face", [(i, (i + shift) % n) for i in range(n)])
        )
    arrived = jnp.concatenate(arrived, axis=0)
    place = (token_ids[:, None] == recv_cells[None, :]).astype(jnp.bfloat16)
    partner = jnp.dot(place, arrived, preferred_element_type=jnp.float32)

    ramp = space_ramp.astype(jnp.float32)
    keep = ramp / (ramp + ramp[::-1])
    take = ramp[::-1] / (ramp + ramp[::-1])
    dep = strip_depth(frames)[:, None]
    w_keep = jnp.where(dep == 0, keep[0], keep[1])
    w_take = jnp.where(dep == 0, take[0], take[1])
    in_strip = dep >= 0
    own = tile_out.astype(jnp.float32)
    spaced = jnp.where(in_strip, w_keep * own + w_take * partner, own).astype(jnp.bfloat16)

    rim = OVT * S * S
    low = spaced[:rim]
    high = spaced[tokens - rim :]
    count = lax.axis_size("tm")
    lower = lax.ppermute(high, "tm", [(i, i + 1) for i in range(count - 1)])
    upper = lax.ppermute(low, "tm", [(i + 1, i) for i in range(count - 1)])
    span_id = lax.axis_index("tm")
    has_lower = span_id > 0
    has_upper = span_id < count - 1
    tramp = time_ramp.astype(jnp.float32)
    hold = tramp / (tramp + tramp[::-1])
    pass_ = tramp[::-1] / (tramp + tramp[::-1])
    blocks = (OVT, S * S, D)
    low_f = low.astype(jnp.float32).reshape(blocks)
    high_f = high.astype(jnp.float32).reshape(blocks)
    hold_low = hold[:, None, None]
    pass_low = pass_[:, None, None]
    hold_high = hold[::-1][:, None, None]
    pass_high = pass_[::-1][:, None, None]
    low_mix = jnp.where(
        has_lower, hold_low * low_f + pass_low * lower.astype(jnp.float32).reshape(blocks), low_f
    ).reshape(rim, D)
    high_mix = jnp.where(
        has_upper, hold_high * high_f + pass_high * upper.astype(jnp.float32).reshape(blocks), high_f
    ).reshape(rim, D)
    result = jnp.concatenate(
        [low_mix.astype(jnp.bfloat16), spaced[rim : tokens - rim], high_mix.astype(jnp.bfloat16)],
        axis=0,
    )
    return result.reshape(1, 1, tokens, D)


def solution(mesh):
    return jax.shard_map(
        per_device,
        mesh=mesh,
        in_specs=(
            P(("groups", "tm"), "face", None, None),
            P("groups", None),
            P("face", None),
            P(None, "face"),
            P(),
            P(),
            P(),
        ),
        out_specs=P(("groups", "tm"), "face", None, None),
        check_vma=False,
    )
```

```python
import math

import jax
import jax.numpy as jnp
import numpy as np
from jax import lax
from jax.experimental import pallas as pl
from jax.experimental.pallas import tpu as pltpu
from jax.sharding import PartitionSpec as P

D = 1152
HD = 72
HEADS = 8
S = 8
OVS = 2
OVT = 4
MID = S - 2 * OVS


NORM_EPS = 1e-06
OFFSETS = (1, -1, 2, -2)
PARTNER_ROUTE = (1, 0, 3, 2)


def modulate(block_in, modulation):
    values = block_in.astype(jnp.float32)
    center = jnp.mean(values, axis=-1, keepdims=True)
    spread = jnp.mean(jnp.square(values - center), axis=-1, keepdims=True)
    normed = (values - center) * lax.rsqrt(spread + NORM_EPS)
    return (normed * (1.0 + modulation[1]) + modulation[0]).astype(jnp.bfloat16)


def attention_kernel(q_ref, k_ref, v_ref, w_ref, x_ref, g_ref, o_ref, acc_ref):
    head = pl.program_id(1)

    @pl.when(head == 0)
    def _():
        acc_ref[...] = jnp.zeros_like(acc_ref)

    scores = lax.dot_general(
        q_ref[0], k_ref[0], (((1,), (1,)), ((), ())), preferred_element_type=jnp.float32
    ) * (1.0 / math.sqrt(HD))
    row_max = jnp.max(scores, axis=-1, keepdims=True)
    weights = jnp.exp(scores - row_max)
    row_sum = jnp.sum(weights, axis=-1, keepdims=True)
    probabilities = (weights * (1.0 / row_sum)).astype(jnp.bfloat16)
    mixed = jnp.dot(probabilities, v_ref[0], preferred_element_type=jnp.float32).astype(
        jnp.bfloat16
    )
    acc_ref[...] += jnp.dot(mixed, w_ref[...], preferred_element_type=jnp.float32)

    @pl.when(head == pl.num_programs(1) - 1)
    def _():
        o_ref[...] = (x_ref[...].astype(jnp.float32) + g_ref[...] * acc_ref[...]).astype(
            o_ref.dtype
        )


def attend_project(stacked, w_out_full, block_in, gate):
    heads, tokens, size = stacked.shape[1:]
    width = block_in.shape[1]
    chunk = tokens
    return pl.pallas_call(
        attention_kernel,
        grid=(tokens // chunk, heads),
        in_specs=[
            pl.BlockSpec((1, chunk, size), lambda i, h: (h, i, 0)),
            pl.BlockSpec((1, tokens, size), lambda i, h: (h, 0, 0)),
            pl.BlockSpec((1, tokens, size), lambda i, h: (h, 0, 0)),
            pl.BlockSpec((size, width), lambda i, h: (h, 0)),
            pl.BlockSpec((chunk, width), lambda i, h: (i, 0)),
            pl.BlockSpec((1, width), lambda i, h: (0, 0)),
        ],
        out_specs=pl.BlockSpec((chunk, width), lambda i, h: (i, 0)),
        out_shape=jax.ShapeDtypeStruct(block_in.shape, block_in.dtype),
        scratch_shapes=[pltpu.VMEM((chunk, width), jnp.float32)],
        compiler_params=pltpu.CompilerParams(dimension_semantics=("arbitrary", "arbitrary")),
    )(stacked[0], stacked[1], stacked[2], w_out_full, block_in, gate.reshape(1, width))


def face_pieces(shard):
    n = lax.axis_size("face")
    me = lax.axis_index("face")

    def fetch(x, src_of):
        return lax.ppermute(x, "face", [(src_of(i), i) for i in range(n)])

    pieces = [(shard, me), (fetch(shard, lambda i: i ^ 1), me ^ 1)]
    for j in range(1, n // 2):
        far = fetch(shard, lambda i: (i + 2 * j) % n)
        pieces.append((far, (me + 2 * j) % n))
        pieces.append((fetch(far, lambda i: i ^ 1), ((me ^ 1) + 2 * j) % n))
    return pieces


def strip_tables(frames):
    frame, depth, pos = np.meshgrid(
        np.arange(frames), np.arange(OVS), np.arange(MID), indexing="ij"
    )

    def token(edge, d, t):
        row = (d, S - 1 - d, OVS + t, OVS + t)[edge]
        col = (OVS + t, OVS + t, d, S - 1 - d)[edge]
        return (frame * (S * S) + row * S + col).reshape(-1)

    recv = np.stack([token(e, depth, pos) for e in range(4)])
    send = np.stack(
        [[token(e, OVS - 1 - depth, pos if flip == 0 else MID - 1 - pos) for flip in range(2)]
         for e in range(4)]
    )
    return recv.astype(np.int32), send.astype(np.int32)


def strip_depth(frames):
    grid = np.full((S, S), -1, np.int32)
    for d in range(OVS):
        grid[d, OVS : S - OVS] = d
        grid[S - 1 - d, OVS : S - OVS] = d
        grid[OVS : S - OVS, d] = d
        grid[OVS : S - OVS, S - 1 - d] = d
    return np.tile(grid.reshape(-1), frames)


def per_device(latents, modulation, w_qkv, w_out, edge_table, space_ramp, time_ramp):
    block_in = latents[0, 0]
    tokens = block_in.shape[0]
    frames = tokens // (S * S)
    n = lax.axis_size("face")
    rows = w_qkv.shape[0]
    moved = modulate(block_in, modulation)
    if n <= 4:
        moved_parts = moved.reshape(tokens, n, rows).transpose(1, 0, 2)
        qkv_sums = None
        for piece, index in face_pieces(w_qkv):
            part = jnp.dot(
                lax.dynamic_index_in_dim(moved_parts, index, 0, keepdims=False),
                piece,
                preferred_element_type=jnp.float32,
            )
            qkv_sums = part if qkv_sums is None else qkv_sums + part
    else:
        qkv_stack = jnp.zeros((n,) + w_qkv.shape, w_qkv.dtype)
        for piece, index in face_pieces(w_qkv):
            qkv_stack = lax.dynamic_update_index_in_dim(qkv_stack, piece, index, 0)
        w_qkv_full = qkv_stack.reshape(n * rows, w_qkv.shape[1])
        qkv_sums = jnp.dot(moved, w_qkv_full, preferred_element_type=jnp.float32)
    qkv_all = qkv_sums.astype(jnp.bfloat16)

    out_stack = jnp.zeros((n,) + w_out.shape, w_out.dtype)
    for piece, index in face_pieces(w_out):
        out_stack = lax.dynamic_update_index_in_dim(out_stack, piece, index, 0)
    w_out_full = out_stack.transpose(1, 0, 2).reshape(w_out.shape[0], n * w_out.shape[1])

    stacked = qkv_all.reshape(tokens, 3, HEADS, HD).transpose(1, 2, 0, 3)
    tile_out = attend_project(stacked, w_out_full, block_in, modulation[2])

    my_rows = lax.dynamic_index_in_dim(edge_table, lax.axis_index("face"), 0, keepdims=False)
    flips = my_rows[:, 2]
    routes = my_rows[:, 3]
    recv_table, send_table = strip_tables(frames)
    send_by_edge = jnp.where(flips[:, None] > 0, send_table[:, 1], send_table[:, 0])
    send_match = routes[None, :] == jnp.asarray(PARTNER_ROUTE, jnp.int32)[:, None]
    send_cells = jnp.sum(jnp.where(send_match[:, :, None], send_by_edge[None], 0), axis=1)
    recv_match = routes[None, :] == jnp.arange(4, dtype=jnp.int32)[:, None]
    recv_cells = jnp.sum(jnp.where(recv_match[:, :, None], recv_table[None], 0), axis=1)
    send_cells = send_cells.reshape(-1)
    recv_cells = recv_cells.reshape(-1)
    token_ids = jnp.arange(tokens, dtype=jnp.int32)
    pick = (send_cells[:, None] == token_ids[None, :]).astype(jnp.bfloat16)
    outgoing = jnp.dot(pick, tile_out, preferred_element_type=jnp.float32).astype(jnp.bfloat16)
    strip_len = frames * OVS * MID
    arrived = []
    for route_id in range(4):
        sent = outgoing[route_id * strip_len : (route_id + 1) * strip_len]
        shift = -OFFSETS[route_id]
        arrived.append(
            lax.ppermute(sent, "face", [(i, (i + shift) % n) for i in range(n)])
        )
    arrived = jnp.concatenate(arrived, axis=0)
    place = (token_ids[:, None] == recv_cells[None, :]).astype(jnp.bfloat16)
    partner = jnp.dot(place, arrived, preferred_element_type=jnp.float32)

    ramp = space_ramp.astype(jnp.float32)
    keep = ramp / (ramp + ramp[::-1])
    take = ramp[::-1] / (ramp + ramp[::-1])
    dep = strip_depth(frames)[:, None]
    w_keep = jnp.where(dep == 0, keep[0], keep[1])
    w_take = jnp.where(dep == 0, take[0], take[1])
    in_strip = dep >= 0
    own = tile_out.astype(jnp.float32)
    spaced = jnp.where(in_strip, w_keep * own + w_take * partner, own).astype(jnp.bfloat16)

    rim = OVT * S * S
    low = spaced[:rim]
    high = spaced[tokens - rim :]
    count = lax.axis_size("tm")
    lower = lax.ppermute(high, "tm", [(i, i + 1) for i in range(count - 1)])
    upper = lax.ppermute(low, "tm", [(i + 1, i) for i in range(count - 1)])
    span_id = lax.axis_index("tm")
    has_lower = span_id > 0
    has_upper = span_id < count - 1
    tramp = time_ramp.astype(jnp.float32)
    hold = tramp / (tramp + tramp[::-1])
    pass_ = tramp[::-1] / (tramp + tramp[::-1])
    blocks = (OVT, S * S, D)
    low_f = low.astype(jnp.float32).reshape(blocks)
    high_f = high.astype(jnp.float32).reshape(blocks)
    hold_low = hold[:, None, None]
    pass_low = pass_[:, None, None]
    hold_high = hold[::-1][:, None, None]
    pass_high = pass_[::-1][:, None, None]
    low_mix = jnp.where(
        has_lower, hold_low * low_f + pass_low * lower.astype(jnp.float32).reshape(blocks), low_f
    ).reshape(rim, D)
    high_mix = jnp.where(
        has_upper, hold_high * high_f + pass_high * upper.astype(jnp.float32).reshape(blocks), high_f
    ).reshape(rim, D)
    result = jnp.concatenate(
        [low_mix.astype(jnp.bfloat16), spaced[rim : tokens - rim], high_mix.astype(jnp.bfloat16)],
        axis=0,
    )
    return result.reshape(1, 1, tokens, D)


def solution(mesh):
    return jax.shard_map(
        per_device,
        mesh=mesh,
        in_specs=(
            P(("groups", "tm"), "face", None, None),
            P("groups", None),
            P("face", None),
            P(None, "face"),
            P(),
            P(),
            P(),
        ),
        out_specs=P(("groups", "tm"), "face", None, None),
        check_vma=False,
    )
```

```python
import math

import jax
import jax.numpy as jnp
import numpy as np
from jax import lax
from jax.experimental import pallas as pl
from jax.experimental.pallas import tpu as pltpu
from jax.sharding import PartitionSpec as P

D = 1152
HD = 72
HEADS = 8
S = 8
OVS = 2
OVT = 4
MID = S - 2 * OVS


NORM_EPS = 1e-06
OFFSETS = (1, -1, 2, -2)
PARTNER_ROUTE = (1, 0, 3, 2)


def modulate(block_in, modulation):
    values = block_in.astype(jnp.float32)
    center = jnp.mean(values, axis=-1, keepdims=True)
    spread = jnp.mean(jnp.square(values - center), axis=-1, keepdims=True)
    normed = (values - center) * lax.rsqrt(spread + NORM_EPS)
    return (normed * (1.0 + modulation[1]) + modulation[0]).astype(jnp.bfloat16)


def attention_kernel(q_ref, k_ref, v_ref, w_ref, x_ref, g_ref, o_ref, acc_ref):
    head = pl.program_id(1)

    @pl.when(head == 0)
    def _():
        acc_ref[...] = jnp.zeros_like(acc_ref)

    scores = lax.dot_general(
        q_ref[0], k_ref[0], (((1,), (1,)), ((), ())), preferred_element_type=jnp.float32
    ) * (1.0 / math.sqrt(HD))
    row_max = jnp.max(scores, axis=-1, keepdims=True)
    weights = jnp.exp(scores - row_max)
    row_sum = jnp.sum(weights, axis=-1, keepdims=True)
    probabilities = (weights * (1.0 / row_sum)).astype(jnp.bfloat16)
    mixed = jnp.dot(probabilities, v_ref[0], preferred_element_type=jnp.float32).astype(
        jnp.bfloat16
    )
    acc_ref[...] += jnp.dot(mixed, w_ref[...], preferred_element_type=jnp.float32)

    @pl.when(head == pl.num_programs(1) - 1)
    def _():
        o_ref[...] = (x_ref[...].astype(jnp.float32) + g_ref[...] * acc_ref[...]).astype(
            o_ref.dtype
        )


def attend_project(queries, keys, values, w_out_full, block_in, gate):
    heads, tokens, size = keys.shape
    chunk = queries.shape[1]
    width = block_in.shape[1]
    return pl.pallas_call(
        attention_kernel,
        grid=(1, heads),
        in_specs=[
            pl.BlockSpec((1, chunk, size), lambda i, h: (h, i, 0)),
            pl.BlockSpec((1, tokens, size), lambda i, h: (h, 0, 0)),
            pl.BlockSpec((1, tokens, size), lambda i, h: (h, 0, 0)),
            pl.BlockSpec((size, width), lambda i, h: (h, 0)),
            pl.BlockSpec((chunk, width), lambda i, h: (i, 0)),
            pl.BlockSpec((1, width), lambda i, h: (0, 0)),
        ],
        out_specs=pl.BlockSpec((chunk, width), lambda i, h: (i, 0)),
        out_shape=jax.ShapeDtypeStruct(block_in.shape, block_in.dtype),
        scratch_shapes=[pltpu.VMEM((chunk, width), jnp.float32)],
        compiler_params=pltpu.CompilerParams(dimension_semantics=("arbitrary", "arbitrary")),
    )(queries, keys, values, w_out_full, block_in, gate.reshape(1, width))


def face_pieces(shard):
    n = lax.axis_size("face")
    me = lax.axis_index("face")

    def fetch(x, src_of):
        return lax.ppermute(x, "face", [(src_of(i), i) for i in range(n)])

    pieces = [(shard, me), (fetch(shard, lambda i: i ^ 1), me ^ 1)]
    for j in range(1, n // 2):
        far = fetch(shard, lambda i: (i + 2 * j) % n)
        pieces.append((far, (me + 2 * j) % n))
        pieces.append((fetch(far, lambda i: i ^ 1), ((me ^ 1) + 2 * j) % n))
    return pieces


def strip_tables(frames):
    frame, depth, pos = np.meshgrid(
        np.arange(frames), np.arange(OVS), np.arange(MID), indexing="ij"
    )

    def token(edge, d, t):
        row = (d, S - 1 - d, OVS + t, OVS + t)[edge]
        col = (OVS + t, OVS + t, d, S - 1 - d)[edge]
        return (frame * (S * S) + row * S + col).reshape(-1)

    recv = np.stack([token(e, depth, pos) for e in range(4)])
    send = np.stack(
        [[token(e, OVS - 1 - depth, pos if flip == 0 else MID - 1 - pos) for flip in range(2)]
         for e in range(4)]
    )
    return recv.astype(np.int32), send.astype(np.int32)


def strip_depth(frames):
    grid = np.full((S, S), -1, np.int32)
    for d in range(OVS):
        grid[d, OVS : S - OVS] = d
        grid[S - 1 - d, OVS : S - OVS] = d
        grid[OVS : S - OVS, d] = d
        grid[OVS : S - OVS, S - 1 - d] = d
    return np.tile(grid.reshape(-1), frames)


def per_device(latents, modulation, w_qkv, w_out, edge_table, space_ramp, time_ramp):
    block_in = latents[0, 0]
    tokens = block_in.shape[0]
    frames = tokens // (S * S)
    n = lax.axis_size("face")
    rows = w_qkv.shape[0]
    moved = modulate(block_in, modulation)
    if n <= 4:
        moved_parts = moved.reshape(tokens, n, rows).transpose(1, 0, 2)
        qkv_sums = None
        for piece, index in face_pieces(w_qkv):
            part = jnp.dot(
                lax.dynamic_index_in_dim(moved_parts, index, 0, keepdims=False),
                piece,
                preferred_element_type=jnp.float32,
            )
            qkv_sums = part if qkv_sums is None else qkv_sums + part
    else:
        qkv_stack = jnp.zeros((n,) + w_qkv.shape, w_qkv.dtype)
        for piece, index in face_pieces(w_qkv):
            qkv_stack = lax.dynamic_update_index_in_dim(qkv_stack, piece, index, 0)
        w_qkv_full = qkv_stack.reshape(n * rows, w_qkv.shape[1])
        qkv_sums = jnp.dot(moved, w_qkv_full, preferred_element_type=jnp.float32)
    qkv_all = qkv_sums.astype(jnp.bfloat16)

    out_stack = jnp.zeros((n,) + w_out.shape, w_out.dtype)
    for piece, index in face_pieces(w_out):
        out_stack = lax.dynamic_update_index_in_dim(out_stack, piece, index, 0)
    w_out_full = out_stack.transpose(1, 0, 2).reshape(w_out.shape[0], n * w_out.shape[1])

    stacked = qkv_all.reshape(tokens, 3, HEADS, HD).transpose(1, 2, 0, 3)
    queries, keys, values = stacked[0], stacked[1], stacked[2]
    rim = OVT * S * S
    mid_a = rim + ((tokens - 2 * rim) // (2 * S * S)) * (S * S)
    gate = modulation[2]

    def tile_part(part_queries, part_in):
        return attend_project(part_queries, keys, values, w_out_full, part_in, gate)

    my_rows = lax.dynamic_index_in_dim(edge_table, lax.axis_index("face"), 0, keepdims=False)
    flips = my_rows[:, 2]
    routes = my_rows[:, 3]
    send_match = routes[None, :] == jnp.asarray(PARTNER_ROUTE, jnp.int32)[:, None]
    recv_match = routes[None, :] == jnp.arange(4, dtype=jnp.int32)[:, None]
    ramp = space_ramp.astype(jnp.float32)
    keep = ramp / (ramp + ramp[::-1])
    take = ramp[::-1] / (ramp + ramp[::-1])

    def strips_out(tile_out):
        part_tokens = tile_out.shape[0]
        part_frames = part_tokens // (S * S)
        _, send_table = strip_tables(part_frames)
        send_by_edge = jnp.where(flips[:, None] > 0, send_table[:, 1], send_table[:, 0])
        send_cells = jnp.sum(jnp.where(send_match[:, :, None], send_by_edge[None], 0), axis=1)
        send_cells = send_cells.reshape(-1)
        token_ids = jnp.arange(part_tokens, dtype=jnp.int32)
        pick = (send_cells[:, None] == token_ids[None, :]).astype(jnp.bfloat16)
        return jnp.dot(pick, tile_out, preferred_element_type=jnp.float32).astype(jnp.bfloat16)

    def strips_in(outgoing):
        strip_len = outgoing.shape[0] // 4
        arrived = []
        for route_id in range(4):
            sent = outgoing[route_id * strip_len : (route_id + 1) * strip_len]
            shift = -OFFSETS[route_id]
            arrived.append(
                lax.ppermute(sent, "face", [(i, (i + shift) % n) for i in range(n)])
            )
        return jnp.concatenate(arrived, axis=0)

    def space_blend(tile_out, arrived):
        part_tokens = tile_out.shape[0]
        part_frames = part_tokens // (S * S)
        recv_table, _ = strip_tables(part_frames)
        recv_cells = jnp.sum(jnp.where(recv_match[:, :, None], recv_table[None], 0), axis=1)
        recv_cells = recv_cells.reshape(-1)
        token_ids = jnp.arange(part_tokens, dtype=jnp.int32)
        place = (token_ids[:, None] == recv_cells[None, :]).astype(jnp.bfloat16)
        partner = jnp.dot(place, arrived, preferred_element_type=jnp.float32)
        dep = strip_depth(part_frames)[:, None]
        w_keep = jnp.where(dep == 0, keep[0], keep[1])
        w_take = jnp.where(dep == 0, take[0], take[1])
        own = tile_out.astype(jnp.float32)
        return jnp.where(dep >= 0, w_keep * own + w_take * partner, own).astype(jnp.bfloat16)

    rim_queries = jnp.concatenate([queries[:, :rim], queries[:, tokens - rim :]], axis=1)
    rim_in = jnp.concatenate([block_in[:rim], block_in[tokens - rim :]], axis=0)
    tile_rim = tile_part(rim_queries, rim_in)
    outgoing_rim = strips_out(tile_rim)
    arrived_rim = strips_in(outgoing_rim)
    first_queries, outgoing_rim = lax.optimization_barrier((queries[:, rim:mid_a], outgoing_rim))
    tile_first = tile_part(first_queries, block_in[rim:mid_a])
    arrived_rim, tile_first = lax.optimization_barrier((arrived_rim, tile_first))
    spaced_rim = space_blend(tile_rim, arrived_rim)
    low, high = lax.optimization_barrier((spaced_rim[:rim], spaced_rim[rim:]))
    count = lax.axis_size("tm")
    lower = lax.ppermute(high, "tm", [(i, i + 1) for i in range(count - 1)])
    upper = lax.ppermute(low, "tm", [(i + 1, i) for i in range(count - 1)])
    second_queries, low, high = lax.optimization_barrier(
        (queries[:, mid_a : tokens - rim], low, high)
    )
    tile_second = tile_part(second_queries, block_in[mid_a : tokens - rim])
    tile_mid = jnp.concatenate([tile_first, tile_second], axis=0)
    spaced_mid = space_blend(tile_mid, strips_in(strips_out(tile_mid)))

    span_id = lax.axis_index("tm")
    has_lower = span_id > 0
    has_upper = span_id < count - 1
    tramp = time_ramp.astype(jnp.float32)
    hold = tramp / (tramp + tramp[::-1])
    pass_ = tramp[::-1] / (tramp + tramp[::-1])
    blocks = (OVT, S * S, D)
    low_f = low.astype(jnp.float32).reshape(blocks)
    high_f = high.astype(jnp.float32).reshape(blocks)
    hold_low = hold[:, None, None]
    pass_low = pass_[:, None, None]
    hold_high = hold[::-1][:, None, None]
    pass_high = pass_[::-1][:, None, None]
    low_mix = jnp.where(
        has_lower, hold_low * low_f + pass_low * lower.astype(jnp.float32).reshape(blocks), low_f
    ).reshape(rim, D)
    high_mix = jnp.where(
        has_upper, hold_high * high_f + pass_high * upper.astype(jnp.float32).reshape(blocks), high_f
    ).reshape(rim, D)
    result = jnp.concatenate(
        [low_mix.astype(jnp.bfloat16), spaced_mid, high_mix.astype(jnp.bfloat16)], axis=0
    )
    return result.reshape(1, 1, tokens, D)


def solution(mesh):
    return jax.shard_map(
        per_device,
        mesh=mesh,
        in_specs=(
            P(("groups", "tm"), "face", None, None),
            P("groups", None),
            P("face", None),
            P(None, "face"),
            P(),
            P(),
            P(),
        ),
        out_specs=P(("groups", "tm"), "face", None, None),
        check_vma=False,
    )
```

```python
import math

import jax
import jax.numpy as jnp
import numpy as np
from jax import lax
from jax.experimental import pallas as pl
from jax.experimental.pallas import tpu as pltpu
from jax.sharding import PartitionSpec as P

D = 1152
HD = 72
HEADS = 8
S = 8
OVS = 2
OVT = 4
MID = S - 2 * OVS


NORM_EPS = 1e-06
OFFSETS = (1, -1, 2, -2)
PARTNER_ROUTE = (1, 0, 3, 2)


def modulate(block_in, modulation):
    values = block_in.astype(jnp.float32)
    center = jnp.mean(values, axis=-1, keepdims=True)
    spread = jnp.mean(jnp.square(values - center), axis=-1, keepdims=True)
    normed = (values - center) * lax.rsqrt(spread + NORM_EPS)
    return (normed * (1.0 + modulation[1]) + modulation[0]).astype(jnp.bfloat16)


def attention_kernel(q_ref, k_ref, v_ref, w_ref, x_ref, g_ref, o_ref, acc_ref):
    head = pl.program_id(1)

    @pl.when(head == 0)
    def _():
        acc_ref[...] = jnp.zeros_like(acc_ref)

    scores = jnp.dot(q_ref[0], k_ref[0], preferred_element_type=jnp.float32) * (
        1.0 / math.sqrt(HD)
    )
    row_max = jnp.max(scores, axis=-1, keepdims=True)
    weights = jnp.exp(scores - row_max)
    row_sum = jnp.sum(weights, axis=-1, keepdims=True)
    probabilities = (weights * (1.0 / row_sum)).astype(jnp.bfloat16)
    mixed = jnp.dot(probabilities, v_ref[0], preferred_element_type=jnp.float32).astype(
        jnp.bfloat16
    )
    acc_ref[...] += jnp.dot(mixed, w_ref[...], preferred_element_type=jnp.float32)

    @pl.when(head == pl.num_programs(1) - 1)
    def _():
        o_ref[...] = (x_ref[...].astype(jnp.float32) + g_ref[...] * acc_ref[...]).astype(
            o_ref.dtype
        )


def attend_project(queries, keys, values, w_out_full, block_in, gate):
    heads, size, tokens = keys.shape
    chunk = queries.shape[1]
    width = block_in.shape[1]
    return pl.pallas_call(
        attention_kernel,
        grid=(1, heads),
        in_specs=[
            pl.BlockSpec((1, chunk, size), lambda i, h: (h, i, 0)),
            pl.BlockSpec((1, size, tokens), lambda i, h: (h, 0, 0)),
            pl.BlockSpec((1, tokens, size), lambda i, h: (h, 0, 0)),
            pl.BlockSpec((size, width), lambda i, h: (h, 0)),
            pl.BlockSpec((chunk, width), lambda i, h: (i, 0)),
            pl.BlockSpec((1, width), lambda i, h: (0, 0)),
        ],
        out_specs=pl.BlockSpec((chunk, width), lambda i, h: (i, 0)),
        out_shape=jax.ShapeDtypeStruct(block_in.shape, block_in.dtype),
        scratch_shapes=[pltpu.VMEM((chunk, width), jnp.float32)],
        compiler_params=pltpu.CompilerParams(dimension_semantics=("arbitrary", "arbitrary")),
    )(queries, keys, values, w_out_full, block_in, gate.reshape(1, width))


def face_pieces(shard):
    n = lax.axis_size("face")
    me = lax.axis_index("face")

    def fetch(x, src_of):
        return lax.ppermute(x, "face", [(src_of(i), i) for i in range(n)])

    pieces = [(shard, me), (fetch(shard, lambda i: i ^ 1), me ^ 1)]
    for j in range(1, n // 2):
        far = fetch(shard, lambda i: (i + 2 * j) % n)
        pieces.append((far, (me + 2 * j) % n))
        pieces.append((fetch(far, lambda i: i ^ 1), ((me ^ 1) + 2 * j) % n))
    return pieces


def strip_tables(frames):
    frame, depth, pos = np.meshgrid(
        np.arange(frames), np.arange(OVS), np.arange(MID), indexing="ij"
    )

    def token(edge, d, t):
        row = (d, S - 1 - d, OVS + t, OVS + t)[edge]
        col = (OVS + t, OVS + t, d, S - 1 - d)[edge]
        return (frame * (S * S) + row * S + col).reshape(-1)

    recv = np.stack([token(e, depth, pos) for e in range(4)])
    send = np.stack(
        [[token(e, OVS - 1 - depth, pos if flip == 0 else MID - 1 - pos) for flip in range(2)]
         for e in range(4)]
    )
    return recv.astype(np.int32), send.astype(np.int32)


def strip_depth(frames):
    grid = np.full((S, S), -1, np.int32)
    for d in range(OVS):
        grid[d, OVS : S - OVS] = d
        grid[S - 1 - d, OVS : S - OVS] = d
        grid[OVS : S - OVS, d] = d
        grid[OVS : S - OVS, S - 1 - d] = d
    return np.tile(grid.reshape(-1), frames)


def per_device(latents, modulation, w_qkv, w_out, edge_table, space_ramp, time_ramp):
    block_in = latents[0, 0]
    tokens = block_in.shape[0]
    frames = tokens // (S * S)
    n = lax.axis_size("face")
    rows = w_qkv.shape[0]
    moved = modulate(block_in, modulation)
    if n <= 4:
        moved_parts = moved.reshape(tokens, n, rows).transpose(1, 0, 2)
        qkv_sums = None
        for piece, index in face_pieces(w_qkv):
            part = jnp.dot(
                lax.dynamic_index_in_dim(moved_parts, index, 0, keepdims=False),
                piece,
                preferred_element_type=jnp.float32,
            )
            qkv_sums = part if qkv_sums is None else qkv_sums + part
    else:
        qkv_stack = jnp.zeros((n,) + w_qkv.shape, w_qkv.dtype)
        for piece, index in face_pieces(w_qkv):
            qkv_stack = lax.dynamic_update_index_in_dim(qkv_stack, piece, index, 0)
        w_qkv_full = qkv_stack.reshape(n * rows, w_qkv.shape[1])
        qkv_sums = jnp.dot(moved, w_qkv_full, preferred_element_type=jnp.float32)
    qkv_all = qkv_sums.astype(jnp.bfloat16)

    out_stack = jnp.zeros((n,) + w_out.shape, w_out.dtype)
    for piece, index in face_pieces(w_out):
        out_stack = lax.dynamic_update_index_in_dim(out_stack, piece, index, 0)
    w_out_full = out_stack.transpose(1, 0, 2).reshape(w_out.shape[0], n * w_out.shape[1])

    split = qkv_all.reshape(tokens, 3, HEADS, HD)
    queries = split[:, 0].transpose(1, 0, 2)
    keys = split[:, 1].transpose(1, 2, 0)
    values = split[:, 2].transpose(1, 0, 2)
    rim = OVT * S * S
    mid_a = rim + ((tokens - 2 * rim) // (2 * S * S)) * (S * S)
    gate = modulation[2]

    def tile_part(part_queries, part_in):
        return attend_project(part_queries, keys, values, w_out_full, part_in, gate)

    my_rows = lax.dynamic_index_in_dim(edge_table, lax.axis_index("face"), 0, keepdims=False)
    flips = my_rows[:, 2]
    routes = my_rows[:, 3]
    send_match = routes[None, :] == jnp.asarray(PARTNER_ROUTE, jnp.int32)[:, None]
    recv_match = routes[None, :] == jnp.arange(4, dtype=jnp.int32)[:, None]
    ramp = space_ramp.astype(jnp.float32)
    keep = ramp / (ramp + ramp[::-1])
    take = ramp[::-1] / (ramp + ramp[::-1])

    def strips_out(tile_out):
        part_tokens = tile_out.shape[0]
        part_frames = part_tokens // (S * S)
        _, send_table = strip_tables(part_frames)
        send_by_edge = jnp.where(flips[:, None] > 0, send_table[:, 1], send_table[:, 0])
        send_cells = jnp.sum(jnp.where(send_match[:, :, None], send_by_edge[None], 0), axis=1)
        send_cells = send_cells.reshape(-1)
        token_ids = jnp.arange(part_tokens, dtype=jnp.int32)
        pick = (send_cells[:, None] == token_ids[None, :]).astype(jnp.bfloat16)
        return jnp.dot(pick, tile_out, preferred_element_type=jnp.float32).astype(jnp.bfloat16)

    def strips_in(outgoing):
        strip_len = outgoing.shape[0] // 4
        arrived = []
        for route_id in range(4):
            sent = outgoing[route_id * strip_len : (route_id + 1) * strip_len]
            shift = -OFFSETS[route_id]
            arrived.append(
                lax.ppermute(sent, "face", [(i, (i + shift) % n) for i in range(n)])
            )
        return jnp.concatenate(arrived, axis=0)

    def space_blend(tile_out, arrived):
        part_tokens = tile_out.shape[0]
        part_frames = part_tokens // (S * S)
        recv_table, _ = strip_tables(part_frames)
        recv_cells = jnp.sum(jnp.where(recv_match[:, :, None], recv_table[None], 0), axis=1)
        recv_cells = recv_cells.reshape(-1)
        token_ids = jnp.arange(part_tokens, dtype=jnp.int32)
        place = (token_ids[:, None] == recv_cells[None, :]).astype(jnp.bfloat16)
        partner = jnp.dot(place, arrived, preferred_element_type=jnp.float32)
        dep = strip_depth(part_frames)[:, None]
        w_keep = jnp.where(dep == 0, keep[0], keep[1])
        w_take = jnp.where(dep == 0, take[0], take[1])
        own = tile_out.astype(jnp.float32)
        return jnp.where(dep >= 0, w_keep * own + w_take * partner, own).astype(jnp.bfloat16)

    rim_queries = jnp.concatenate([queries[:, :rim], queries[:, tokens - rim :]], axis=1)
    rim_in = jnp.concatenate([block_in[:rim], block_in[tokens - rim :]], axis=0)
    tile_rim = tile_part(rim_queries, rim_in)
    outgoing_rim = strips_out(tile_rim)
    arrived_rim = strips_in(outgoing_rim)
    first_queries, outgoing_rim = lax.optimization_barrier((queries[:, rim:mid_a], outgoing_rim))
    tile_first = tile_part(first_queries, block_in[rim:mid_a])
    arrived_rim, tile_first = lax.optimization_barrier((arrived_rim, tile_first))
    spaced_rim = space_blend(tile_rim, arrived_rim)
    low, high = lax.optimization_barrier((spaced_rim[:rim], spaced_rim[rim:]))
    count = lax.axis_size("tm")
    lower = lax.ppermute(high, "tm", [(i, i + 1) for i in range(count - 1)])
    upper = lax.ppermute(low, "tm", [(i + 1, i) for i in range(count - 1)])
    second_queries, low, high = lax.optimization_barrier(
        (queries[:, mid_a : tokens - rim], low, high)
    )
    tile_second = tile_part(second_queries, block_in[mid_a : tokens - rim])
    lower, upper, tile_second = lax.optimization_barrier((lower, upper, tile_second))
    tile_mid = jnp.concatenate([tile_first, tile_second], axis=0)
    spaced_mid = space_blend(tile_mid, strips_in(strips_out(tile_mid)))

    span_id = lax.axis_index("tm")
    has_lower = span_id > 0
    has_upper = span_id < count - 1
    tramp = time_ramp.astype(jnp.float32)
    hold = tramp / (tramp + tramp[::-1])
    pass_ = tramp[::-1] / (tramp + tramp[::-1])
    blocks = (OVT, S * S, D)
    low_f = low.astype(jnp.float32).reshape(blocks)
    high_f = high.astype(jnp.float32).reshape(blocks)
    hold_low = hold[:, None, None]
    pass_low = pass_[:, None, None]
    hold_high = hold[::-1][:, None, None]
    pass_high = pass_[::-1][:, None, None]
    low_mix = jnp.where(
        has_lower, hold_low * low_f + pass_low * lower.astype(jnp.float32).reshape(blocks), low_f
    ).reshape(rim, D)
    high_mix = jnp.where(
        has_upper, hold_high * high_f + pass_high * upper.astype(jnp.float32).reshape(blocks), high_f
    ).reshape(rim, D)
    result = jnp.concatenate(
        [low_mix.astype(jnp.bfloat16), spaced_mid, high_mix.astype(jnp.bfloat16)], axis=0
    )
    return result.reshape(1, 1, tokens, D)


def solution(mesh):
    return jax.shard_map(
        per_device,
        mesh=mesh,
        in_specs=(
            P(("groups", "tm"), "face", None, None),
            P("groups", None),
            P("face", None),
            P(None, "face"),
            P(),
            P(),
            P(),
        ),
        out_specs=P(("groups", "tm"), "face", None, None),
        check_vma=False,
    )
```

```python
import math

import jax
import jax.numpy as jnp
import numpy as np
from jax import lax
from jax.experimental import pallas as pl
from jax.experimental.pallas import tpu as pltpu
from jax.sharding import PartitionSpec as P

D = 1152
HD = 72
HEADS = 8
S = 8
OVS = 2
OVT = 4
MID = S - 2 * OVS


NORM_EPS = 1e-06
OFFSETS = (1, -1, 2, -2)
PARTNER_ROUTE = (1, 0, 3, 2)


def modulate(block_in, modulation):
    values = block_in.astype(jnp.float32)
    center = jnp.mean(values, axis=-1, keepdims=True)
    spread = jnp.mean(jnp.square(values - center), axis=-1, keepdims=True)
    normed = (values - center) * lax.rsqrt(spread + NORM_EPS)
    return (normed * (1.0 + modulation[1]) + modulation[0]).astype(jnp.bfloat16)


def attention_kernel(q_ref, k_ref, v_ref, w_ref, x_ref, g_ref, o_ref, acc_ref):
    head = pl.program_id(1)

    @pl.when(head == 0)
    def _():
        acc_ref[...] = jnp.zeros_like(acc_ref)

    scores = jnp.dot(q_ref[0], k_ref[0], preferred_element_type=jnp.float32) * (
        1.0 / math.sqrt(HD)
    )
    row_max = jnp.max(scores, axis=-1, keepdims=True)
    weights = jnp.exp(scores - row_max)
    row_sum = jnp.sum(weights, axis=-1, keepdims=True)
    probabilities = (weights * (1.0 / row_sum)).astype(jnp.bfloat16)
    mixed = jnp.dot(probabilities, v_ref[0], preferred_element_type=jnp.float32).astype(
        jnp.bfloat16
    )
    acc_ref[...] += jnp.dot(mixed, w_ref[...], preferred_element_type=jnp.float32)

    @pl.when(head == pl.num_programs(1) - 1)
    def _():
        o_ref[...] = (x_ref[...].astype(jnp.float32) + g_ref[...] * acc_ref[...]).astype(
            o_ref.dtype
        )


def attend_project(queries, keys, values, w_out_full, block_in, gate):
    heads, size, tokens = keys.shape
    chunk = queries.shape[1]
    width = block_in.shape[1]
    return pl.pallas_call(
        attention_kernel,
        grid=(1, heads),
        in_specs=[
            pl.BlockSpec((1, chunk, size), lambda i, h: (h, i, 0)),
            pl.BlockSpec((1, size, tokens), lambda i, h: (h, 0, 0)),
            pl.BlockSpec((1, tokens, size), lambda i, h: (h, 0, 0)),
            pl.BlockSpec((size, width), lambda i, h: (h, 0)),
            pl.BlockSpec((chunk, width), lambda i, h: (i, 0)),
            pl.BlockSpec((1, width), lambda i, h: (0, 0)),
        ],
        out_specs=pl.BlockSpec((chunk, width), lambda i, h: (i, 0)),
        out_shape=jax.ShapeDtypeStruct(block_in.shape, block_in.dtype),
        scratch_shapes=[pltpu.VMEM((chunk, width), jnp.float32)],
        compiler_params=pltpu.CompilerParams(dimension_semantics=("arbitrary", "arbitrary")),
    )(queries, keys, values, w_out_full, block_in, gate.reshape(1, width))


def face_pieces(shard):
    n = lax.axis_size("face")
    me = lax.axis_index("face")

    def fetch(x, src_of):
        return lax.ppermute(x, "face", [(src_of(i), i) for i in range(n)])

    pieces = [(shard, me), (fetch(shard, lambda i: i ^ 1), me ^ 1)]
    for j in range(1, n // 2):
        far = fetch(shard, lambda i: (i + 2 * j) % n)
        pieces.append((far, (me + 2 * j) % n))
        pieces.append((fetch(far, lambda i: i ^ 1), ((me ^ 1) + 2 * j) % n))
    return pieces


def strip_tables(frames):
    frame, depth, pos = np.meshgrid(
        np.arange(frames), np.arange(OVS), np.arange(MID), indexing="ij"
    )

    def token(edge, d, t):
        row = (d, S - 1 - d, OVS + t, OVS + t)[edge]
        col = (OVS + t, OVS + t, d, S - 1 - d)[edge]
        return (frame * (S * S) + row * S + col).reshape(-1)

    recv = np.stack([token(e, depth, pos) for e in range(4)])
    send = np.stack(
        [[token(e, OVS - 1 - depth, pos if flip == 0 else MID - 1 - pos) for flip in range(2)]
         for e in range(4)]
    )
    return recv.astype(np.int32), send.astype(np.int32)


def strip_depth(frames):
    grid = np.full((S, S), -1, np.int32)
    for d in range(OVS):
        grid[d, OVS : S - OVS] = d
        grid[S - 1 - d, OVS : S - OVS] = d
        grid[OVS : S - OVS, d] = d
        grid[OVS : S - OVS, S - 1 - d] = d
    return np.tile(grid.reshape(-1), frames)


def per_device(latents, modulation, w_qkv, w_out, edge_table, space_ramp, time_ramp):
    block_in = latents[0, 0]
    tokens = block_in.shape[0]
    frames = tokens // (S * S)
    n = lax.axis_size("face")
    rows = w_qkv.shape[0]
    moved = modulate(block_in, modulation)
    qkv_pieces = face_pieces(w_qkv)
    w_out_late, _ = lax.optimization_barrier((w_out, [piece for piece, _ in qkv_pieces]))
    if n <= 4:
        moved_parts = moved.reshape(tokens, n, rows).transpose(1, 0, 2)
        qkv_sums = None
        for piece, index in qkv_pieces:
            part = jnp.dot(
                lax.dynamic_index_in_dim(moved_parts, index, 0, keepdims=False),
                piece,
                preferred_element_type=jnp.float32,
            )
            qkv_sums = part if qkv_sums is None else qkv_sums + part
    else:
        qkv_stack = jnp.zeros((n,) + w_qkv.shape, w_qkv.dtype)
        for piece, index in qkv_pieces:
            qkv_stack = lax.dynamic_update_index_in_dim(qkv_stack, piece, index, 0)
        w_qkv_full = qkv_stack.reshape(n * rows, w_qkv.shape[1])
        qkv_sums = jnp.dot(moved, w_qkv_full, preferred_element_type=jnp.float32)
    qkv_all = qkv_sums.astype(jnp.bfloat16)

    out_stack = jnp.zeros((n,) + w_out.shape, w_out.dtype)
    for piece, index in face_pieces(w_out_late):
        out_stack = lax.dynamic_update_index_in_dim(out_stack, piece, index, 0)
    w_out_full = out_stack.transpose(1, 0, 2).reshape(w_out.shape[0], n * w_out.shape[1])

    split = qkv_all.reshape(tokens, 3, HEADS, HD)
    queries = split[:, 0].transpose(1, 0, 2)
    keys = split[:, 1].transpose(1, 2, 0)
    values = split[:, 2].transpose(1, 0, 2)
    rim = OVT * S * S
    mid_a = rim + ((tokens - 2 * rim) // (2 * S * S)) * (S * S)
    gate = modulation[2]

    def tile_part(part_queries, part_in):
        return attend_project(part_queries, keys, values, w_out_full, part_in, gate)

    my_rows = lax.dynamic_index_in_dim(edge_table, lax.axis_index("face"), 0, keepdims=False)
    flips = my_rows[:, 2]
    routes = my_rows[:, 3]
    send_match = routes[None, :] == jnp.asarray(PARTNER_ROUTE, jnp.int32)[:, None]
    recv_match = routes[None, :] == jnp.arange(4, dtype=jnp.int32)[:, None]
    ramp = space_ramp.astype(jnp.float32)
    keep = ramp / (ramp + ramp[::-1])
    take = ramp[::-1] / (ramp + ramp[::-1])

    def strips_out(tile_out):
        part_tokens = tile_out.shape[0]
        part_frames = part_tokens // (S * S)
        _, send_table = strip_tables(part_frames)
        send_by_edge = jnp.where(flips[:, None] > 0, send_table[:, 1], send_table[:, 0])
        send_cells = jnp.sum(jnp.where(send_match[:, :, None], send_by_edge[None], 0), axis=1)
        send_cells = send_cells.reshape(-1)
        token_ids = jnp.arange(part_tokens, dtype=jnp.int32)
        pick = (send_cells[:, None] == token_ids[None, :]).astype(jnp.bfloat16)
        return jnp.dot(pick, tile_out, preferred_element_type=jnp.float32).astype(jnp.bfloat16)

    def strips_in(outgoing):
        strip_len = outgoing.shape[0] // 4
        arrived = []
        for route_id in range(4):
            sent = outgoing[route_id * strip_len : (route_id + 1) * strip_len]
            shift = -OFFSETS[route_id]
            arrived.append(
                lax.ppermute(sent, "face", [(i, (i + shift) % n) for i in range(n)])
            )
        return jnp.concatenate(arrived, axis=0)

    def space_blend(tile_out, arrived):
        part_tokens = tile_out.shape[0]
        part_frames = part_tokens // (S * S)
        recv_table, _ = strip_tables(part_frames)
        recv_cells = jnp.sum(jnp.where(recv_match[:, :, None], recv_table[None], 0), axis=1)
        recv_cells = recv_cells.reshape(-1)
        token_ids = jnp.arange(part_tokens, dtype=jnp.int32)
        place = (token_ids[:, None] == recv_cells[None, :]).astype(jnp.bfloat16)
        partner = jnp.dot(place, arrived, preferred_element_type=jnp.float32)
        dep = strip_depth(part_frames)[:, None]
        w_keep = jnp.where(dep == 0, keep[0], keep[1])
        w_take = jnp.where(dep == 0, take[0], take[1])
        own = tile_out.astype(jnp.float32)
        return jnp.where(dep >= 0, w_keep * own + w_take * partner, own).astype(jnp.bfloat16)

    rim_queries = jnp.concatenate([queries[:, :rim], queries[:, tokens - rim :]], axis=1)
    rim_in = jnp.concatenate([block_in[:rim], block_in[tokens - rim :]], axis=0)
    tile_rim = tile_part(rim_queries, rim_in)
    outgoing_rim = strips_out(tile_rim)
    arrived_rim = strips_in(outgoing_rim)
    first_queries, outgoing_rim = lax.optimization_barrier((queries[:, rim:mid_a], outgoing_rim))
    tile_first = tile_part(first_queries, block_in[rim:mid_a])
    arrived_rim, tile_first = lax.optimization_barrier((arrived_rim, tile_first))
    spaced_rim = space_blend(tile_rim, arrived_rim)
    low, high = lax.optimization_barrier((spaced_rim[:rim], spaced_rim[rim:]))
    count = lax.axis_size("tm")
    lower = lax.ppermute(high, "tm", [(i, i + 1) for i in range(count - 1)])
    upper = lax.ppermute(low, "tm", [(i + 1, i) for i in range(count - 1)])
    second_queries, low, high = lax.optimization_barrier(
        (queries[:, mid_a : tokens - rim], low, high)
    )
    tile_second = tile_part(second_queries, block_in[mid_a : tokens - rim])
    lower, upper, tile_second = lax.optimization_barrier((lower, upper, tile_second))
    tile_mid = jnp.concatenate([tile_first, tile_second], axis=0)
    spaced_mid = space_blend(tile_mid, strips_in(strips_out(tile_mid)))

    span_id = lax.axis_index("tm")
    has_lower = span_id > 0
    has_upper = span_id < count - 1
    tramp = time_ramp.astype(jnp.float32)
    hold = tramp / (tramp + tramp[::-1])
    pass_ = tramp[::-1] / (tramp + tramp[::-1])
    blocks = (OVT, S * S, D)
    low_f = low.astype(jnp.float32).reshape(blocks)
    high_f = high.astype(jnp.float32).reshape(blocks)
    hold_low = hold[:, None, None]
    pass_low = pass_[:, None, None]
    hold_high = hold[::-1][:, None, None]
    pass_high = pass_[::-1][:, None, None]
    low_mix = jnp.where(
        has_lower, hold_low * low_f + pass_low * lower.astype(jnp.float32).reshape(blocks), low_f
    ).reshape(rim, D)
    high_mix = jnp.where(
        has_upper, hold_high * high_f + pass_high * upper.astype(jnp.float32).reshape(blocks), high_f
    ).reshape(rim, D)
    result = jnp.concatenate(
        [low_mix.astype(jnp.bfloat16), spaced_mid, high_mix.astype(jnp.bfloat16)], axis=0
    )
    return result.reshape(1, 1, tokens, D)


def solution(mesh):
    return jax.shard_map(
        per_device,
        mesh=mesh,
        in_specs=(
            P(("groups", "tm"), "face", None, None),
            P("groups", None),
            P("face", None),
            P(None, "face"),
            P(),
            P(),
            P(),
        ),
        out_specs=P(("groups", "tm"), "face", None, None),
        check_vma=False,
    )
```

```python
import math

import jax
import jax.numpy as jnp
import numpy as np
from jax import lax
from jax.experimental import pallas as pl
from jax.experimental.pallas import tpu as pltpu
from jax.sharding import PartitionSpec as P

D = 1152
HD = 72
HEADS = 8
S = 8
OVS = 2
OVT = 4
MID = S - 2 * OVS


NORM_EPS = 1e-06
OFFSETS = (1, -1, 2, -2)
PARTNER_ROUTE = (1, 0, 3, 2)


def modulate(block_in, modulation):
    values = block_in.astype(jnp.float32)
    center = jnp.mean(values, axis=-1, keepdims=True)
    spread = jnp.mean(jnp.square(values - center), axis=-1, keepdims=True)
    normed = (values - center) * lax.rsqrt(spread + NORM_EPS)
    return (normed * (1.0 + modulation[1]) + modulation[0]).astype(jnp.bfloat16)


def attention_kernel(q_ref, k_ref, v_ref, w_ref, x_ref, g_ref, o_ref, acc_ref):
    head = pl.program_id(1)

    @pl.when(head == 0)
    def _():
        acc_ref[...] = jnp.zeros_like(acc_ref)

    scores = jnp.dot(q_ref[0], k_ref[0], preferred_element_type=jnp.float32) * (
        1.0 / math.sqrt(HD)
    )
    row_max = jnp.max(scores, axis=-1, keepdims=True)
    weights = jnp.exp(scores - row_max)
    row_sum = jnp.sum(weights, axis=-1, keepdims=True)
    probabilities = (weights * (1.0 / row_sum)).astype(jnp.bfloat16)
    mixed = jnp.dot(probabilities, v_ref[0], preferred_element_type=jnp.float32).astype(
        jnp.bfloat16
    )
    acc_ref[...] += jnp.dot(mixed, w_ref[...], preferred_element_type=jnp.float32)

    @pl.when(head == pl.num_programs(1) - 1)
    def _():
        o_ref[...] = (x_ref[...].astype(jnp.float32) + g_ref[...] * acc_ref[...]).astype(
            o_ref.dtype
        )


def attend_project(queries, keys, values, w_out_full, block_in, gate):
    heads, size, tokens = keys.shape
    chunk = queries.shape[1]
    width = block_in.shape[1]
    return pl.pallas_call(
        attention_kernel,
        grid=(1, heads),
        in_specs=[
            pl.BlockSpec((1, chunk, size), lambda i, h: (h, i, 0)),
            pl.BlockSpec((1, size, tokens), lambda i, h: (h, 0, 0)),
            pl.BlockSpec((1, tokens, size), lambda i, h: (h, 0, 0)),
            pl.BlockSpec((size, width), lambda i, h: (h, 0)),
            pl.BlockSpec((chunk, width), lambda i, h: (i, 0)),
            pl.BlockSpec((1, width), lambda i, h: (0, 0)),
        ],
        out_specs=pl.BlockSpec((chunk, width), lambda i, h: (i, 0)),
        out_shape=jax.ShapeDtypeStruct(block_in.shape, block_in.dtype),
        scratch_shapes=[pltpu.VMEM((chunk, width), jnp.float32)],
        compiler_params=pltpu.CompilerParams(dimension_semantics=("arbitrary", "arbitrary")),
    )(queries, keys, values, w_out_full, block_in, gate.reshape(1, width))


def face_pieces(shard):
    n = lax.axis_size("face")
    me = lax.axis_index("face")

    def fetch(x, src_of):
        return lax.ppermute(x, "face", [(src_of(i), i) for i in range(n)])

    pieces = [(shard, me), (fetch(shard, lambda i: i ^ 1), me ^ 1)]
    for j in range(1, n // 2):
        far = fetch(shard, lambda i: (i + 2 * j) % n)
        pieces.append((far, (me + 2 * j) % n))
        pieces.append((fetch(far, lambda i: i ^ 1), ((me ^ 1) + 2 * j) % n))
    return pieces


def strip_tables(frames):
    frame, depth, pos = np.meshgrid(
        np.arange(frames), np.arange(OVS), np.arange(MID), indexing="ij"
    )

    def token(edge, d, t):
        row = (d, S - 1 - d, OVS + t, OVS + t)[edge]
        col = (OVS + t, OVS + t, d, S - 1 - d)[edge]
        return (frame * (S * S) + row * S + col).reshape(-1)

    recv = np.stack([token(e, depth, pos) for e in range(4)])
    send = np.stack(
        [[token(e, OVS - 1 - depth, pos if flip == 0 else MID - 1 - pos) for flip in range(2)]
         for e in range(4)]
    )
    return recv.astype(np.int32), send.astype(np.int32)


def strip_depth(frames):
    grid = np.full((S, S), -1, np.int32)
    for d in range(OVS):
        grid[d, OVS : S - OVS] = d
        grid[S - 1 - d, OVS : S - OVS] = d
        grid[OVS : S - OVS, d] = d
        grid[OVS : S - OVS, S - 1 - d] = d
    return np.tile(grid.reshape(-1), frames)


def per_device(latents, modulation, w_qkv, w_out, edge_table, space_ramp, time_ramp):
    block_in = latents[0, 0]
    tokens = block_in.shape[0]
    frames = tokens // (S * S)
    n = lax.axis_size("face")
    rows = w_qkv.shape[0]
    moved = modulate(block_in, modulation)
    qkv_pieces = face_pieces(w_qkv)
    w_out_late, _ = lax.optimization_barrier((w_out, [piece for piece, _ in qkv_pieces]))
    if n <= 4:
        me = lax.axis_index("face")
        core = me % 2
        chips = n // 2
        moved_chips = moved.reshape(tokens, chips, 2 * rows).transpose(1, 0, 2)

        def chip_weight(same_core, other_core):
            stack = jnp.zeros((2,) + w_qkv.shape, w_qkv.dtype)
            stack = lax.dynamic_update_index_in_dim(stack, same_core, core, 0)
            stack = lax.dynamic_update_index_in_dim(stack, other_core, 1 - core, 0)
            return stack.reshape(2 * rows, w_qkv.shape[1])

        qkv_sums = None
        for j in range(chips):
            weight = chip_weight(qkv_pieces[2 * j][0], qkv_pieces[2 * j + 1][0])
            part = jnp.dot(
                lax.dynamic_index_in_dim(moved_chips, (me // 2 + j) % chips, 0, keepdims=False),
                weight,
                preferred_element_type=jnp.float32,
            )
            qkv_sums = part if qkv_sums is None else qkv_sums + part
    else:
        qkv_stack = jnp.zeros((n,) + w_qkv.shape, w_qkv.dtype)
        for piece, index in qkv_pieces:
            qkv_stack = lax.dynamic_update_index_in_dim(qkv_stack, piece, index, 0)
        w_qkv_full = qkv_stack.reshape(n * rows, w_qkv.shape[1])
        qkv_sums = jnp.dot(moved, w_qkv_full, preferred_element_type=jnp.float32)
    qkv_all = qkv_sums.astype(jnp.bfloat16)

    out_stack = jnp.zeros((n,) + w_out.shape, w_out.dtype)
    for piece, index in face_pieces(w_out_late):
        out_stack = lax.dynamic_update_index_in_dim(out_stack, piece, index, 0)
    w_out_full = out_stack.transpose(1, 0, 2).reshape(w_out.shape[0], n * w_out.shape[1])

    split = qkv_all.reshape(tokens, 3, HEADS, HD)
    queries = split[:, 0].transpose(1, 0, 2)
    keys = split[:, 1].transpose(1, 2, 0)
    values = split[:, 2].transpose(1, 0, 2)
    rim = OVT * S * S
    mid_a = rim + ((tokens - 2 * rim) // (2 * S * S)) * (S * S)
    gate = modulation[2]

    def tile_part(part_queries, part_in):
        return attend_project(part_queries, keys, values, w_out_full, part_in, gate)

    my_rows = lax.dynamic_index_in_dim(edge_table, lax.axis_index("face"), 0, keepdims=False)
    flips = my_rows[:, 2]
    routes = my_rows[:, 3]
    send_match = routes[None, :] == jnp.asarray(PARTNER_ROUTE, jnp.int32)[:, None]
    recv_match = routes[None, :] == jnp.arange(4, dtype=jnp.int32)[:, None]
    ramp = space_ramp.astype(jnp.float32)
    keep = ramp / (ramp + ramp[::-1])
    take = ramp[::-1] / (ramp + ramp[::-1])

    def strips_out(tile_out):
        part_tokens = tile_out.shape[0]
        part_frames = part_tokens // (S * S)
        _, send_table = strip_tables(part_frames)
        send_by_edge = jnp.where(flips[:, None] > 0, send_table[:, 1], send_table[:, 0])
        send_cells = jnp.sum(jnp.where(send_match[:, :, None], send_by_edge[None], 0), axis=1)
        send_cells = send_cells.reshape(-1)
        token_ids = jnp.arange(part_tokens, dtype=jnp.int32)
        pick = (send_cells[:, None] == token_ids[None, :]).astype(jnp.bfloat16)
        return jnp.dot(pick, tile_out, preferred_element_type=jnp.float32).astype(jnp.bfloat16)

    def strips_in(outgoing):
        strip_len = outgoing.shape[0] // 4
        arrived = []
        for route_id in range(4):
            sent = outgoing[route_id * strip_len : (route_id + 1) * strip_len]
            shift = -OFFSETS[route_id]
            arrived.append(
                lax.ppermute(sent, "face", [(i, (i + shift) % n) for i in range(n)])
            )
        return jnp.concatenate(arrived, axis=0)

    def space_blend(tile_out, arrived):
        part_tokens = tile_out.shape[0]
        part_frames = part_tokens // (S * S)
        recv_table, _ = strip_tables(part_frames)
        recv_cells = jnp.sum(jnp.where(recv_match[:, :, None], recv_table[None], 0), axis=1)
        recv_cells = recv_cells.reshape(-1)
        token_ids = jnp.arange(part_tokens, dtype=jnp.int32)
        place = (token_ids[:, None] == recv_cells[None, :]).astype(jnp.bfloat16)
        partner = jnp.dot(place, arrived, preferred_element_type=jnp.float32)
        dep = strip_depth(part_frames)[:, None]
        w_keep = jnp.where(dep == 0, keep[0], keep[1])
        w_take = jnp.where(dep == 0, take[0], take[1])
        own = tile_out.astype(jnp.float32)
        return jnp.where(dep >= 0, w_keep * own + w_take * partner, own).astype(jnp.bfloat16)

    rim_queries = jnp.concatenate([queries[:, :rim], queries[:, tokens - rim :]], axis=1)
    rim_in = jnp.concatenate([block_in[:rim], block_in[tokens - rim :]], axis=0)
    tile_rim = tile_part(rim_queries, rim_in)
    outgoing_rim = strips_out(tile_rim)
    arrived_rim = strips_in(outgoing_rim)
    first_queries, outgoing_rim = lax.optimization_barrier((queries[:, rim:mid_a], outgoing_rim))
    tile_first = tile_part(first_queries, block_in[rim:mid_a])
    arrived_rim, tile_first = lax.optimization_barrier((arrived_rim, tile_first))
    spaced_rim = space_blend(tile_rim, arrived_rim)
    low, high = lax.optimization_barrier((spaced_rim[:rim], spaced_rim[rim:]))
    count = lax.axis_size("tm")
    lower = lax.ppermute(high, "tm", [(i, i + 1) for i in range(count - 1)])
    upper = lax.ppermute(low, "tm", [(i + 1, i) for i in range(count - 1)])
    second_queries, low, high = lax.optimization_barrier(
        (queries[:, mid_a : tokens - rim], low, high)
    )
    tile_second = tile_part(second_queries, block_in[mid_a : tokens - rim])
    lower, upper, tile_second = lax.optimization_barrier((lower, upper, tile_second))
    tile_mid = jnp.concatenate([tile_first, tile_second], axis=0)
    spaced_mid = space_blend(tile_mid, strips_in(strips_out(tile_mid)))

    span_id = lax.axis_index("tm")
    has_lower = span_id > 0
    has_upper = span_id < count - 1
    tramp = time_ramp.astype(jnp.float32)
    hold = tramp / (tramp + tramp[::-1])
    pass_ = tramp[::-1] / (tramp + tramp[::-1])
    blocks = (OVT, S * S, D)
    low_f = low.astype(jnp.float32).reshape(blocks)
    high_f = high.astype(jnp.float32).reshape(blocks)
    hold_low = hold[:, None, None]
    pass_low = pass_[:, None, None]
    hold_high = hold[::-1][:, None, None]
    pass_high = pass_[::-1][:, None, None]
    low_mix = jnp.where(
        has_lower, hold_low * low_f + pass_low * lower.astype(jnp.float32).reshape(blocks), low_f
    ).reshape(rim, D)
    high_mix = jnp.where(
        has_upper, hold_high * high_f + pass_high * upper.astype(jnp.float32).reshape(blocks), high_f
    ).reshape(rim, D)
    result = jnp.concatenate(
        [low_mix.astype(jnp.bfloat16), spaced_mid, high_mix.astype(jnp.bfloat16)], axis=0
    )
    return result.reshape(1, 1, tokens, D)


def solution(mesh):
    return jax.shard_map(
        per_device,
        mesh=mesh,
        in_specs=(
            P(("groups", "tm"), "face", None, None),
            P("groups", None),
            P("face", None),
            P(None, "face"),
            P(),
            P(),
            P(),
        ),
        out_specs=P(("groups", "tm"), "face", None, None),
        check_vma=False,
    )
```

```python
import math

import jax
import jax.numpy as jnp
import numpy as np
from jax import lax
from jax.experimental import pallas as pl
from jax.experimental.pallas import tpu as pltpu
from jax.sharding import PartitionSpec as P

D = 1152
HD = 72
HEADS = 8
S = 8
OVS = 2
OVT = 4
MID = S - 2 * OVS


NORM_EPS = 1e-06
OFFSETS = (1, -1, 2, -2)
PARTNER_ROUTE = (1, 0, 3, 2)


def modulate(block_in, modulation):
    values = block_in.astype(jnp.float32)
    center = jnp.mean(values, axis=-1, keepdims=True)
    spread = jnp.mean(jnp.square(values - center), axis=-1, keepdims=True)
    normed = (values - center) * lax.rsqrt(spread + NORM_EPS)
    return (normed * (1.0 + modulation[1]) + modulation[0]).astype(jnp.bfloat16)


def attention_kernel(q_ref, k_ref, v_ref, w_ref, x_ref, g_ref, o_ref, acc_ref):
    head = pl.program_id(1)

    @pl.when(head == 0)
    def _():
        acc_ref[...] = jnp.zeros_like(acc_ref)

    scores = jnp.dot(q_ref[0], k_ref[0], preferred_element_type=jnp.float32) * (
        1.0 / math.sqrt(HD)
    )
    row_max = jnp.max(scores, axis=-1, keepdims=True)
    weights = jnp.exp(scores - row_max)
    row_sum = jnp.sum(weights, axis=-1, keepdims=True)
    probabilities = (weights * (1.0 / row_sum)).astype(jnp.bfloat16)
    mixed = jnp.dot(probabilities, v_ref[0], preferred_element_type=jnp.float32).astype(
        jnp.bfloat16
    )
    acc_ref[...] += jnp.dot(mixed, w_ref[...], preferred_element_type=jnp.float32)

    @pl.when(head == pl.num_programs(1) - 1)
    def _():
        o_ref[...] = (x_ref[...].astype(jnp.float32) + g_ref[...] * acc_ref[...]).astype(
            o_ref.dtype
        )


def attend_project(queries, keys, values, w_out_full, block_in, gate):
    heads, size, tokens = keys.shape
    chunk = queries.shape[1]
    width = block_in.shape[1]
    return pl.pallas_call(
        attention_kernel,
        grid=(1, heads),
        in_specs=[
            pl.BlockSpec((1, chunk, size), lambda i, h: (h, i, 0)),
            pl.BlockSpec((1, size, tokens), lambda i, h: (h, 0, 0)),
            pl.BlockSpec((1, tokens, size), lambda i, h: (h, 0, 0)),
            pl.BlockSpec((size, width), lambda i, h: (h, 0)),
            pl.BlockSpec((chunk, width), lambda i, h: (i, 0)),
            pl.BlockSpec((1, width), lambda i, h: (0, 0)),
        ],
        out_specs=pl.BlockSpec((chunk, width), lambda i, h: (i, 0)),
        out_shape=jax.ShapeDtypeStruct(block_in.shape, block_in.dtype),
        scratch_shapes=[pltpu.VMEM((chunk, width), jnp.float32)],
        compiler_params=pltpu.CompilerParams(dimension_semantics=("arbitrary", "arbitrary")),
    )(queries, keys, values, w_out_full, block_in, gate.reshape(1, width))


def face_pieces(shard):
    n = lax.axis_size("face")
    me = lax.axis_index("face")

    def fetch(x, src_of):
        return lax.ppermute(x, "face", [(src_of(i), i) for i in range(n)])

    pieces = [(shard, me), (fetch(shard, lambda i: i ^ 1), me ^ 1)]
    for j in range(1, n // 2):
        far = fetch(shard, lambda i: (i + 2 * j) % n)
        pieces.append((far, (me + 2 * j) % n))
        pieces.append((fetch(far, lambda i: i ^ 1), ((me ^ 1) + 2 * j) % n))
    return pieces


def strip_tables(frames):
    frame, depth, pos = np.meshgrid(
        np.arange(frames), np.arange(OVS), np.arange(MID), indexing="ij"
    )

    def token(edge, d, t):
        row = (d, S - 1 - d, OVS + t, OVS + t)[edge]
        col = (OVS + t, OVS + t, d, S - 1 - d)[edge]
        return (frame * (S * S) + row * S + col).reshape(-1)

    recv = np.stack([token(e, depth, pos) for e in range(4)])
    send = np.stack(
        [[token(e, OVS - 1 - depth, pos if flip == 0 else MID - 1 - pos) for flip in range(2)]
         for e in range(4)]
    )
    return recv.astype(np.int32), send.astype(np.int32)


def strip_depth(frames):
    grid = np.full((S, S), -1, np.int32)
    for d in range(OVS):
        grid[d, OVS : S - OVS] = d
        grid[S - 1 - d, OVS : S - OVS] = d
        grid[OVS : S - OVS, d] = d
        grid[OVS : S - OVS, S - 1 - d] = d
    return np.tile(grid.reshape(-1), frames)


def per_device(latents, modulation, w_qkv, w_out, edge_table, space_ramp, time_ramp):
    block_in = latents[0, 0]
    tokens = block_in.shape[0]
    frames = tokens // (S * S)
    n = lax.axis_size("face")
    rows = w_qkv.shape[0]
    moved = modulate(block_in, modulation)
    if n == 4:
        me = lax.axis_index("face")
        core = me % 2

        def fetch(x, src_of):
            return lax.ppermute(x, "face", [(src_of(i), i) for i in range(n)])

        moved_chips = moved.reshape(tokens, 2, 2 * rows).transpose(1, 0, 2)

        def chip_weight(same_core, other_core):
            stack = jnp.zeros((2,) + w_qkv.shape, w_qkv.dtype)
            stack = lax.dynamic_update_index_in_dim(stack, same_core, core, 0)
            stack = lax.dynamic_update_index_in_dim(stack, other_core, 1 - core, 0)
            return stack.reshape(2 * rows, w_qkv.shape[1])

        def chip_part(chip, weight):
            return jnp.dot(
                lax.dynamic_index_in_dim(moved_chips, chip, 0, keepdims=False),
                weight,
                preferred_element_type=jnp.float32,
            )

        sib = fetch(w_qkv, lambda i: i ^ 1)
        far = fetch(w_qkv, lambda i: (i + 2) % n)
        local = chip_part(me // 2, chip_weight(w_qkv, sib))
        local, far = lax.optimization_barrier((local, far))
        fwd = fetch(far, lambda i: i ^ 1)
        qkv_sums = local + chip_part(1 - me // 2, chip_weight(far, fwd))
        w_out_late, _ = lax.optimization_barrier((w_out, (far, fwd)))
    else:
        qkv_pieces = face_pieces(w_qkv)
        w_out_late, _ = lax.optimization_barrier((w_out, [piece for piece, _ in qkv_pieces]))
        qkv_stack = jnp.zeros((n,) + w_qkv.shape, w_qkv.dtype)
        for piece, index in qkv_pieces:
            qkv_stack = lax.dynamic_update_index_in_dim(qkv_stack, piece, index, 0)
        w_qkv_full = qkv_stack.reshape(n * rows, w_qkv.shape[1])
        qkv_sums = jnp.dot(moved, w_qkv_full, preferred_element_type=jnp.float32)
    qkv_all = qkv_sums.astype(jnp.bfloat16)

    out_stack = jnp.zeros((n,) + w_out.shape, w_out.dtype)
    for piece, index in face_pieces(w_out_late):
        out_stack = lax.dynamic_update_index_in_dim(out_stack, piece, index, 0)
    w_out_full = out_stack.transpose(1, 0, 2).reshape(w_out.shape[0], n * w_out.shape[1])

    split = qkv_all.reshape(tokens, 3, HEADS, HD)
    queries = split[:, 0].transpose(1, 0, 2)
    keys = split[:, 1].transpose(1, 2, 0)
    values = split[:, 2].transpose(1, 0, 2)
    rim = OVT * S * S
    mid_a = rim + ((tokens - 2 * rim) // (2 * S * S)) * (S * S)
    gate = modulation[2]

    def tile_part(part_queries, part_in):
        return attend_project(part_queries, keys, values, w_out_full, part_in, gate)

    my_rows = lax.dynamic_index_in_dim(edge_table, lax.axis_index("face"), 0, keepdims=False)
    flips = my_rows[:, 2]
    routes = my_rows[:, 3]
    send_match = routes[None, :] == jnp.asarray(PARTNER_ROUTE, jnp.int32)[:, None]
    recv_match = routes[None, :] == jnp.arange(4, dtype=jnp.int32)[:, None]
    ramp = space_ramp.astype(jnp.float32)
    keep = ramp / (ramp + ramp[::-1])
    take = ramp[::-1] / (ramp + ramp[::-1])

    def strips_out(tile_out):
        part_tokens = tile_out.shape[0]
        part_frames = part_tokens // (S * S)
        _, send_table = strip_tables(part_frames)
        send_by_edge = jnp.where(flips[:, None] > 0, send_table[:, 1], send_table[:, 0])
        send_cells = jnp.sum(jnp.where(send_match[:, :, None], send_by_edge[None], 0), axis=1)
        send_cells = send_cells.reshape(-1)
        token_ids = jnp.arange(part_tokens, dtype=jnp.int32)
        pick = (send_cells[:, None] == token_ids[None, :]).astype(jnp.bfloat16)
        return jnp.dot(pick, tile_out, preferred_element_type=jnp.float32).astype(jnp.bfloat16)

    def strips_in(outgoing):
        strip_len = outgoing.shape[0] // 4
        arrived = []
        for route_id in range(4):
            sent = outgoing[route_id * strip_len : (route_id + 1) * strip_len]
            shift = -OFFSETS[route_id]
            arrived.append(
                lax.ppermute(sent, "face", [(i, (i + shift) % n) for i in range(n)])
            )
        return jnp.concatenate(arrived, axis=0)

    def space_blend(tile_out, arrived):
        part_tokens = tile_out.shape[0]
        part_frames = part_tokens // (S * S)
        recv_table, _ = strip_tables(part_frames)
        recv_cells = jnp.sum(jnp.where(recv_match[:, :, None], recv_table[None], 0), axis=1)
        recv_cells = recv_cells.reshape(-1)
        token_ids = jnp.arange(part_tokens, dtype=jnp.int32)
        place = (token_ids[:, None] == recv_cells[None, :]).astype(jnp.bfloat16)
        partner = jnp.dot(place, arrived, preferred_element_type=jnp.float32)
        dep = strip_depth(part_frames)[:, None]
        w_keep = jnp.where(dep == 0, keep[0], keep[1])
        w_take = jnp.where(dep == 0, take[0], take[1])
        own = tile_out.astype(jnp.float32)
        return jnp.where(dep >= 0, w_keep * own + w_take * partner, own).astype(jnp.bfloat16)

    rim_queries = jnp.concatenate([queries[:, :rim], queries[:, tokens - rim :]], axis=1)
    rim_in = jnp.concatenate([block_in[:rim], block_in[tokens - rim :]], axis=0)
    tile_rim = tile_part(rim_queries, rim_in)
    outgoing_rim = strips_out(tile_rim)
    arrived_rim = strips_in(outgoing_rim)
    first_queries, outgoing_rim = lax.optimization_barrier((queries[:, rim:mid_a], outgoing_rim))
    tile_first = tile_part(first_queries, block_in[rim:mid_a])
    arrived_rim, tile_first = lax.optimization_barrier((arrived_rim, tile_first))
    spaced_rim = space_blend(tile_rim, arrived_rim)
    low, high = lax.optimization_barrier((spaced_rim[:rim], spaced_rim[rim:]))
    count = lax.axis_size("tm")
    lower = lax.ppermute(high, "tm", [(i, i + 1) for i in range(count - 1)])
    upper = lax.ppermute(low, "tm", [(i + 1, i) for i in range(count - 1)])
    second_queries, low, high = lax.optimization_barrier(
        (queries[:, mid_a : tokens - rim], low, high)
    )
    tile_second = tile_part(second_queries, block_in[mid_a : tokens - rim])
    lower, upper, tile_second = lax.optimization_barrier((lower, upper, tile_second))
    tile_mid = jnp.concatenate([tile_first, tile_second], axis=0)
    spaced_mid = space_blend(tile_mid, strips_in(strips_out(tile_mid)))

    span_id = lax.axis_index("tm")
    has_lower = span_id > 0
    has_upper = span_id < count - 1
    tramp = time_ramp.astype(jnp.float32)
    hold = tramp / (tramp + tramp[::-1])
    pass_ = tramp[::-1] / (tramp + tramp[::-1])
    blocks = (OVT, S * S, D)
    low_f = low.astype(jnp.float32).reshape(blocks)
    high_f = high.astype(jnp.float32).reshape(blocks)
    hold_low = hold[:, None, None]
    pass_low = pass_[:, None, None]
    hold_high = hold[::-1][:, None, None]
    pass_high = pass_[::-1][:, None, None]
    low_mix = jnp.where(
        has_lower, hold_low * low_f + pass_low * lower.astype(jnp.float32).reshape(blocks), low_f
    ).reshape(rim, D)
    high_mix = jnp.where(
        has_upper, hold_high * high_f + pass_high * upper.astype(jnp.float32).reshape(blocks), high_f
    ).reshape(rim, D)
    result = jnp.concatenate(
        [low_mix.astype(jnp.bfloat16), spaced_mid, high_mix.astype(jnp.bfloat16)], axis=0
    )
    return result.reshape(1, 1, tokens, D)


def solution(mesh):
    return jax.shard_map(
        per_device,
        mesh=mesh,
        in_specs=(
            P(("groups", "tm"), "face", None, None),
            P("groups", None),
            P("face", None),
            P(None, "face"),
            P(),
            P(),
            P(),
        ),
        out_specs=P(("groups", "tm"), "face", None, None),
        check_vma=False,
    )
```

```python
import math

import jax
import jax.numpy as jnp
import numpy as np
from jax import lax
from jax.experimental import pallas as pl
from jax.experimental.pallas import tpu as pltpu
from jax.sharding import PartitionSpec as P

D = 1152
HD = 72
HEADS = 8
S = 8
OVS = 2
OVT = 4
MID = S - 2 * OVS


NORM_EPS = 1e-06
OFFSETS = (1, -1, 2, -2)
PARTNER_ROUTE = (1, 0, 3, 2)


def modulate(block_in, modulation):
    values = block_in.astype(jnp.float32)
    center = jnp.mean(values, axis=-1, keepdims=True)
    spread = jnp.mean(jnp.square(values - center), axis=-1, keepdims=True)
    normed = (values - center) * lax.rsqrt(spread + NORM_EPS)
    return (normed * (1.0 + modulation[1]) + modulation[0]).astype(jnp.bfloat16)


HEADS_PER_STEP = 2


def attention_kernel(*refs):
    x_ref, g_ref, o_ref, acc_ref = refs[-4:]
    per_head = refs[:-4]
    step = pl.program_id(1)

    @pl.when(step == 0)
    def _():
        acc_ref[...] = jnp.zeros_like(acc_ref)

    total = None
    for j in range(HEADS_PER_STEP):
        q_ref, k_ref, v_ref, w_ref = per_head[4 * j : 4 * j + 4]
        scores = jnp.dot(q_ref[0], k_ref[0], preferred_element_type=jnp.float32) * (
            1.0 / math.sqrt(HD)
        )
        row_max = jnp.max(scores, axis=-1, keepdims=True)
        weights = jnp.exp(scores - row_max)
        row_sum = jnp.sum(weights, axis=-1, keepdims=True)
        probabilities = (weights * (1.0 / row_sum)).astype(jnp.bfloat16)
        mixed = jnp.dot(probabilities, v_ref[0], preferred_element_type=jnp.float32).astype(
            jnp.bfloat16
        )
        part = jnp.dot(mixed, w_ref[...], preferred_element_type=jnp.float32)
        total = part if total is None else total + part
    acc_ref[...] += total

    @pl.when(step == pl.num_programs(1) - 1)
    def _():
        o_ref[...] = (x_ref[...].astype(jnp.float32) + g_ref[...] * acc_ref[...]).astype(
            o_ref.dtype
        )


def attend_project(queries, keys, values, w_out_full, block_in, gate):
    heads, size, tokens = keys.shape
    chunk = queries.shape[1]
    width = block_in.shape[1]
    hb = HEADS_PER_STEP
    in_specs = []
    operands = []
    for j in range(hb):
        in_specs += [
            pl.BlockSpec((1, chunk, size), lambda i, h, j=j: (hb * h + j, i, 0)),
            pl.BlockSpec((1, size, tokens), lambda i, h, j=j: (hb * h + j, 0, 0)),
            pl.BlockSpec((1, tokens, size), lambda i, h, j=j: (hb * h + j, 0, 0)),
            pl.BlockSpec((size, width), lambda i, h, j=j: (hb * h + j, 0)),
        ]
        operands += [queries, keys, values, w_out_full]
    in_specs += [
        pl.BlockSpec((chunk, width), lambda i, h: (i, 0)),
        pl.BlockSpec((1, width), lambda i, h: (0, 0)),
    ]
    return pl.pallas_call(
        attention_kernel,
        grid=(1, heads // hb),
        in_specs=in_specs,
        out_specs=pl.BlockSpec((chunk, width), lambda i, h: (i, 0)),
        out_shape=jax.ShapeDtypeStruct(block_in.shape, block_in.dtype),
        scratch_shapes=[pltpu.VMEM((chunk, width), jnp.float32)],
        compiler_params=pltpu.CompilerParams(dimension_semantics=("arbitrary", "arbitrary")),
    )(*operands, block_in, gate.reshape(1, width))


def face_pieces(shard):
    n = lax.axis_size("face")
    me = lax.axis_index("face")

    def fetch(x, src_of):
        return lax.ppermute(x, "face", [(src_of(i), i) for i in range(n)])

    pieces = [(shard, me), (fetch(shard, lambda i: i ^ 1), me ^ 1)]
    for j in range(1, n // 2):
        far = fetch(shard, lambda i: (i + 2 * j) % n)
        pieces.append((far, (me + 2 * j) % n))
        pieces.append((fetch(far, lambda i: i ^ 1), ((me ^ 1) + 2 * j) % n))
    return pieces


def strip_tables(frames):
    frame, depth, pos = np.meshgrid(
        np.arange(frames), np.arange(OVS), np.arange(MID), indexing="ij"
    )

    def token(edge, d, t):
        row = (d, S - 1 - d, OVS + t, OVS + t)[edge]
        col = (OVS + t, OVS + t, d, S - 1 - d)[edge]
        return (frame * (S * S) + row * S + col).reshape(-1)

    recv = np.stack([token(e, depth, pos) for e in range(4)])
    send = np.stack(
        [[token(e, OVS - 1 - depth, pos if flip == 0 else MID - 1 - pos) for flip in range(2)]
         for e in range(4)]
    )
    return recv.astype(np.int32), send.astype(np.int32)


def strip_depth(frames):
    grid = np.full((S, S), -1, np.int32)
    for d in range(OVS):
        grid[d, OVS : S - OVS] = d
        grid[S - 1 - d, OVS : S - OVS] = d
        grid[OVS : S - OVS, d] = d
        grid[OVS : S - OVS, S - 1 - d] = d
    return np.tile(grid.reshape(-1), frames)


def per_device(latents, modulation, w_qkv, w_out, edge_table, space_ramp, time_ramp):
    block_in = latents[0, 0]
    tokens = block_in.shape[0]
    frames = tokens // (S * S)
    n = lax.axis_size("face")
    rows = w_qkv.shape[0]
    moved = modulate(block_in, modulation)
    if n == 4:
        me = lax.axis_index("face")
        core = me % 2

        def fetch(x, src_of):
            return lax.ppermute(x, "face", [(src_of(i), i) for i in range(n)])

        moved_chips = moved.reshape(tokens, 2, 2 * rows).transpose(1, 0, 2)

        def chip_weight(same_core, other_core):
            stack = jnp.zeros((2,) + w_qkv.shape, w_qkv.dtype)
            stack = lax.dynamic_update_index_in_dim(stack, same_core, core, 0)
            stack = lax.dynamic_update_index_in_dim(stack, other_core, 1 - core, 0)
            return stack.reshape(2 * rows, w_qkv.shape[1])

        def chip_part(chip, weight):
            return jnp.dot(
                lax.dynamic_index_in_dim(moved_chips, chip, 0, keepdims=False),
                weight,
                preferred_element_type=jnp.float32,
            )

        sib = fetch(w_qkv, lambda i: i ^ 1)
        far = fetch(w_qkv, lambda i: (i + 2) % n)
        local = chip_part(me // 2, chip_weight(w_qkv, sib))
        local, far = lax.optimization_barrier((local, far))
        fwd = fetch(far, lambda i: i ^ 1)
        qkv_sums = local + chip_part(1 - me // 2, chip_weight(far, fwd))
        w_out_late, _ = lax.optimization_barrier((w_out, (far, fwd)))
    else:
        qkv_pieces = face_pieces(w_qkv)
        w_out_late, _ = lax.optimization_barrier((w_out, [piece for piece, _ in qkv_pieces]))
        qkv_stack = jnp.zeros((n,) + w_qkv.shape, w_qkv.dtype)
        for piece, index in qkv_pieces:
            qkv_stack = lax.dynamic_update_index_in_dim(qkv_stack, piece, index, 0)
        w_qkv_full = qkv_stack.reshape(n * rows, w_qkv.shape[1])
        qkv_sums = jnp.dot(moved, w_qkv_full, preferred_element_type=jnp.float32)
    qkv_all = qkv_sums.astype(jnp.bfloat16)

    out_stack = jnp.zeros((n,) + w_out.shape, w_out.dtype)
    for piece, index in face_pieces(w_out_late):
        out_stack = lax.dynamic_update_index_in_dim(out_stack, piece, index, 0)
    w_out_full = out_stack.transpose(1, 0, 2).reshape(w_out.shape[0], n * w_out.shape[1])

    split = qkv_all.reshape(tokens, 3, HEADS, HD)
    queries = split[:, 0].transpose(1, 0, 2)
    keys = split[:, 1].transpose(1, 2, 0)
    values = split[:, 2].transpose(1, 0, 2)
    rim = OVT * S * S
    mid_a = rim + ((tokens - 2 * rim) // (2 * S * S)) * (S * S)
    gate = modulation[2]

    def tile_part(part_queries, part_in):
        return attend_project(part_queries, keys, values, w_out_full, part_in, gate)

    my_rows = lax.dynamic_index_in_dim(edge_table, lax.axis_index("face"), 0, keepdims=False)
    flips = my_rows[:, 2]
    routes = my_rows[:, 3]
    send_match = routes[None, :] == jnp.asarray(PARTNER_ROUTE, jnp.int32)[:, None]
    recv_match = routes[None, :] == jnp.arange(4, dtype=jnp.int32)[:, None]
    ramp = space_ramp.astype(jnp.float32)
    keep = ramp / (ramp + ramp[::-1])
    take = ramp[::-1] / (ramp + ramp[::-1])

    def strips_out(tile_out):
        part_tokens = tile_out.shape[0]
        part_frames = part_tokens // (S * S)
        _, send_table = strip_tables(part_frames)
        send_by_edge = jnp.where(flips[:, None] > 0, send_table[:, 1], send_table[:, 0])
        send_cells = jnp.sum(jnp.where(send_match[:, :, None], send_by_edge[None], 0), axis=1)
        send_cells = send_cells.reshape(-1)
        token_ids = jnp.arange(part_tokens, dtype=jnp.int32)
        pick = (send_cells[:, None] == token_ids[None, :]).astype(jnp.bfloat16)
        return jnp.dot(pick, tile_out, preferred_element_type=jnp.float32).astype(jnp.bfloat16)

    def strips_in(outgoing):
        strip_len = outgoing.shape[0] // 4
        arrived = []
        for route_id in range(4):
            sent = outgoing[route_id * strip_len : (route_id + 1) * strip_len]
            shift = -OFFSETS[route_id]
            arrived.append(
                lax.ppermute(sent, "face", [(i, (i + shift) % n) for i in range(n)])
            )
        return jnp.concatenate(arrived, axis=0)

    def space_blend(tile_out, arrived):
        part_tokens = tile_out.shape[0]
        part_frames = part_tokens // (S * S)
        recv_table, _ = strip_tables(part_frames)
        recv_cells = jnp.sum(jnp.where(recv_match[:, :, None], recv_table[None], 0), axis=1)
        recv_cells = recv_cells.reshape(-1)
        token_ids = jnp.arange(part_tokens, dtype=jnp.int32)
        place = (token_ids[:, None] == recv_cells[None, :]).astype(jnp.bfloat16)
        partner = jnp.dot(place, arrived, preferred_element_type=jnp.float32)
        dep = strip_depth(part_frames)[:, None]
        w_keep = jnp.where(dep == 0, keep[0], keep[1])
        w_take = jnp.where(dep == 0, take[0], take[1])
        own = tile_out.astype(jnp.float32)
        return jnp.where(dep >= 0, w_keep * own + w_take * partner, own).astype(jnp.bfloat16)

    rim_queries = jnp.concatenate([queries[:, :rim], queries[:, tokens - rim :]], axis=1)
    rim_in = jnp.concatenate([block_in[:rim], block_in[tokens - rim :]], axis=0)
    tile_rim = tile_part(rim_queries, rim_in)
    outgoing_rim = strips_out(tile_rim)
    arrived_rim = strips_in(outgoing_rim)
    first_queries, outgoing_rim = lax.optimization_barrier((queries[:, rim:mid_a], outgoing_rim))
    tile_first = tile_part(first_queries, block_in[rim:mid_a])
    arrived_rim, tile_first = lax.optimization_barrier((arrived_rim, tile_first))
    spaced_rim = space_blend(tile_rim, arrived_rim)
    low, high = lax.optimization_barrier((spaced_rim[:rim], spaced_rim[rim:]))
    count = lax.axis_size("tm")
    lower = lax.ppermute(high, "tm", [(i, i + 1) for i in range(count - 1)])
    upper = lax.ppermute(low, "tm", [(i + 1, i) for i in range(count - 1)])
    second_queries, low, high = lax.optimization_barrier(
        (queries[:, mid_a : tokens - rim], low, high)
    )
    tile_second = tile_part(second_queries, block_in[mid_a : tokens - rim])
    lower, upper, tile_second = lax.optimization_barrier((lower, upper, tile_second))
    tile_mid = jnp.concatenate([tile_first, tile_second], axis=0)
    spaced_mid = space_blend(tile_mid, strips_in(strips_out(tile_mid)))

    span_id = lax.axis_index("tm")
    has_lower = span_id > 0
    has_upper = span_id < count - 1
    tramp = time_ramp.astype(jnp.float32)
    hold = tramp / (tramp + tramp[::-1])
    pass_ = tramp[::-1] / (tramp + tramp[::-1])
    blocks = (OVT, S * S, D)
    low_f = low.astype(jnp.float32).reshape(blocks)
    high_f = high.astype(jnp.float32).reshape(blocks)
    hold_low = hold[:, None, None]
    pass_low = pass_[:, None, None]
    hold_high = hold[::-1][:, None, None]
    pass_high = pass_[::-1][:, None, None]
    low_mix = jnp.where(
        has_lower, hold_low * low_f + pass_low * lower.astype(jnp.float32).reshape(blocks), low_f
    ).reshape(rim, D)
    high_mix = jnp.where(
        has_upper, hold_high * high_f + pass_high * upper.astype(jnp.float32).reshape(blocks), high_f
    ).reshape(rim, D)
    result = jnp.concatenate(
        [low_mix.astype(jnp.bfloat16), spaced_mid, high_mix.astype(jnp.bfloat16)], axis=0
    )
    return result.reshape(1, 1, tokens, D)


def solution(mesh):
    return jax.shard_map(
        per_device,
        mesh=mesh,
        in_specs=(
            P(("groups", "tm"), "face", None, None),
            P("groups", None),
            P("face", None),
            P(None, "face"),
            P(),
            P(),
            P(),
        ),
        out_specs=P(("groups", "tm"), "face", None, None),
        check_vma=False,
    )
```

```python
import math

import jax
import jax.numpy as jnp
import numpy as np
from jax import lax
from jax.experimental import pallas as pl
from jax.experimental.pallas import tpu as pltpu
from jax.sharding import PartitionSpec as P

D = 1152
HD = 72
HEADS = 8
S = 8
OVS = 2
OVT = 4
MID = S - 2 * OVS


NORM_EPS = 1e-06
OFFSETS = (1, -1, 2, -2)
PARTNER_ROUTE = (1, 0, 3, 2)


def modulate(block_in, modulation):
    values = block_in.astype(jnp.float32)
    center = jnp.mean(values, axis=-1, keepdims=True)
    spread = jnp.mean(jnp.square(values - center), axis=-1, keepdims=True)
    normed = (values - center) * lax.rsqrt(spread + NORM_EPS)
    return (normed * (1.0 + modulation[1]) + modulation[0]).astype(jnp.bfloat16)


HEADS_PER_STEP = 2


def attention_kernel(q_ref, k_ref, v_ref, o_ref):
    for j in range(HEADS_PER_STEP):
        scores = jnp.dot(q_ref[j], k_ref[j], preferred_element_type=jnp.float32) * (
            1.0 / math.sqrt(HD)
        )
        row_max = jnp.max(scores, axis=-1, keepdims=True)
        weights = jnp.exp(scores - row_max)
        row_sum = jnp.sum(weights, axis=-1, keepdims=True)
        probabilities = (weights * (1.0 / row_sum)).astype(jnp.bfloat16)
        o_ref[j] = jnp.dot(probabilities, v_ref[j], preferred_element_type=jnp.float32).astype(
            o_ref.dtype
        )


def attend_project(queries, keys, values, w_out_full, block_in, gate):
    heads, size, tokens = keys.shape
    chunk = queries.shape[1]
    hb = HEADS_PER_STEP
    mixed = pl.pallas_call(
        attention_kernel,
        grid=(heads // hb,),
        in_specs=[
            pl.BlockSpec((hb, chunk, size), lambda h: (h, 0, 0)),
            pl.BlockSpec((hb, size, tokens), lambda h: (h, 0, 0)),
            pl.BlockSpec((hb, tokens, size), lambda h: (h, 0, 0)),
        ],
        out_specs=pl.BlockSpec((hb, chunk, size), lambda h: (h, 0, 0)),
        out_shape=jax.ShapeDtypeStruct(queries.shape, queries.dtype),
        compiler_params=pltpu.CompilerParams(dimension_semantics=("arbitrary",)),
    )(queries, keys, values)
    mixed = mixed.transpose(1, 0, 2).reshape(chunk, heads * size)
    projected = jnp.dot(mixed, w_out_full, preferred_element_type=jnp.float32)
    return (block_in.astype(jnp.float32) + gate * projected).astype(block_in.dtype)


def face_pieces(shard):
    n = lax.axis_size("face")
    me = lax.axis_index("face")

    def fetch(x, src_of):
        return lax.ppermute(x, "face", [(src_of(i), i) for i in range(n)])

    pieces = [(shard, me), (fetch(shard, lambda i: i ^ 1), me ^ 1)]
    for j in range(1, n // 2):
        far = fetch(shard, lambda i: (i + 2 * j) % n)
        pieces.append((far, (me + 2 * j) % n))
        pieces.append((fetch(far, lambda i: i ^ 1), ((me ^ 1) + 2 * j) % n))
    return pieces


def strip_tables(frames):
    frame, depth, pos = np.meshgrid(
        np.arange(frames), np.arange(OVS), np.arange(MID), indexing="ij"
    )

    def token(edge, d, t):
        row = (d, S - 1 - d, OVS + t, OVS + t)[edge]
        col = (OVS + t, OVS + t, d, S - 1 - d)[edge]
        return (frame * (S * S) + row * S + col).reshape(-1)

    recv = np.stack([token(e, depth, pos) for e in range(4)])
    send = np.stack(
        [[token(e, OVS - 1 - depth, pos if flip == 0 else MID - 1 - pos) for flip in range(2)]
         for e in range(4)]
    )
    return recv.astype(np.int32), send.astype(np.int32)


def strip_depth(frames):
    grid = np.full((S, S), -1, np.int32)
    for d in range(OVS):
        grid[d, OVS : S - OVS] = d
        grid[S - 1 - d, OVS : S - OVS] = d
        grid[OVS : S - OVS, d] = d
        grid[OVS : S - OVS, S - 1 - d] = d
    return np.tile(grid.reshape(-1), frames)


def per_device(latents, modulation, w_qkv, w_out, edge_table, space_ramp, time_ramp):
    block_in = latents[0, 0]
    tokens = block_in.shape[0]
    frames = tokens // (S * S)
    n = lax.axis_size("face")
    rows = w_qkv.shape[0]
    moved = modulate(block_in, modulation)
    if n == 4:
        me = lax.axis_index("face")
        core = me % 2

        def fetch(x, src_of):
            return lax.ppermute(x, "face", [(src_of(i), i) for i in range(n)])

        moved_chips = moved.reshape(tokens, 2, 2 * rows).transpose(1, 0, 2)

        def chip_weight(same_core, other_core):
            stack = jnp.zeros((2,) + w_qkv.shape, w_qkv.dtype)
            stack = lax.dynamic_update_index_in_dim(stack, same_core, core, 0)
            stack = lax.dynamic_update_index_in_dim(stack, other_core, 1 - core, 0)
            return stack.reshape(2 * rows, w_qkv.shape[1])

        def chip_part(chip, weight):
            return jnp.dot(
                lax.dynamic_index_in_dim(moved_chips, chip, 0, keepdims=False),
                weight,
                preferred_element_type=jnp.float32,
            )

        sib = fetch(w_qkv, lambda i: i ^ 1)
        far = fetch(w_qkv, lambda i: (i + 2) % n)
        local = chip_part(me // 2, chip_weight(w_qkv, sib))
        local, far = lax.optimization_barrier((local, far))
        fwd = fetch(far, lambda i: i ^ 1)
        qkv_sums = local + chip_part(1 - me // 2, chip_weight(far, fwd))
        w_out_late, _ = lax.optimization_barrier((w_out, (far, fwd)))
    else:
        qkv_pieces = face_pieces(w_qkv)
        w_out_late, _ = lax.optimization_barrier((w_out, [piece for piece, _ in qkv_pieces]))
        qkv_stack = jnp.zeros((n,) + w_qkv.shape, w_qkv.dtype)
        for piece, index in qkv_pieces:
            qkv_stack = lax.dynamic_update_index_in_dim(qkv_stack, piece, index, 0)
        w_qkv_full = qkv_stack.reshape(n * rows, w_qkv.shape[1])
        qkv_sums = jnp.dot(moved, w_qkv_full, preferred_element_type=jnp.float32)
    qkv_all = qkv_sums.astype(jnp.bfloat16)

    out_stack = jnp.zeros((n,) + w_out.shape, w_out.dtype)
    for piece, index in face_pieces(w_out_late):
        out_stack = lax.dynamic_update_index_in_dim(out_stack, piece, index, 0)
    w_out_full = out_stack.transpose(1, 0, 2).reshape(w_out.shape[0], n * w_out.shape[1])

    split = qkv_all.reshape(tokens, 3, HEADS, HD)
    queries = split[:, 0].transpose(1, 0, 2)
    keys = split[:, 1].transpose(1, 2, 0)
    values = split[:, 2].transpose(1, 0, 2)
    rim = OVT * S * S
    mid_a = rim + ((tokens - 2 * rim) // (2 * S * S)) * (S * S)
    gate = modulation[2]

    def tile_part(part_queries, part_in):
        return attend_project(part_queries, keys, values, w_out_full, part_in, gate)

    my_rows = lax.dynamic_index_in_dim(edge_table, lax.axis_index("face"), 0, keepdims=False)
    flips = my_rows[:, 2]
    routes = my_rows[:, 3]
    send_match = routes[None, :] == jnp.asarray(PARTNER_ROUTE, jnp.int32)[:, None]
    recv_match = routes[None, :] == jnp.arange(4, dtype=jnp.int32)[:, None]
    ramp = space_ramp.astype(jnp.float32)
    keep = ramp / (ramp + ramp[::-1])
    take = ramp[::-1] / (ramp + ramp[::-1])

    def strips_out(tile_out):
        part_tokens = tile_out.shape[0]
        part_frames = part_tokens // (S * S)
        _, send_table = strip_tables(part_frames)
        send_by_edge = jnp.where(flips[:, None] > 0, send_table[:, 1], send_table[:, 0])
        send_cells = jnp.sum(jnp.where(send_match[:, :, None], send_by_edge[None], 0), axis=1)
        send_cells = send_cells.reshape(-1)
        token_ids = jnp.arange(part_tokens, dtype=jnp.int32)
        pick = (send_cells[:, None] == token_ids[None, :]).astype(jnp.bfloat16)
        return jnp.dot(pick, tile_out, preferred_element_type=jnp.float32).astype(jnp.bfloat16)

    def strips_in(outgoing):
        strip_len = outgoing.shape[0] // 4
        arrived = []
        for route_id in range(4):
            sent = outgoing[route_id * strip_len : (route_id + 1) * strip_len]
            shift = -OFFSETS[route_id]
            arrived.append(
                lax.ppermute(sent, "face", [(i, (i + shift) % n) for i in range(n)])
            )
        return jnp.concatenate(arrived, axis=0)

    def space_blend(tile_out, arrived):
        part_tokens = tile_out.shape[0]
        part_frames = part_tokens // (S * S)
        recv_table, _ = strip_tables(part_frames)
        recv_cells = jnp.sum(jnp.where(recv_match[:, :, None], recv_table[None], 0), axis=1)
        recv_cells = recv_cells.reshape(-1)
        token_ids = jnp.arange(part_tokens, dtype=jnp.int32)
        place = (token_ids[:, None] == recv_cells[None, :]).astype(jnp.bfloat16)
        partner = jnp.dot(place, arrived, preferred_element_type=jnp.float32)
        dep = strip_depth(part_frames)[:, None]
        w_keep = jnp.where(dep == 0, keep[0], keep[1])
        w_take = jnp.where(dep == 0, take[0], take[1])
        own = tile_out.astype(jnp.float32)
        return jnp.where(dep >= 0, w_keep * own + w_take * partner, own).astype(jnp.bfloat16)

    rim_queries = jnp.concatenate([queries[:, :rim], queries[:, tokens - rim :]], axis=1)
    rim_in = jnp.concatenate([block_in[:rim], block_in[tokens - rim :]], axis=0)
    tile_rim = tile_part(rim_queries, rim_in)
    outgoing_rim = strips_out(tile_rim)
    arrived_rim = strips_in(outgoing_rim)
    first_queries, outgoing_rim = lax.optimization_barrier((queries[:, rim:mid_a], outgoing_rim))
    tile_first = tile_part(first_queries, block_in[rim:mid_a])
    arrived_rim, tile_first = lax.optimization_barrier((arrived_rim, tile_first))
    spaced_rim = space_blend(tile_rim, arrived_rim)
    low, high = lax.optimization_barrier((spaced_rim[:rim], spaced_rim[rim:]))
    count = lax.axis_size("tm")
    lower = lax.ppermute(high, "tm", [(i, i + 1) for i in range(count - 1)])
    upper = lax.ppermute(low, "tm", [(i + 1, i) for i in range(count - 1)])
    second_queries, low, high = lax.optimization_barrier(
        (queries[:, mid_a : tokens - rim], low, high)
    )
    tile_second = tile_part(second_queries, block_in[mid_a : tokens - rim])
    lower, upper, tile_second = lax.optimization_barrier((lower, upper, tile_second))
    tile_mid = jnp.concatenate([tile_first, tile_second], axis=0)
    spaced_mid = space_blend(tile_mid, strips_in(strips_out(tile_mid)))

    span_id = lax.axis_index("tm")
    has_lower = span_id > 0
    has_upper = span_id < count - 1
    tramp = time_ramp.astype(jnp.float32)
    hold = tramp / (tramp + tramp[::-1])
    pass_ = tramp[::-1] / (tramp + tramp[::-1])
    blocks = (OVT, S * S, D)
    low_f = low.astype(jnp.float32).reshape(blocks)
    high_f = high.astype(jnp.float32).reshape(blocks)
    hold_low = hold[:, None, None]
    pass_low = pass_[:, None, None]
    hold_high = hold[::-1][:, None, None]
    pass_high = pass_[::-1][:, None, None]
    low_mix = jnp.where(
        has_lower, hold_low * low_f + pass_low * lower.astype(jnp.float32).reshape(blocks), low_f
    ).reshape(rim, D)
    high_mix = jnp.where(
        has_upper, hold_high * high_f + pass_high * upper.astype(jnp.float32).reshape(blocks), high_f
    ).reshape(rim, D)
    result = jnp.concatenate(
        [low_mix.astype(jnp.bfloat16), spaced_mid, high_mix.astype(jnp.bfloat16)], axis=0
    )
    return result.reshape(1, 1, tokens, D)


def solution(mesh):
    return jax.shard_map(
        per_device,
        mesh=mesh,
        in_specs=(
            P(("groups", "tm"), "face", None, None),
            P("groups", None),
            P("face", None),
            P(None, "face"),
            P(),
            P(),
            P(),
        ),
        out_specs=P(("groups", "tm"), "face", None, None),
        check_vma=False,
    )
```

```python
import math

import jax
import jax.numpy as jnp
import numpy as np
from jax import lax
from jax.experimental import pallas as pl
from jax.experimental.pallas import tpu as pltpu
from jax.sharding import PartitionSpec as P

D = 1152
HD = 72
HEADS = 8
S = 8
OVS = 2
OVT = 4
MID = S - 2 * OVS


NORM_EPS = 1e-06
OFFSETS = (1, -1, 2, -2)
PARTNER_ROUTE = (1, 0, 3, 2)


def modulate(block_in, modulation):
    values = block_in.astype(jnp.float32)
    center = jnp.mean(values, axis=-1, keepdims=True)
    spread = jnp.mean(jnp.square(values - center), axis=-1, keepdims=True)
    normed = (values - center) * lax.rsqrt(spread + NORM_EPS)
    return (normed * (1.0 + modulation[1]) + modulation[0]).astype(jnp.bfloat16)


def attention_kernel(q_ref, k_ref, v_ref, o_ref):
    for j in range(q_ref.shape[0]):
        scores = jnp.dot(q_ref[j], k_ref[j], preferred_element_type=jnp.float32) * (
            1.0 / math.sqrt(HD)
        )
        row_max = jnp.max(scores, axis=-1, keepdims=True)
        weights = jnp.exp(scores - row_max)
        row_sum = jnp.sum(weights, axis=-1, keepdims=True)
        probabilities = (weights * (1.0 / row_sum)).astype(jnp.bfloat16)
        o_ref[:, j * HD : (j + 1) * HD] = jnp.dot(
            probabilities, v_ref[j], preferred_element_type=jnp.float32
        ).astype(o_ref.dtype)


def attend_project(queries, keys, values, w_out_full, block_in, gate):
    heads, size, tokens = keys.shape
    chunk = queries.shape[1]
    mixed = pl.pallas_call(
        attention_kernel,
        out_shape=jax.ShapeDtypeStruct((chunk, heads * size), queries.dtype),
    )(queries, keys, values)
    projected = jnp.dot(mixed, w_out_full, preferred_element_type=jnp.float32)
    return (block_in.astype(jnp.float32) + gate * projected).astype(block_in.dtype)


def face_pieces(shard):
    n = lax.axis_size("face")
    me = lax.axis_index("face")

    def fetch(x, src_of):
        return lax.ppermute(x, "face", [(src_of(i), i) for i in range(n)])

    pieces = [(shard, me), (fetch(shard, lambda i: i ^ 1), me ^ 1)]
    for j in range(1, n // 2):
        far = fetch(shard, lambda i: (i + 2 * j) % n)
        pieces.append((far, (me + 2 * j) % n))
        pieces.append((fetch(far, lambda i: i ^ 1), ((me ^ 1) + 2 * j) % n))
    return pieces


def strip_tables(frames):
    frame, depth, pos = np.meshgrid(
        np.arange(frames), np.arange(OVS), np.arange(MID), indexing="ij"
    )

    def token(edge, d, t):
        row = (d, S - 1 - d, OVS + t, OVS + t)[edge]
        col = (OVS + t, OVS + t, d, S - 1 - d)[edge]
        return (frame * (S * S) + row * S + col).reshape(-1)

    recv = np.stack([token(e, depth, pos) for e in range(4)])
    send = np.stack(
        [[token(e, OVS - 1 - depth, pos if flip == 0 else MID - 1 - pos) for flip in range(2)]
         for e in range(4)]
    )
    return recv.astype(np.int32), send.astype(np.int32)


def strip_depth(frames):
    grid = np.full((S, S), -1, np.int32)
    for d in range(OVS):
        grid[d, OVS : S - OVS] = d
        grid[S - 1 - d, OVS : S - OVS] = d
        grid[OVS : S - OVS, d] = d
        grid[OVS : S - OVS, S - 1 - d] = d
    return np.tile(grid.reshape(-1), frames)


def per_device(latents, modulation, w_qkv, w_out, edge_table, space_ramp, time_ramp):
    block_in = latents[0, 0]
    tokens = block_in.shape[0]
    frames = tokens // (S * S)
    n = lax.axis_size("face")
    rows = w_qkv.shape[0]
    moved = modulate(block_in, modulation)
    if n == 4:
        me = lax.axis_index("face")
        core = me % 2

        def fetch(x, src_of):
            return lax.ppermute(x, "face", [(src_of(i), i) for i in range(n)])

        moved_chips = moved.reshape(tokens, 2, 2 * rows).transpose(1, 0, 2)

        def chip_weight(same_core, other_core):
            stack = jnp.zeros((2,) + w_qkv.shape, w_qkv.dtype)
            stack = lax.dynamic_update_index_in_dim(stack, same_core, core, 0)
            stack = lax.dynamic_update_index_in_dim(stack, other_core, 1 - core, 0)
            return stack.reshape(2 * rows, w_qkv.shape[1])

        def chip_part(chip, weight):
            return jnp.dot(
                lax.dynamic_index_in_dim(moved_chips, chip, 0, keepdims=False),
                weight,
                preferred_element_type=jnp.float32,
            )

        sib = fetch(w_qkv, lambda i: i ^ 1)
        far = fetch(w_qkv, lambda i: (i + 2) % n)
        local = chip_part(me // 2, chip_weight(w_qkv, sib))
        local, far = lax.optimization_barrier((local, far))
        fwd = fetch(far, lambda i: i ^ 1)
        qkv_sums = local + chip_part(1 - me // 2, chip_weight(far, fwd))
        w_out_late, _ = lax.optimization_barrier((w_out, (far, fwd)))
    else:
        qkv_pieces = face_pieces(w_qkv)
        w_out_late, _ = lax.optimization_barrier((w_out, [piece for piece, _ in qkv_pieces]))
        qkv_stack = jnp.zeros((n,) + w_qkv.shape, w_qkv.dtype)
        for piece, index in qkv_pieces:
            qkv_stack = lax.dynamic_update_index_in_dim(qkv_stack, piece, index, 0)
        w_qkv_full = qkv_stack.reshape(n * rows, w_qkv.shape[1])
        qkv_sums = jnp.dot(moved, w_qkv_full, preferred_element_type=jnp.float32)
    qkv_all = qkv_sums.astype(jnp.bfloat16)

    out_stack = jnp.zeros((n,) + w_out.shape, w_out.dtype)
    for piece, index in face_pieces(w_out_late):
        out_stack = lax.dynamic_update_index_in_dim(out_stack, piece, index, 0)
    w_out_full = out_stack.transpose(1, 0, 2).reshape(w_out.shape[0], n * w_out.shape[1])

    split = qkv_all.reshape(tokens, 3, HEADS, HD)
    queries = split[:, 0].transpose(1, 0, 2)
    keys = split[:, 1].transpose(1, 2, 0)
    values = split[:, 2].transpose(1, 0, 2)
    rim = OVT * S * S
    mid_a = rim + ((tokens - 2 * rim) // (2 * S * S)) * (S * S)
    gate = modulation[2]

    def tile_part(part_queries, part_in):
        return attend_project(part_queries, keys, values, w_out_full, part_in, gate)

    my_rows = lax.dynamic_index_in_dim(edge_table, lax.axis_index("face"), 0, keepdims=False)
    flips = my_rows[:, 2]
    routes = my_rows[:, 3]
    send_match = routes[None, :] == jnp.asarray(PARTNER_ROUTE, jnp.int32)[:, None]
    recv_match = routes[None, :] == jnp.arange(4, dtype=jnp.int32)[:, None]
    ramp = space_ramp.astype(jnp.float32)
    keep = ramp / (ramp + ramp[::-1])
    take = ramp[::-1] / (ramp + ramp[::-1])

    def strips_out(tile_out):
        part_tokens = tile_out.shape[0]
        part_frames = part_tokens // (S * S)
        _, send_table = strip_tables(part_frames)
        send_by_edge = jnp.where(flips[:, None] > 0, send_table[:, 1], send_table[:, 0])
        send_cells = jnp.sum(jnp.where(send_match[:, :, None], send_by_edge[None], 0), axis=1)
        send_cells = send_cells.reshape(-1)
        token_ids = jnp.arange(part_tokens, dtype=jnp.int32)
        pick = (send_cells[:, None] == token_ids[None, :]).astype(jnp.bfloat16)
        return jnp.dot(pick, tile_out, preferred_element_type=jnp.float32).astype(jnp.bfloat16)

    def strips_in(outgoing):
        strip_len = outgoing.shape[0] // 4
        arrived = []
        for route_id in range(4):
            sent = outgoing[route_id * strip_len : (route_id + 1) * strip_len]
            shift = -OFFSETS[route_id]
            arrived.append(
                lax.ppermute(sent, "face", [(i, (i + shift) % n) for i in range(n)])
            )
        return jnp.concatenate(arrived, axis=0)

    def space_blend(tile_out, arrived):
        part_tokens = tile_out.shape[0]
        part_frames = part_tokens // (S * S)
        recv_table, _ = strip_tables(part_frames)
        recv_cells = jnp.sum(jnp.where(recv_match[:, :, None], recv_table[None], 0), axis=1)
        recv_cells = recv_cells.reshape(-1)
        token_ids = jnp.arange(part_tokens, dtype=jnp.int32)
        place = (token_ids[:, None] == recv_cells[None, :]).astype(jnp.bfloat16)
        partner = jnp.dot(place, arrived, preferred_element_type=jnp.float32)
        dep = strip_depth(part_frames)[:, None]
        w_keep = jnp.where(dep == 0, keep[0], keep[1])
        w_take = jnp.where(dep == 0, take[0], take[1])
        own = tile_out.astype(jnp.float32)
        return jnp.where(dep >= 0, w_keep * own + w_take * partner, own).astype(jnp.bfloat16)

    rim_queries = jnp.concatenate([queries[:, :rim], queries[:, tokens - rim :]], axis=1)
    rim_in = jnp.concatenate([block_in[:rim], block_in[tokens - rim :]], axis=0)
    tile_rim = tile_part(rim_queries, rim_in)
    outgoing_rim = strips_out(tile_rim)
    arrived_rim = strips_in(outgoing_rim)
    first_queries, outgoing_rim = lax.optimization_barrier((queries[:, rim:mid_a], outgoing_rim))
    tile_first = tile_part(first_queries, block_in[rim:mid_a])
    arrived_rim, tile_first = lax.optimization_barrier((arrived_rim, tile_first))
    spaced_rim = space_blend(tile_rim, arrived_rim)
    low, high = lax.optimization_barrier((spaced_rim[:rim], spaced_rim[rim:]))
    count = lax.axis_size("tm")
    lower = lax.ppermute(high, "tm", [(i, i + 1) for i in range(count - 1)])
    upper = lax.ppermute(low, "tm", [(i + 1, i) for i in range(count - 1)])
    second_queries, low, high = lax.optimization_barrier(
        (queries[:, mid_a : tokens - rim], low, high)
    )
    tile_second = tile_part(second_queries, block_in[mid_a : tokens - rim])
    lower, upper, tile_second = lax.optimization_barrier((lower, upper, tile_second))
    tile_mid = jnp.concatenate([tile_first, tile_second], axis=0)
    spaced_mid = space_blend(tile_mid, strips_in(strips_out(tile_mid)))

    span_id = lax.axis_index("tm")
    has_lower = span_id > 0
    has_upper = span_id < count - 1
    tramp = time_ramp.astype(jnp.float32)
    hold = tramp / (tramp + tramp[::-1])
    pass_ = tramp[::-1] / (tramp + tramp[::-1])
    blocks = (OVT, S * S, D)
    low_f = low.astype(jnp.float32).reshape(blocks)
    high_f = high.astype(jnp.float32).reshape(blocks)
    hold_low = hold[:, None, None]
    pass_low = pass_[:, None, None]
    hold_high = hold[::-1][:, None, None]
    pass_high = pass_[::-1][:, None, None]
    low_mix = jnp.where(
        has_lower, hold_low * low_f + pass_low * lower.astype(jnp.float32).reshape(blocks), low_f
    ).reshape(rim, D)
    high_mix = jnp.where(
        has_upper, hold_high * high_f + pass_high * upper.astype(jnp.float32).reshape(blocks), high_f
    ).reshape(rim, D)
    result = jnp.concatenate(
        [low_mix.astype(jnp.bfloat16), spaced_mid, high_mix.astype(jnp.bfloat16)], axis=0
    )
    return result.reshape(1, 1, tokens, D)


def solution(mesh):
    return jax.shard_map(
        per_device,
        mesh=mesh,
        in_specs=(
            P(("groups", "tm"), "face", None, None),
            P("groups", None),
            P("face", None),
            P(None, "face"),
            P(),
            P(),
            P(),
        ),
        out_specs=P(("groups", "tm"), "face", None, None),
        check_vma=False,
    )
```

```python
import math

import jax
import jax.numpy as jnp
import numpy as np
from jax import lax
from jax.experimental import pallas as pl
from jax.experimental.pallas import tpu as pltpu
from jax.sharding import PartitionSpec as P

D = 1152
HD = 72
HEADS = 8
S = 8
OVS = 2
OVT = 4
MID = S - 2 * OVS


NORM_EPS = 1e-06
OFFSETS = (1, -1, 2, -2)
PARTNER_ROUTE = (1, 0, 3, 2)


def modulate(block_in, modulation):
    values = block_in.astype(jnp.float32)
    center = jnp.mean(values, axis=-1, keepdims=True)
    spread = jnp.mean(jnp.square(values - center), axis=-1, keepdims=True)
    normed = (values - center) * lax.rsqrt(spread + NORM_EPS)
    return (normed * (1.0 + modulation[1]) + modulation[0]).astype(jnp.bfloat16)


HEADS_PER_STEP = 2


def attention_kernel(*refs):
    x_ref, g_ref, o_ref, acc_ref = refs[-4:]
    per_head = refs[:-4]
    step = pl.program_id(1)

    @pl.when(step == 0)
    def _():
        acc_ref[...] = jnp.zeros_like(acc_ref)

    total = None
    for j in range(HEADS_PER_STEP):
        q_ref, k_ref, v_ref, w_ref = per_head[4 * j : 4 * j + 4]
        scores = jnp.dot(q_ref[0], k_ref[0], preferred_element_type=jnp.float32) * (
            1.0 / math.sqrt(HD)
        )
        row_max = jnp.max(scores, axis=-1, keepdims=True)
        weights = jnp.exp(scores - row_max)
        row_sum = jnp.sum(weights, axis=-1, keepdims=True)
        probabilities = (weights * (1.0 / row_sum)).astype(jnp.bfloat16)
        mixed = jnp.dot(probabilities, v_ref[0], preferred_element_type=jnp.float32).astype(
            jnp.bfloat16
        )
        part = jnp.dot(mixed, w_ref[...], preferred_element_type=jnp.float32)
        total = part if total is None else total + part
    acc_ref[...] += total

    @pl.when(step == pl.num_programs(1) - 1)
    def _():
        o_ref[...] = (x_ref[...].astype(jnp.float32) + g_ref[...] * acc_ref[...]).astype(
            o_ref.dtype
        )


def attend_project(queries, keys, values, w_out_full, block_in, gate):
    heads, size, tokens = keys.shape
    chunk = queries.shape[1]
    width = block_in.shape[1]
    hb = HEADS_PER_STEP
    in_specs = []
    operands = []
    for j in range(hb):
        in_specs += [
            pl.BlockSpec((1, chunk, size), lambda i, h, j=j: (hb * h + j, i, 0)),
            pl.BlockSpec((1, size, tokens), lambda i, h, j=j: (hb * h + j, 0, 0)),
            pl.BlockSpec((1, tokens, size), lambda i, h, j=j: (hb * h + j, 0, 0)),
            pl.BlockSpec((size, width), lambda i, h, j=j: (hb * h + j, 0)),
        ]
        operands += [queries, keys, values, w_out_full]
    in_specs += [
        pl.BlockSpec((chunk, width), lambda i, h: (i, 0)),
        pl.BlockSpec((1, width), lambda i, h: (0, 0)),
    ]
    return pl.pallas_call(
        attention_kernel,
        grid=(1, heads // hb),
        in_specs=in_specs,
        out_specs=pl.BlockSpec((chunk, width), lambda i, h: (i, 0)),
        out_shape=jax.ShapeDtypeStruct(block_in.shape, block_in.dtype),
        scratch_shapes=[pltpu.VMEM((chunk, width), jnp.float32)],
        compiler_params=pltpu.CompilerParams(dimension_semantics=("arbitrary", "arbitrary")),
    )(*operands, block_in, gate.reshape(1, width))


def face_pieces(shard):
    n = lax.axis_size("face")
    me = lax.axis_index("face")

    def fetch(x, src_of):
        return lax.ppermute(x, "face", [(src_of(i), i) for i in range(n)])

    pieces = [(shard, me), (fetch(shard, lambda i: i ^ 1), me ^ 1)]
    for j in range(1, n // 2):
        far = fetch(shard, lambda i: (i + 2 * j) % n)
        pieces.append((far, (me + 2 * j) % n))
        pieces.append((fetch(far, lambda i: i ^ 1), ((me ^ 1) + 2 * j) % n))
    return pieces


def strip_tables(frames):
    frame, depth, pos = np.meshgrid(
        np.arange(frames), np.arange(OVS), np.arange(MID), indexing="ij"
    )

    def token(edge, d, t):
        row = (d, S - 1 - d, OVS + t, OVS + t)[edge]
        col = (OVS + t, OVS + t, d, S - 1 - d)[edge]
        return (frame * (S * S) + row * S + col).reshape(-1)

    recv = np.stack([token(e, depth, pos) for e in range(4)])
    send = np.stack(
        [[token(e, OVS - 1 - depth, pos if flip == 0 else MID - 1 - pos) for flip in range(2)]
         for e in range(4)]
    )
    return recv.astype(np.int32), send.astype(np.int32)


def strip_depth(frames):
    grid = np.full((S, S), -1, np.int32)
    for d in range(OVS):
        grid[d, OVS : S - OVS] = d
        grid[S - 1 - d, OVS : S - OVS] = d
        grid[OVS : S - OVS, d] = d
        grid[OVS : S - OVS, S - 1 - d] = d
    return np.tile(grid.reshape(-1), frames)


def per_device(latents, modulation, w_qkv, w_out, edge_table, space_ramp, time_ramp):
    block_in = latents[0, 0]
    tokens = block_in.shape[0]
    frames = tokens // (S * S)
    n = lax.axis_size("face")
    rows = w_qkv.shape[0]
    moved = modulate(block_in, modulation)
    if n == 4:
        me = lax.axis_index("face")
        core = me % 2

        def fetch(x, src_of):
            return lax.ppermute(x, "face", [(src_of(i), i) for i in range(n)])

        moved_chips = moved.reshape(tokens, 2, 2 * rows).transpose(1, 0, 2)

        def chip_weight(same_core, other_core):
            stack = jnp.zeros((2,) + w_qkv.shape, w_qkv.dtype)
            stack = lax.dynamic_update_index_in_dim(stack, same_core, core, 0)
            stack = lax.dynamic_update_index_in_dim(stack, other_core, 1 - core, 0)
            return stack.reshape(2 * rows, w_qkv.shape[1])

        def chip_part(chip, weight):
            return jnp.dot(
                lax.dynamic_index_in_dim(moved_chips, chip, 0, keepdims=False),
                weight,
                preferred_element_type=jnp.float32,
            )

        sib = fetch(w_qkv, lambda i: i ^ 1)
        far = fetch(w_qkv, lambda i: (i + 2) % n)
        local = chip_part(me // 2, chip_weight(w_qkv, sib))
        local, far = lax.optimization_barrier((local, far))
        fwd = fetch(far, lambda i: i ^ 1)
        qkv_sums = local + chip_part(1 - me // 2, chip_weight(far, fwd))
        w_out_late, _ = lax.optimization_barrier((w_out, (far, fwd)))
    else:
        qkv_pieces = face_pieces(w_qkv)
        w_out_late, _ = lax.optimization_barrier((w_out, [piece for piece, _ in qkv_pieces]))
        qkv_stack = jnp.zeros((n,) + w_qkv.shape, w_qkv.dtype)
        for piece, index in qkv_pieces:
            qkv_stack = lax.dynamic_update_index_in_dim(qkv_stack, piece, index, 0)
        w_qkv_full = qkv_stack.reshape(n * rows, w_qkv.shape[1])
        qkv_sums = jnp.dot(moved, w_qkv_full, preferred_element_type=jnp.float32)
    qkv_all = qkv_sums.astype(jnp.bfloat16)

    out_stack = jnp.zeros((n,) + w_out.shape, w_out.dtype)
    for piece, index in face_pieces(w_out_late):
        out_stack = lax.dynamic_update_index_in_dim(out_stack, piece, index, 0)
    w_out_full = out_stack.transpose(1, 0, 2).reshape(w_out.shape[0], n * w_out.shape[1])

    split = qkv_all.reshape(tokens, 3, HEADS, HD)
    queries = split[:, 0].transpose(1, 0, 2)
    keys = split[:, 1].transpose(1, 2, 0)
    values = split[:, 2].transpose(1, 0, 2)
    rim = OVT * S * S
    mid_a = rim + ((tokens - 2 * rim) // (2 * S * S)) * (S * S)
    gate = modulation[2]

    def tile_part(part_queries, part_in):
        return attend_project(part_queries, keys, values, w_out_full, part_in, gate)

    my_rows = lax.dynamic_index_in_dim(edge_table, lax.axis_index("face"), 0, keepdims=False)
    flips = my_rows[:, 2]
    routes = my_rows[:, 3]
    send_match = routes[None, :] == jnp.asarray(PARTNER_ROUTE, jnp.int32)[:, None]
    recv_match = routes[None, :] == jnp.arange(4, dtype=jnp.int32)[:, None]
    ramp = space_ramp.astype(jnp.float32)
    keep = ramp / (ramp + ramp[::-1])
    take = ramp[::-1] / (ramp + ramp[::-1])

    def strips_out(tile_out):
        part_tokens = tile_out.shape[0]
        part_frames = part_tokens // (S * S)
        _, send_table = strip_tables(part_frames)
        send_by_edge = jnp.where(flips[:, None] > 0, send_table[:, 1], send_table[:, 0])
        send_cells = jnp.sum(jnp.where(send_match[:, :, None], send_by_edge[None], 0), axis=1)
        send_cells = send_cells.reshape(-1)
        token_ids = jnp.arange(part_tokens, dtype=jnp.int32)
        pick = (send_cells[:, None] == token_ids[None, :]).astype(jnp.bfloat16)
        return jnp.dot(pick, tile_out, preferred_element_type=jnp.float32).astype(jnp.bfloat16)

    def strips_in(outgoing):
        strip_len = outgoing.shape[0] // 4
        arrived = []
        for route_id in range(4):
            sent = outgoing[route_id * strip_len : (route_id + 1) * strip_len]
            shift = -OFFSETS[route_id]
            arrived.append(
                lax.ppermute(sent, "face", [(i, (i + shift) % n) for i in range(n)])
            )
        return jnp.concatenate(arrived, axis=0)

    def space_blend(tile_out, arrived):
        part_tokens = tile_out.shape[0]
        part_frames = part_tokens // (S * S)
        recv_table, _ = strip_tables(part_frames)
        recv_cells = jnp.sum(jnp.where(recv_match[:, :, None], recv_table[None], 0), axis=1)
        recv_cells = recv_cells.reshape(-1)
        token_ids = jnp.arange(part_tokens, dtype=jnp.int32)
        place = (token_ids[:, None] == recv_cells[None, :]).astype(jnp.bfloat16)
        partner = jnp.dot(place, arrived, preferred_element_type=jnp.float32)
        dep = strip_depth(part_frames)[:, None]
        own = tile_out.astype(jnp.float32)
        mixed = jnp.where(
            dep == 0,
            keep[0] * own + take[0] * partner,
            jnp.where(dep == 1, keep[1] * own + take[1] * partner, own),
        )
        return mixed.astype(jnp.bfloat16)

    rim_queries = jnp.concatenate([queries[:, :rim], queries[:, tokens - rim :]], axis=1)
    rim_in = jnp.concatenate([block_in[:rim], block_in[tokens - rim :]], axis=0)
    tile_rim = tile_part(rim_queries, rim_in)
    outgoing_rim = strips_out(tile_rim)
    arrived_rim = strips_in(outgoing_rim)
    first_queries, outgoing_rim = lax.optimization_barrier((queries[:, rim:mid_a], outgoing_rim))
    tile_first = tile_part(first_queries, block_in[rim:mid_a])
    arrived_rim, tile_first = lax.optimization_barrier((arrived_rim, tile_first))
    spaced_rim = space_blend(tile_rim, arrived_rim)
    low, high = lax.optimization_barrier((spaced_rim[:rim], spaced_rim[rim:]))
    count = lax.axis_size("tm")
    lower = lax.ppermute(high, "tm", [(i, i + 1) for i in range(count - 1)])
    upper = lax.ppermute(low, "tm", [(i + 1, i) for i in range(count - 1)])
    outgoing_first = strips_out(tile_first)
    arrived_first = strips_in(outgoing_first)
    second_queries, low, high, outgoing_first = lax.optimization_barrier(
        (queries[:, mid_a : tokens - rim], low, high, outgoing_first)
    )
    tile_second = tile_part(second_queries, block_in[mid_a : tokens - rim])
    lower, upper, arrived_first, tile_second = lax.optimization_barrier(
        (lower, upper, arrived_first, tile_second)
    )
    spaced_mid = jnp.concatenate(
        [
            space_blend(tile_first, arrived_first),
            space_blend(tile_second, strips_in(strips_out(tile_second))),
        ],
        axis=0,
    )

    span_id = lax.axis_index("tm")
    has_lower = span_id > 0
    has_upper = span_id < count - 1
    tramp = time_ramp.astype(jnp.float32)
    hold = tramp / (tramp + tramp[::-1])
    pass_ = tramp[::-1] / (tramp + tramp[::-1])
    blocks = (OVT, S * S, D)
    low_f = low.astype(jnp.float32).reshape(blocks)
    high_f = high.astype(jnp.float32).reshape(blocks)
    hold_low = hold[:, None, None]
    pass_low = pass_[:, None, None]
    hold_high = hold[::-1][:, None, None]
    pass_high = pass_[::-1][:, None, None]
    low_mix = jnp.where(
        has_lower, hold_low * low_f + pass_low * lower.astype(jnp.float32).reshape(blocks), low_f
    ).reshape(rim, D)
    high_mix = jnp.where(
        has_upper, hold_high * high_f + pass_high * upper.astype(jnp.float32).reshape(blocks), high_f
    ).reshape(rim, D)
    result = jnp.concatenate(
        [low_mix.astype(jnp.bfloat16), spaced_mid, high_mix.astype(jnp.bfloat16)], axis=0
    )
    return result.reshape(1, 1, tokens, D)


def solution(mesh):
    return jax.shard_map(
        per_device,
        mesh=mesh,
        in_specs=(
            P(("groups", "tm"), "face", None, None),
            P("groups", None),
            P("face", None),
            P(None, "face"),
            P(),
            P(),
            P(),
        ),
        out_specs=P(("groups", "tm"), "face", None, None),
        check_vma=False,
    )
```

```python
import math

import jax
import jax.numpy as jnp
import numpy as np
from jax import lax
from jax.experimental import pallas as pl
from jax.experimental.pallas import tpu as pltpu
from jax.sharding import PartitionSpec as P

D = 1152
HD = 72
HEADS = 8
S = 8
OVS = 2
OVT = 4
MID = S - 2 * OVS


NORM_EPS = 1e-06
OFFSETS = (1, -1, 2, -2)
PARTNER_ROUTE = (1, 0, 3, 2)


def modulate(block_in, modulation):
    values = block_in.astype(jnp.float32)
    center = jnp.mean(values, axis=-1, keepdims=True)
    spread = jnp.mean(jnp.square(values - center), axis=-1, keepdims=True)
    normed = (values - center) * lax.rsqrt(spread + NORM_EPS)
    return (normed * (1.0 + modulation[1]) + modulation[0]).astype(jnp.bfloat16)


HEADS_PER_STEP = 2


def attention_kernel(*refs):
    x_ref, g_ref, o_ref, acc_ref = refs[-4:]
    per_head = refs[:-4]
    step = pl.program_id(1)

    @pl.when(step == 0)
    def _():
        acc_ref[...] = jnp.zeros_like(acc_ref)

    total = None
    for j in range(HEADS_PER_STEP):
        q_ref, k_ref, v_ref, w_ref = per_head[4 * j : 4 * j + 4]
        scores = jnp.dot(q_ref[0], k_ref[0], preferred_element_type=jnp.float32) * (
            1.0 / math.sqrt(HD)
        )
        row_max = jnp.max(scores, axis=-1, keepdims=True)
        weights = jnp.exp(scores - row_max)
        row_sum = jnp.sum(weights, axis=-1, keepdims=True)
        probabilities = (weights * (1.0 / row_sum)).astype(jnp.bfloat16)
        mixed = jnp.dot(probabilities, v_ref[0], preferred_element_type=jnp.float32).astype(
            jnp.bfloat16
        )
        part = jnp.dot(mixed, w_ref[...], preferred_element_type=jnp.float32)
        total = part if total is None else total + part
    acc_ref[...] += total

    @pl.when(step == pl.num_programs(1) - 1)
    def _():
        o_ref[...] = (x_ref[...].astype(jnp.float32) + g_ref[...] * acc_ref[...]).astype(
            o_ref.dtype
        )


def attend_project(queries, keys, values, w_out_full, block_in, gate):
    heads, size, tokens = keys.shape
    chunk = queries.shape[1]
    width = block_in.shape[1]
    hb = HEADS_PER_STEP
    in_specs = []
    operands = []
    for j in range(hb):
        in_specs += [
            pl.BlockSpec((1, chunk, size), lambda i, h, j=j: (hb * h + j, i, 0)),
            pl.BlockSpec((1, size, tokens), lambda i, h, j=j: (hb * h + j, 0, 0)),
            pl.BlockSpec((1, tokens, size), lambda i, h, j=j: (hb * h + j, 0, 0)),
            pl.BlockSpec((size, width), lambda i, h, j=j: (hb * h + j, 0)),
        ]
        operands += [queries, keys, values, w_out_full]
    in_specs += [
        pl.BlockSpec((chunk, width), lambda i, h: (i, 0)),
        pl.BlockSpec((1, width), lambda i, h: (0, 0)),
    ]
    return pl.pallas_call(
        attention_kernel,
        grid=(1, heads // hb),
        in_specs=in_specs,
        out_specs=pl.BlockSpec((chunk, width), lambda i, h: (i, 0)),
        out_shape=jax.ShapeDtypeStruct(block_in.shape, block_in.dtype),
        scratch_shapes=[pltpu.VMEM((chunk, width), jnp.float32)],
        compiler_params=pltpu.CompilerParams(dimension_semantics=("arbitrary", "arbitrary")),
    )(*operands, block_in, gate.reshape(1, width))


def face_pieces(shard):
    n = lax.axis_size("face")
    me = lax.axis_index("face")

    def fetch(x, src_of):
        return lax.ppermute(x, "face", [(src_of(i), i) for i in range(n)])

    pieces = [(shard, me), (fetch(shard, lambda i: i ^ 1), me ^ 1)]
    for j in range(1, n // 2):
        far = fetch(shard, lambda i: (i + 2 * j) % n)
        pieces.append((far, (me + 2 * j) % n))
        pieces.append((fetch(far, lambda i: i ^ 1), ((me ^ 1) + 2 * j) % n))
    return pieces


def strip_tables(frames):
    frame, depth, pos = np.meshgrid(
        np.arange(frames), np.arange(OVS), np.arange(MID), indexing="ij"
    )

    def token(edge, d, t):
        row = (d, S - 1 - d, OVS + t, OVS + t)[edge]
        col = (OVS + t, OVS + t, d, S - 1 - d)[edge]
        return (frame * (S * S) + row * S + col).reshape(-1)

    recv = np.stack([token(e, depth, pos) for e in range(4)])
    send = np.stack(
        [[token(e, OVS - 1 - depth, pos if flip == 0 else MID - 1 - pos) for flip in range(2)]
         for e in range(4)]
    )
    return recv.astype(np.int32), send.astype(np.int32)


def strip_depth(frames):
    grid = np.full((S, S), -1, np.int32)
    for d in range(OVS):
        grid[d, OVS : S - OVS] = d
        grid[S - 1 - d, OVS : S - OVS] = d
        grid[OVS : S - OVS, d] = d
        grid[OVS : S - OVS, S - 1 - d] = d
    return np.tile(grid.reshape(-1), frames)


def per_device(latents, modulation, w_qkv, w_out, edge_table, space_ramp, time_ramp):
    block_in = latents[0, 0]
    tokens = block_in.shape[0]
    frames = tokens // (S * S)
    n = lax.axis_size("face")
    rows = w_qkv.shape[0]
    moved = modulate(block_in, modulation)
    if n == 4:
        me = lax.axis_index("face")
        core = me % 2

        def fetch(x, src_of):
            return lax.ppermute(x, "face", [(src_of(i), i) for i in range(n)])

        moved_chips = moved.reshape(tokens, 2, 2 * rows).transpose(1, 0, 2)

        def chip_weight(same_core, other_core):
            stack = jnp.zeros((2,) + w_qkv.shape, w_qkv.dtype)
            stack = lax.dynamic_update_index_in_dim(stack, same_core, core, 0)
            stack = lax.dynamic_update_index_in_dim(stack, other_core, 1 - core, 0)
            return stack.reshape(2 * rows, w_qkv.shape[1])

        def chip_part(chip, weight):
            return jnp.dot(
                lax.dynamic_index_in_dim(moved_chips, chip, 0, keepdims=False),
                weight,
                preferred_element_type=jnp.float32,
            )

        sib = fetch(w_qkv, lambda i: i ^ 1)
        far = fetch(w_qkv, lambda i: (i + 2) % n)
        local = chip_part(me // 2, chip_weight(w_qkv, sib))
        local, far = lax.optimization_barrier((local, far))
        fwd = fetch(far, lambda i: i ^ 1)
        qkv_sums = local + chip_part(1 - me // 2, chip_weight(far, fwd))
        w_out_late, _ = lax.optimization_barrier((w_out, (far, fwd)))
    else:
        qkv_pieces = face_pieces(w_qkv)
        w_out_late, _ = lax.optimization_barrier((w_out, [piece for piece, _ in qkv_pieces]))
        qkv_stack = jnp.zeros((n,) + w_qkv.shape, w_qkv.dtype)
        for piece, index in qkv_pieces:
            qkv_stack = lax.dynamic_update_index_in_dim(qkv_stack, piece, index, 0)
        w_qkv_full = qkv_stack.reshape(n * rows, w_qkv.shape[1])
        qkv_sums = jnp.dot(moved, w_qkv_full, preferred_element_type=jnp.float32)
    qkv_all = qkv_sums.astype(jnp.bfloat16)

    out_stack = jnp.zeros((n,) + w_out.shape, w_out.dtype)
    for piece, index in face_pieces(w_out_late):
        out_stack = lax.dynamic_update_index_in_dim(out_stack, piece, index, 0)
    w_out_full = out_stack.transpose(1, 0, 2).reshape(w_out.shape[0], n * w_out.shape[1])

    split = qkv_all.reshape(tokens, 3, HEADS, HD)
    queries = split[:, 0].transpose(1, 0, 2)
    keys = split[:, 1].transpose(1, 2, 0)
    values = split[:, 2].transpose(1, 0, 2)
    rim = OVT * S * S
    mid_a = rim + ((tokens - 2 * rim) // (2 * S * S)) * (S * S)
    gate = modulation[2]

    def tile_part(part_queries, part_in):
        return attend_project(part_queries, keys, values, w_out_full, part_in, gate)

    my_rows = lax.dynamic_index_in_dim(edge_table, lax.axis_index("face"), 0, keepdims=False)
    flips = my_rows[:, 2]
    routes = my_rows[:, 3]
    send_match = routes[None, :] == jnp.asarray(PARTNER_ROUTE, jnp.int32)[:, None]
    recv_match = routes[None, :] == jnp.arange(4, dtype=jnp.int32)[:, None]
    ramp = space_ramp.astype(jnp.float32)
    keep = ramp / (ramp + ramp[::-1])
    take = ramp[::-1] / (ramp + ramp[::-1])

    def strips_out(tile_out):
        part_tokens = tile_out.shape[0]
        part_frames = part_tokens // (S * S)
        _, send_table = strip_tables(part_frames)
        send_by_edge = jnp.where(flips[:, None] > 0, send_table[:, 1], send_table[:, 0])
        send_cells = jnp.sum(jnp.where(send_match[:, :, None], send_by_edge[None], 0), axis=1)
        send_cells = send_cells.reshape(-1)
        token_ids = jnp.arange(part_tokens, dtype=jnp.int32)
        pick = (send_cells[:, None] == token_ids[None, :]).astype(jnp.bfloat16)
        return jnp.dot(pick, tile_out, preferred_element_type=jnp.float32).astype(jnp.bfloat16)

    def strips_in(outgoing):
        strip_len = outgoing.shape[0] // 4
        arrived = []
        for route_id in range(4):
            sent = outgoing[route_id * strip_len : (route_id + 1) * strip_len]
            shift = -OFFSETS[route_id]
            arrived.append(
                lax.ppermute(sent, "face", [(i, (i + shift) % n) for i in range(n)])
            )
        return jnp.concatenate(arrived, axis=0)

    def space_blend(tile_out, arrived):
        part_tokens = tile_out.shape[0]
        part_frames = part_tokens // (S * S)
        recv_table, _ = strip_tables(part_frames)
        recv_cells = jnp.sum(jnp.where(recv_match[:, :, None], recv_table[None], 0), axis=1)
        recv_cells = recv_cells.reshape(-1)
        token_ids = jnp.arange(part_tokens, dtype=jnp.int32)
        place = (token_ids[:, None] == recv_cells[None, :]).astype(jnp.bfloat16)
        partner = jnp.dot(place, arrived, preferred_element_type=jnp.float32)
        dep = strip_depth(part_frames)[:, None]
        w_keep = jnp.where(dep == 0, keep[0], keep[1])
        w_take = jnp.where(dep == 0, take[0], take[1])
        own = tile_out.astype(jnp.float32)
        return jnp.where(dep >= 0, w_keep * own + w_take * partner, own).astype(jnp.bfloat16)

    rim_queries = jnp.concatenate([queries[:, :rim], queries[:, tokens - rim :]], axis=1)
    rim_in = jnp.concatenate([block_in[:rim], block_in[tokens - rim :]], axis=0)
    tile_rim = tile_part(rim_queries, rim_in)
    outgoing_rim = strips_out(tile_rim)
    arrived_rim = strips_in(outgoing_rim)
    first_queries, outgoing_rim = lax.optimization_barrier((queries[:, rim:mid_a], outgoing_rim))
    tile_first = tile_part(first_queries, block_in[rim:mid_a])
    arrived_rim, tile_first = lax.optimization_barrier((arrived_rim, tile_first))
    spaced_rim = space_blend(tile_rim, arrived_rim)
    low, high = lax.optimization_barrier((spaced_rim[:rim], spaced_rim[rim:]))
    count = lax.axis_size("tm")
    lower = lax.ppermute(high, "tm", [(i, i + 1) for i in range(count - 1)])
    upper = lax.ppermute(low, "tm", [(i + 1, i) for i in range(count - 1)])
    outgoing_first = strips_out(tile_first)
    arrived_first = strips_in(outgoing_first)
    second_queries, low, high, outgoing_first = lax.optimization_barrier(
        (queries[:, mid_a : tokens - rim], low, high, outgoing_first)
    )
    tile_second = tile_part(second_queries, block_in[mid_a : tokens - rim])
    lower, upper, arrived_first, tile_second = lax.optimization_barrier(
        (lower, upper, arrived_first, tile_second)
    )
    spaced_mid = jnp.concatenate(
        [
            space_blend(tile_first, arrived_first),
            space_blend(tile_second, strips_in(strips_out(tile_second))),
        ],
        axis=0,
    )

    span_id = lax.axis_index("tm")
    has_lower = span_id > 0
    has_upper = span_id < count - 1
    tramp = time_ramp.astype(jnp.float32)
    hold = tramp / (tramp + tramp[::-1])
    pass_ = tramp[::-1] / (tramp + tramp[::-1])
    blocks = (OVT, S * S, D)
    low_f = low.astype(jnp.float32).reshape(blocks)
    high_f = high.astype(jnp.float32).reshape(blocks)
    hold_low = hold[:, None, None]
    pass_low = pass_[:, None, None]
    hold_high = hold[::-1][:, None, None]
    pass_high = pass_[::-1][:, None, None]
    low_mix = jnp.where(
        has_lower, hold_low * low_f + pass_low * lower.astype(jnp.float32).reshape(blocks), low_f
    ).reshape(rim, D)
    high_mix = jnp.where(
        has_upper, hold_high * high_f + pass_high * upper.astype(jnp.float32).reshape(blocks), high_f
    ).reshape(rim, D)
    result = jnp.concatenate(
        [low_mix.astype(jnp.bfloat16), spaced_mid, high_mix.astype(jnp.bfloat16)], axis=0
    )
    return result.reshape(1, 1, tokens, D)


def solution(mesh):
    return jax.shard_map(
        per_device,
        mesh=mesh,
        in_specs=(
            P(("groups", "tm"), "face", None, None),
            P("groups", None),
            P("face", None),
            P(None, "face"),
            P(),
            P(),
            P(),
        ),
        out_specs=P(("groups", "tm"), "face", None, None),
        check_vma=False,
    )
```

```python
import math

import jax
import jax.numpy as jnp
import numpy as np
from jax import lax
from jax.experimental import pallas as pl
from jax.experimental.pallas import tpu as pltpu
from jax.sharding import PartitionSpec as P

D = 1152
HD = 72
HEADS = 8
S = 8
OVS = 2
OVT = 4
MID = S - 2 * OVS


NORM_EPS = 1e-06
OFFSETS = (1, -1, 2, -2)
PARTNER_ROUTE = (1, 0, 3, 2)


def modulate(block_in, modulation):
    values = block_in.astype(jnp.float32)
    center = jnp.mean(values, axis=-1, keepdims=True)
    spread = jnp.mean(jnp.square(values - center), axis=-1, keepdims=True)
    normed = (values - center) * lax.rsqrt(spread + NORM_EPS)
    return (normed * (1.0 + modulation[1]) + modulation[0]).astype(jnp.bfloat16)


HEADS_PER_STEP = 2


def attention_kernel(*refs):
    x_ref, g_ref, o_ref, acc_ref = refs[-4:]
    per_head = refs[:-4]
    step = pl.program_id(1)

    @pl.when(step == 0)
    def _():
        acc_ref[...] = jnp.zeros_like(acc_ref)

    total = None
    for j in range(HEADS_PER_STEP):
        q_ref, k_ref, v_ref, w_ref = per_head[4 * j : 4 * j + 4]
        scores = jnp.dot(q_ref[0], k_ref[0], preferred_element_type=jnp.float32) * (
            1.0 / math.sqrt(HD)
        )
        row_max = jnp.max(scores, axis=-1, keepdims=True)
        weights = jnp.exp(scores - row_max)
        row_sum = jnp.sum(weights, axis=-1, keepdims=True)
        probabilities = (weights * (1.0 / row_sum)).astype(jnp.bfloat16)
        mixed = jnp.dot(probabilities, v_ref[0], preferred_element_type=jnp.float32).astype(
            jnp.bfloat16
        )
        part = jnp.dot(mixed, w_ref[...], preferred_element_type=jnp.float32)
        total = part if total is None else total + part
    acc_ref[...] += total

    @pl.when(step == pl.num_programs(1) - 1)
    def _():
        o_ref[...] = (x_ref[...].astype(jnp.float32) + g_ref[...] * acc_ref[...]).astype(
            o_ref.dtype
        )


def attend_project(queries, keys, values, w_out_full, block_in, gate):
    heads, size, tokens = keys.shape
    chunk = queries.shape[1]
    width = block_in.shape[1]
    hb = HEADS_PER_STEP
    in_specs = []
    operands = []
    for j in range(hb):
        in_specs += [
            pl.BlockSpec((1, chunk, size), lambda i, h, j=j: (hb * h + j, i, 0)),
            pl.BlockSpec((1, size, tokens), lambda i, h, j=j: (hb * h + j, 0, 0)),
            pl.BlockSpec((1, tokens, size), lambda i, h, j=j: (hb * h + j, 0, 0)),
            pl.BlockSpec((size, width), lambda i, h, j=j: (hb * h + j, 0)),
        ]
        operands += [queries, keys, values, w_out_full]
    in_specs += [
        pl.BlockSpec((chunk, width), lambda i, h: (i, 0)),
        pl.BlockSpec((1, width), lambda i, h: (0, 0)),
    ]
    return pl.pallas_call(
        attention_kernel,
        grid=(1, heads // hb),
        in_specs=in_specs,
        out_specs=pl.BlockSpec((chunk, width), lambda i, h: (i, 0)),
        out_shape=jax.ShapeDtypeStruct(block_in.shape, block_in.dtype),
        scratch_shapes=[pltpu.VMEM((chunk, width), jnp.float32)],
        compiler_params=pltpu.CompilerParams(dimension_semantics=("arbitrary", "arbitrary")),
    )(*operands, block_in, gate.reshape(1, width))


def face_pieces(shard):
    n = lax.axis_size("face")
    me = lax.axis_index("face")

    def fetch(x, src_of):
        return lax.ppermute(x, "face", [(src_of(i), i) for i in range(n)])

    pieces = [(shard, me), (fetch(shard, lambda i: i ^ 1), me ^ 1)]
    for j in range(1, n // 2):
        far = fetch(shard, lambda i: (i + 2 * j) % n)
        pieces.append((far, (me + 2 * j) % n))
        pieces.append((fetch(far, lambda i: i ^ 1), ((me ^ 1) + 2 * j) % n))
    return pieces


def strip_tables(frames):
    frame, depth, pos = np.meshgrid(
        np.arange(frames), np.arange(OVS), np.arange(MID), indexing="ij"
    )

    def token(edge, d, t):
        row = (d, S - 1 - d, OVS + t, OVS + t)[edge]
        col = (OVS + t, OVS + t, d, S - 1 - d)[edge]
        return (frame * (S * S) + row * S + col).reshape(-1)

    recv = np.stack([token(e, depth, pos) for e in range(4)])
    send = np.stack(
        [[token(e, OVS - 1 - depth, pos if flip == 0 else MID - 1 - pos) for flip in range(2)]
         for e in range(4)]
    )
    return recv.astype(np.int32), send.astype(np.int32)


def strip_depth(frames):
    grid = np.full((S, S), -1, np.int32)
    for d in range(OVS):
        grid[d, OVS : S - OVS] = d
        grid[S - 1 - d, OVS : S - OVS] = d
        grid[OVS : S - OVS, d] = d
        grid[OVS : S - OVS, S - 1 - d] = d
    return np.tile(grid.reshape(-1), frames)


def per_device(latents, modulation, w_qkv, w_out, edge_table, space_ramp, time_ramp):
    block_in = latents[0, 0]
    tokens = block_in.shape[0]
    frames = tokens // (S * S)
    n = lax.axis_size("face")
    rows = w_qkv.shape[0]
    moved = modulate(block_in, modulation)
    if n == 4:
        me = lax.axis_index("face")
        core = me % 2

        def fetch(x, src_of):
            return lax.ppermute(x, "face", [(src_of(i), i) for i in range(n)])

        moved_chips = moved.reshape(tokens, 2, 2 * rows).transpose(1, 0, 2)

        def chip_weight(same_core, other_core):
            stack = jnp.zeros((2,) + w_qkv.shape, w_qkv.dtype)
            stack = lax.dynamic_update_index_in_dim(stack, same_core, core, 0)
            stack = lax.dynamic_update_index_in_dim(stack, other_core, 1 - core, 0)
            return stack.reshape(2 * rows, w_qkv.shape[1])

        def chip_part(chip, weight):
            return jnp.dot(
                lax.dynamic_index_in_dim(moved_chips, chip, 0, keepdims=False),
                weight,
                preferred_element_type=jnp.float32,
            )

        sib = fetch(w_qkv, lambda i: i ^ 1)
        far = fetch(w_qkv, lambda i: (i + 2) % n)
        local = chip_part(me // 2, chip_weight(w_qkv, sib))
        local, far = lax.optimization_barrier((local, far))
        fwd = fetch(far, lambda i: i ^ 1)
        qkv_sums = local + chip_part(1 - me // 2, chip_weight(far, fwd))
        w_out_late, _ = lax.optimization_barrier((w_out, (far, fwd)))
    else:
        qkv_pieces = face_pieces(w_qkv)
        w_out_late, _ = lax.optimization_barrier((w_out, [piece for piece, _ in qkv_pieces]))
        qkv_stack = jnp.zeros((n,) + w_qkv.shape, w_qkv.dtype)
        for piece, index in qkv_pieces:
            qkv_stack = lax.dynamic_update_index_in_dim(qkv_stack, piece, index, 0)
        w_qkv_full = qkv_stack.reshape(n * rows, w_qkv.shape[1])
        qkv_sums = jnp.dot(moved, w_qkv_full, preferred_element_type=jnp.float32)
    qkv_all = qkv_sums.astype(jnp.bfloat16)

    out_stack = jnp.zeros((n,) + w_out.shape, w_out.dtype)
    for piece, index in face_pieces(w_out_late):
        out_stack = lax.dynamic_update_index_in_dim(out_stack, piece, index, 0)
    w_out_full = out_stack.transpose(1, 0, 2).reshape(w_out.shape[0], n * w_out.shape[1])

    split = qkv_all.reshape(tokens, 3, HEADS, HD)
    queries = split[:, 0].transpose(1, 0, 2)
    keys = split[:, 1].transpose(1, 2, 0)
    values = split[:, 2].transpose(1, 0, 2)
    rim = OVT * S * S
    mid_a = rim + ((tokens - 2 * rim) // (2 * S * S)) * (S * S)
    gate = modulation[2]

    def tile_part(part_queries, part_in):
        return attend_project(part_queries, keys, values, w_out_full, part_in, gate)

    my_rows = lax.dynamic_index_in_dim(edge_table, lax.axis_index("face"), 0, keepdims=False)
    flips = my_rows[:, 2]
    routes = my_rows[:, 3]
    send_match = routes[None, :] == jnp.asarray(PARTNER_ROUTE, jnp.int32)[:, None]
    recv_match = routes[None, :] == jnp.arange(4, dtype=jnp.int32)[:, None]
    ramp = space_ramp.astype(jnp.float32)
    keep = ramp / (ramp + ramp[::-1])
    take = ramp[::-1] / (ramp + ramp[::-1])

    def strips_out(tile_out):
        part_tokens = tile_out.shape[0]
        part_frames = part_tokens // (S * S)
        _, send_table = strip_tables(part_frames)
        send_by_edge = jnp.where(flips[:, None] > 0, send_table[:, 1], send_table[:, 0])
        send_cells = jnp.sum(jnp.where(send_match[:, :, None], send_by_edge[None], 0), axis=1)
        send_cells = send_cells.reshape(-1)
        token_ids = jnp.arange(part_tokens, dtype=jnp.int32)
        pick = (send_cells[:, None] == token_ids[None, :]).astype(jnp.bfloat16)
        return jnp.dot(pick, tile_out, preferred_element_type=jnp.float32).astype(jnp.bfloat16)

    def strips_in(outgoing):
        strip_len = outgoing.shape[0] // 4
        arrived = []
        for route_id in range(4):
            sent = outgoing[route_id * strip_len : (route_id + 1) * strip_len]
            shift = -OFFSETS[route_id]
            arrived.append(
                lax.ppermute(sent, "face", [(i, (i + shift) % n) for i in range(n)])
            )
        return jnp.concatenate(arrived, axis=0)

    def space_blend(tile_out, arrived):
        part_tokens = tile_out.shape[0]
        part_frames = part_tokens // (S * S)
        recv_table, _ = strip_tables(part_frames)
        recv_cells = jnp.sum(jnp.where(recv_match[:, :, None], recv_table[None], 0), axis=1)
        recv_cells = recv_cells.reshape(-1)
        token_ids = jnp.arange(part_tokens, dtype=jnp.int32)
        place = (token_ids[:, None] == recv_cells[None, :]).astype(jnp.bfloat16)
        partner = jnp.dot(place, arrived, preferred_element_type=jnp.float32)
        dep = strip_depth(1)[:, None]
        w_keep = jnp.where(dep == 0, keep[0], keep[1])
        w_take = jnp.where(dep == 0, take[0], take[1])
        grid_shape = (part_frames, S * S, tile_out.shape[1])
        own = tile_out.astype(jnp.float32).reshape(grid_shape)
        partner = partner.reshape(grid_shape)
        mixed = jnp.where(dep >= 0, w_keep * own + w_take * partner, own)
        return mixed.reshape(tile_out.shape).astype(jnp.bfloat16)

    rim_queries = jnp.concatenate([queries[:, :rim], queries[:, tokens - rim :]], axis=1)
    rim_in = jnp.concatenate([block_in[:rim], block_in[tokens - rim :]], axis=0)
    tile_rim = tile_part(rim_queries, rim_in)
    outgoing_rim = strips_out(tile_rim)
    arrived_rim = strips_in(outgoing_rim)
    first_queries, outgoing_rim = lax.optimization_barrier((queries[:, rim:mid_a], outgoing_rim))
    tile_first = tile_part(first_queries, block_in[rim:mid_a])
    arrived_rim, tile_first = lax.optimization_barrier((arrived_rim, tile_first))
    spaced_rim = space_blend(tile_rim, arrived_rim)
    low, high = lax.optimization_barrier((spaced_rim[:rim], spaced_rim[rim:]))
    count = lax.axis_size("tm")
    lower = lax.ppermute(high, "tm", [(i, i + 1) for i in range(count - 1)])
    upper = lax.ppermute(low, "tm", [(i + 1, i) for i in range(count - 1)])
    outgoing_first = strips_out(tile_first)
    arrived_first = strips_in(outgoing_first)
    second_queries, low, high, outgoing_first = lax.optimization_barrier(
        (queries[:, mid_a : tokens - rim], low, high, outgoing_first)
    )
    tile_second = tile_part(second_queries, block_in[mid_a : tokens - rim])
    lower, upper, arrived_first, tile_second = lax.optimization_barrier(
        (lower, upper, arrived_first, tile_second)
    )
    spaced_mid = jnp.concatenate(
        [
            space_blend(tile_first, arrived_first),
            space_blend(tile_second, strips_in(strips_out(tile_second))),
        ],
        axis=0,
    )

    span_id = lax.axis_index("tm")
    has_lower = span_id > 0
    has_upper = span_id < count - 1
    tramp = time_ramp.astype(jnp.float32)
    hold = tramp / (tramp + tramp[::-1])
    pass_ = tramp[::-1] / (tramp + tramp[::-1])
    blocks = (OVT, S * S, D)
    low_f = low.astype(jnp.float32).reshape(blocks)
    high_f = high.astype(jnp.float32).reshape(blocks)
    hold_low = hold[:, None, None]
    pass_low = pass_[:, None, None]
    hold_high = hold[::-1][:, None, None]
    pass_high = pass_[::-1][:, None, None]
    low_mix = jnp.where(
        has_lower, hold_low * low_f + pass_low * lower.astype(jnp.float32).reshape(blocks), low_f
    ).reshape(rim, D)
    high_mix = jnp.where(
        has_upper, hold_high * high_f + pass_high * upper.astype(jnp.float32).reshape(blocks), high_f
    ).reshape(rim, D)
    result = jnp.concatenate(
        [low_mix.astype(jnp.bfloat16), spaced_mid, high_mix.astype(jnp.bfloat16)], axis=0
    )
    return result.reshape(1, 1, tokens, D)


def solution(mesh):
    return jax.shard_map(
        per_device,
        mesh=mesh,
        in_specs=(
            P(("groups", "tm"), "face", None, None),
            P("groups", None),
            P("face", None),
            P(None, "face"),
            P(),
            P(),
            P(),
        ),
        out_specs=P(("groups", "tm"), "face", None, None),
        check_vma=False,
    )
```

```python
import math

import jax
import jax.numpy as jnp
import numpy as np
from jax import lax
from jax.experimental import pallas as pl
from jax.experimental.pallas import tpu as pltpu
from jax.sharding import PartitionSpec as P

D = 1152
HD = 72
HEADS = 8
S = 8
OVS = 2
OVT = 4
MID = S - 2 * OVS


NORM_EPS = 1e-06
OFFSETS = (1, -1, 2, -2)
PARTNER_ROUTE = (1, 0, 3, 2)


def modulate(block_in, modulation):
    values = block_in.astype(jnp.float32)
    center = jnp.mean(values, axis=-1, keepdims=True)
    spread = jnp.mean(jnp.square(values - center), axis=-1, keepdims=True)
    normed = (values - center) * lax.rsqrt(spread + NORM_EPS)
    return (normed * (1.0 + modulation[1]) + modulation[0]).astype(jnp.bfloat16)


HEADS_PER_STEP = 2


def attention_kernel(*refs):
    x_ref, g_ref, o_ref, acc_ref = refs[-4:]
    per_head = refs[:-4]
    step = pl.program_id(1)

    @pl.when(step == 0)
    def _():
        acc_ref[...] = jnp.zeros_like(acc_ref)

    total = None
    for j in range(HEADS_PER_STEP):
        q_ref, k_ref, v_ref, w_ref = per_head[4 * j : 4 * j + 4]
        scores = jnp.dot(q_ref[0], k_ref[0], preferred_element_type=jnp.float32) * (
            1.0 / math.sqrt(HD)
        )
        row_max = jnp.max(scores, axis=-1, keepdims=True)
        weights = jnp.exp(scores - row_max)
        row_sum = jnp.sum(weights, axis=-1, keepdims=True)
        probabilities = (weights * (1.0 / row_sum)).astype(jnp.bfloat16)
        mixed = jnp.dot(probabilities, v_ref[0], preferred_element_type=jnp.float32).astype(
            jnp.bfloat16
        )
        part = jnp.dot(mixed, w_ref[...], preferred_element_type=jnp.float32)
        total = part if total is None else total + part
    acc_ref[...] += total

    @pl.when(step == pl.num_programs(1) - 1)
    def _():
        o_ref[...] = (x_ref[...].astype(jnp.float32) + g_ref[...] * acc_ref[...]).astype(
            o_ref.dtype
        )


def attend_project(queries, keys, values, w_out_full, block_in, gate):
    heads, size, tokens = keys.shape
    chunk = queries.shape[1]
    width = block_in.shape[1]
    hb = HEADS_PER_STEP
    in_specs = []
    operands = []
    for j in range(hb):
        in_specs += [
            pl.BlockSpec((1, chunk, size), lambda i, h, j=j: (hb * h + j, i, 0)),
            pl.BlockSpec((1, size, tokens), lambda i, h, j=j: (hb * h + j, 0, 0)),
            pl.BlockSpec((1, tokens, size), lambda i, h, j=j: (hb * h + j, 0, 0)),
            pl.BlockSpec((size, width), lambda i, h, j=j: (hb * h + j, 0)),
        ]
        operands += [queries, keys, values, w_out_full]
    in_specs += [
        pl.BlockSpec((chunk, width), lambda i, h: (i, 0)),
        pl.BlockSpec((1, width), lambda i, h: (0, 0)),
    ]
    return pl.pallas_call(
        attention_kernel,
        grid=(1, heads // hb),
        in_specs=in_specs,
        out_specs=pl.BlockSpec((chunk, width), lambda i, h: (i, 0)),
        out_shape=jax.ShapeDtypeStruct(block_in.shape, block_in.dtype),
        scratch_shapes=[pltpu.VMEM((chunk, width), jnp.float32)],
        compiler_params=pltpu.CompilerParams(dimension_semantics=("arbitrary", "arbitrary")),
    )(*operands, block_in, gate.reshape(1, width))


def face_pieces(shard):
    n = lax.axis_size("face")
    me = lax.axis_index("face")

    def fetch(x, src_of):
        return lax.ppermute(x, "face", [(src_of(i), i) for i in range(n)])

    pieces = [(shard, me), (fetch(shard, lambda i: i ^ 1), me ^ 1)]
    for j in range(1, n // 2):
        far = fetch(shard, lambda i: (i + 2 * j) % n)
        pieces.append((far, (me + 2 * j) % n))
        pieces.append((fetch(far, lambda i: i ^ 1), ((me ^ 1) + 2 * j) % n))
    return pieces


def strip_tables(frames):
    frame, depth, pos = np.meshgrid(
        np.arange(frames), np.arange(OVS), np.arange(MID), indexing="ij"
    )

    def token(edge, d, t):
        row = (d, S - 1 - d, OVS + t, OVS + t)[edge]
        col = (OVS + t, OVS + t, d, S - 1 - d)[edge]
        return (frame * (S * S) + row * S + col).reshape(-1)

    recv = np.stack([token(e, depth, pos) for e in range(4)])
    send = np.stack(
        [[token(e, OVS - 1 - depth, pos if flip == 0 else MID - 1 - pos) for flip in range(2)]
         for e in range(4)]
    )
    return recv.astype(np.int32), send.astype(np.int32)


def strip_depth(frames):
    grid = np.full((S, S), -1, np.int32)
    for d in range(OVS):
        grid[d, OVS : S - OVS] = d
        grid[S - 1 - d, OVS : S - OVS] = d
        grid[OVS : S - OVS, d] = d
        grid[OVS : S - OVS, S - 1 - d] = d
    return np.tile(grid.reshape(-1), frames)


def per_device(latents, modulation, w_qkv, w_out, edge_table, space_ramp, time_ramp):
    block_in = latents[0, 0]
    tokens = block_in.shape[0]
    frames = tokens // (S * S)
    n = lax.axis_size("face")
    rows = w_qkv.shape[0]
    moved = modulate(block_in, modulation)
    if n == 4:
        me = lax.axis_index("face")
        core = me % 2

        def fetch(x, src_of):
            return lax.ppermute(x, "face", [(src_of(i), i) for i in range(n)])

        def chip_weight(same_core, other_core):
            tripled = jnp.concatenate([same_core, other_core, same_core], axis=0)
            return lax.dynamic_slice_in_dim(tripled, core * rows, 2 * rows, axis=0)

        def chip_part(chip, weight):
            return jnp.dot(
                lax.dynamic_slice_in_dim(moved, chip * 2 * rows, 2 * rows, axis=1),
                weight,
                preferred_element_type=jnp.float32,
            )

        sib = fetch(w_qkv, lambda i: i ^ 1)
        far = fetch(w_qkv, lambda i: (i + 2) % n)
        local = chip_part(me // 2, chip_weight(w_qkv, sib))
        local, far = lax.optimization_barrier((local, far))
        fwd = fetch(far, lambda i: i ^ 1)
        qkv_sums = local + chip_part(1 - me // 2, chip_weight(far, fwd))
        w_out_late, _ = lax.optimization_barrier((w_out, (far, fwd)))
    else:
        qkv_pieces = face_pieces(w_qkv)
        w_out_late, _ = lax.optimization_barrier((w_out, [piece for piece, _ in qkv_pieces]))
        qkv_stack = jnp.zeros((n,) + w_qkv.shape, w_qkv.dtype)
        for piece, index in qkv_pieces:
            qkv_stack = lax.dynamic_update_index_in_dim(qkv_stack, piece, index, 0)
        w_qkv_full = qkv_stack.reshape(n * rows, w_qkv.shape[1])
        qkv_sums = jnp.dot(moved, w_qkv_full, preferred_element_type=jnp.float32)
    qkv_all = qkv_sums.astype(jnp.bfloat16)

    out_stack = jnp.zeros((n,) + w_out.shape, w_out.dtype)
    for piece, index in face_pieces(w_out_late):
        out_stack = lax.dynamic_update_index_in_dim(out_stack, piece, index, 0)
    w_out_full = out_stack.transpose(1, 0, 2).reshape(w_out.shape[0], n * w_out.shape[1])

    split = qkv_all.reshape(tokens, 3, HEADS, HD)
    queries = split[:, 0].transpose(1, 0, 2)
    keys = split[:, 1].transpose(1, 2, 0)
    values = split[:, 2].transpose(1, 0, 2)
    rim = OVT * S * S
    mid_a = rim + ((tokens - 2 * rim) // (2 * S * S)) * (S * S)
    gate = modulation[2]

    def tile_part(part_queries, part_in):
        return attend_project(part_queries, keys, values, w_out_full, part_in, gate)

    my_rows = lax.dynamic_index_in_dim(edge_table, lax.axis_index("face"), 0, keepdims=False)
    flips = my_rows[:, 2]
    routes = my_rows[:, 3]
    send_match = routes[None, :] == jnp.asarray(PARTNER_ROUTE, jnp.int32)[:, None]
    recv_match = routes[None, :] == jnp.arange(4, dtype=jnp.int32)[:, None]
    ramp = space_ramp.astype(jnp.float32)
    keep = ramp / (ramp + ramp[::-1])
    take = ramp[::-1] / (ramp + ramp[::-1])

    def strips_out(tile_out):
        part_tokens = tile_out.shape[0]
        part_frames = part_tokens // (S * S)
        _, send_table = strip_tables(part_frames)
        send_by_edge = jnp.where(flips[:, None] > 0, send_table[:, 1], send_table[:, 0])
        send_cells = jnp.sum(jnp.where(send_match[:, :, None], send_by_edge[None], 0), axis=1)
        send_cells = send_cells.reshape(-1)
        token_ids = jnp.arange(part_tokens, dtype=jnp.int32)
        pick = (send_cells[:, None] == token_ids[None, :]).astype(jnp.bfloat16)
        return jnp.dot(pick, tile_out, preferred_element_type=jnp.float32).astype(jnp.bfloat16)

    def strips_in(outgoing):
        strip_len = outgoing.shape[0] // 4
        arrived = []
        for route_id in range(4):
            sent = outgoing[route_id * strip_len : (route_id + 1) * strip_len]
            shift = -OFFSETS[route_id]
            arrived.append(
                lax.ppermute(sent, "face", [(i, (i + shift) % n) for i in range(n)])
            )
        return jnp.concatenate(arrived, axis=0)

    def space_blend(tile_out, arrived):
        part_tokens = tile_out.shape[0]
        part_frames = part_tokens // (S * S)
        recv_table, _ = strip_tables(part_frames)
        recv_cells = jnp.sum(jnp.where(recv_match[:, :, None], recv_table[None], 0), axis=1)
        recv_cells = recv_cells.reshape(-1)
        token_ids = jnp.arange(part_tokens, dtype=jnp.int32)
        place = (token_ids[:, None] == recv_cells[None, :]).astype(jnp.bfloat16)
        partner = jnp.dot(place, arrived, preferred_element_type=jnp.float32)
        dep = strip_depth(1)[:, None]
        w_keep = jnp.where(dep == 0, keep[0], keep[1])
        w_take = jnp.where(dep == 0, take[0], take[1])
        grid_shape = (part_frames, S * S, tile_out.shape[1])
        own = tile_out.astype(jnp.float32).reshape(grid_shape)
        partner = partner.reshape(grid_shape)
        mixed = jnp.where(dep >= 0, w_keep * own + w_take * partner, own)
        return mixed.reshape(tile_out.shape).astype(jnp.bfloat16)

    rim_queries = jnp.concatenate([queries[:, :rim], queries[:, tokens - rim :]], axis=1)
    rim_in = jnp.concatenate([block_in[:rim], block_in[tokens - rim :]], axis=0)
    tile_rim = tile_part(rim_queries, rim_in)
    outgoing_rim = strips_out(tile_rim)
    arrived_rim = strips_in(outgoing_rim)
    first_queries, outgoing_rim = lax.optimization_barrier((queries[:, rim:mid_a], outgoing_rim))
    tile_first = tile_part(first_queries, block_in[rim:mid_a])
    arrived_rim, tile_first = lax.optimization_barrier((arrived_rim, tile_first))
    spaced_rim = space_blend(tile_rim, arrived_rim)
    low, high = lax.optimization_barrier((spaced_rim[:rim], spaced_rim[rim:]))
    count = lax.axis_size("tm")
    lower = lax.ppermute(high, "tm", [(i, i + 1) for i in range(count - 1)])
    upper = lax.ppermute(low, "tm", [(i + 1, i) for i in range(count - 1)])
    outgoing_first = strips_out(tile_first)
    arrived_first = strips_in(outgoing_first)
    second_queries, low, high, outgoing_first = lax.optimization_barrier(
        (queries[:, mid_a : tokens - rim], low, high, outgoing_first)
    )
    tile_second = tile_part(second_queries, block_in[mid_a : tokens - rim])
    lower, upper, arrived_first, tile_second = lax.optimization_barrier(
        (lower, upper, arrived_first, tile_second)
    )
    spaced_mid = jnp.concatenate(
        [
            space_blend(tile_first, arrived_first),
            space_blend(tile_second, strips_in(strips_out(tile_second))),
        ],
        axis=0,
    )

    span_id = lax.axis_index("tm")
    has_lower = span_id > 0
    has_upper = span_id < count - 1
    tramp = time_ramp.astype(jnp.float32)
    hold = tramp / (tramp + tramp[::-1])
    pass_ = tramp[::-1] / (tramp + tramp[::-1])
    blocks = (OVT, S * S, D)
    low_f = low.astype(jnp.float32).reshape(blocks)
    high_f = high.astype(jnp.float32).reshape(blocks)
    hold_low = hold[:, None, None]
    pass_low = pass_[:, None, None]
    hold_high = hold[::-1][:, None, None]
    pass_high = pass_[::-1][:, None, None]
    low_mix = jnp.where(
        has_lower, hold_low * low_f + pass_low * lower.astype(jnp.float32).reshape(blocks), low_f
    ).reshape(rim, D)
    high_mix = jnp.where(
        has_upper, hold_high * high_f + pass_high * upper.astype(jnp.float32).reshape(blocks), high_f
    ).reshape(rim, D)
    result = jnp.concatenate(
        [low_mix.astype(jnp.bfloat16), spaced_mid, high_mix.astype(jnp.bfloat16)], axis=0
    )
    return result.reshape(1, 1, tokens, D)


def solution(mesh):
    return jax.shard_map(
        per_device,
        mesh=mesh,
        in_specs=(
            P(("groups", "tm"), "face", None, None),
            P("groups", None),
            P("face", None),
            P(None, "face"),
            P(),
            P(),
            P(),
        ),
        out_specs=P(("groups", "tm"), "face", None, None),
        check_vma=False,
    )
```

```python
import math

import jax
import jax.numpy as jnp
import numpy as np
from jax import lax
from jax.experimental import pallas as pl
from jax.experimental.pallas import tpu as pltpu
from jax.sharding import PartitionSpec as P

D = 1152
HD = 72
HEADS = 8
S = 8
OVS = 2
OVT = 4
MID = S - 2 * OVS


NORM_EPS = 1e-06
OFFSETS = (1, -1, 2, -2)
PARTNER_ROUTE = (1, 0, 3, 2)


def modulate(block_in, modulation):
    values = block_in.astype(jnp.float32)
    center = jnp.mean(values, axis=-1, keepdims=True)
    spread = jnp.mean(jnp.square(values - center), axis=-1, keepdims=True)
    normed = (values - center) * lax.rsqrt(spread + NORM_EPS)
    return (normed * (1.0 + modulation[1]) + modulation[0]).astype(jnp.bfloat16)


HEADS_PER_STEP = 2


def attention_kernel(*refs):
    x_ref, g_ref, o_ref, acc_ref = refs[-4:]
    per_head = refs[:-4]
    step = pl.program_id(1)

    @pl.when(step == 0)
    def _():
        acc_ref[...] = jnp.zeros_like(acc_ref)

    total = None
    for j in range(HEADS_PER_STEP):
        q_ref, k_ref, v_ref, w_ref = per_head[4 * j : 4 * j + 4]
        scores = jnp.dot(q_ref[0], k_ref[0], preferred_element_type=jnp.float32) * (
            1.0 / math.sqrt(HD)
        )
        row_max = jnp.max(scores, axis=-1, keepdims=True)
        weights = jnp.exp(scores - row_max)
        row_sum = jnp.sum(weights, axis=-1, keepdims=True)
        probabilities = (weights * (1.0 / row_sum)).astype(jnp.bfloat16)
        mixed = jnp.dot(probabilities, v_ref[0], preferred_element_type=jnp.float32).astype(
            jnp.bfloat16
        )
        part = jnp.dot(mixed, w_ref[...], preferred_element_type=jnp.float32)
        total = part if total is None else total + part
    acc_ref[...] += total

    @pl.when(step == pl.num_programs(1) - 1)
    def _():
        o_ref[...] = (x_ref[...].astype(jnp.float32) + g_ref[...] * acc_ref[...]).astype(
            o_ref.dtype
        )


def attend_project(queries, keys, values, w_out_full, block_in, gate):
    heads, size, tokens = keys.shape
    chunk = queries.shape[1]
    width = block_in.shape[1]
    hb = HEADS_PER_STEP
    in_specs = []
    operands = []
    for j in range(hb):
        in_specs += [
            pl.BlockSpec((1, chunk, size), lambda i, h, j=j: (hb * h + j, i, 0)),
            pl.BlockSpec((1, size, tokens), lambda i, h, j=j: (hb * h + j, 0, 0)),
            pl.BlockSpec((1, tokens, size), lambda i, h, j=j: (hb * h + j, 0, 0)),
            pl.BlockSpec((size, width), lambda i, h, j=j: (hb * h + j, 0)),
        ]
        operands += [queries, keys, values, w_out_full]
    in_specs += [
        pl.BlockSpec((chunk, width), lambda i, h: (i, 0)),
        pl.BlockSpec((1, width), lambda i, h: (0, 0)),
    ]
    return pl.pallas_call(
        attention_kernel,
        grid=(1, heads // hb),
        in_specs=in_specs,
        out_specs=pl.BlockSpec((chunk, width), lambda i, h: (i, 0)),
        out_shape=jax.ShapeDtypeStruct(block_in.shape, block_in.dtype),
        scratch_shapes=[pltpu.VMEM((chunk, width), jnp.float32)],
        compiler_params=pltpu.CompilerParams(dimension_semantics=("arbitrary", "arbitrary")),
    )(*operands, block_in, gate.reshape(1, width))


def face_pieces(shard):
    n = lax.axis_size("face")
    me = lax.axis_index("face")

    def fetch(x, src_of):
        return lax.ppermute(x, "face", [(src_of(i), i) for i in range(n)])

    pieces = [(shard, me), (fetch(shard, lambda i: i ^ 1), me ^ 1)]
    for j in range(1, n // 2):
        far = fetch(shard, lambda i: (i + 2 * j) % n)
        pieces.append((far, (me + 2 * j) % n))
        pieces.append((fetch(far, lambda i: i ^ 1), ((me ^ 1) + 2 * j) % n))
    return pieces


def strip_tables(frames):
    frame, depth, pos = np.meshgrid(
        np.arange(frames), np.arange(OVS), np.arange(MID), indexing="ij"
    )

    def token(edge, d, t):
        row = (d, S - 1 - d, OVS + t, OVS + t)[edge]
        col = (OVS + t, OVS + t, d, S - 1 - d)[edge]
        return (frame * (S * S) + row * S + col).reshape(-1)

    recv = np.stack([token(e, depth, pos) for e in range(4)])
    send = np.stack(
        [[token(e, OVS - 1 - depth, pos if flip == 0 else MID - 1 - pos) for flip in range(2)]
         for e in range(4)]
    )
    return recv.astype(np.int32), send.astype(np.int32)


def strip_depth(frames):
    grid = np.full((S, S), -1, np.int32)
    for d in range(OVS):
        grid[d, OVS : S - OVS] = d
        grid[S - 1 - d, OVS : S - OVS] = d
        grid[OVS : S - OVS, d] = d
        grid[OVS : S - OVS, S - 1 - d] = d
    return np.tile(grid.reshape(-1), frames)


def per_device(latents, modulation, w_qkv, w_out, edge_table, space_ramp, time_ramp):
    block_in = latents[0, 0]
    tokens = block_in.shape[0]
    frames = tokens // (S * S)
    n = lax.axis_size("face")
    rows = w_qkv.shape[0]
    rim = OVT * S * S
    block_in = jnp.concatenate(
        [block_in[:rim], block_in[tokens - rim :], block_in[rim : tokens - rim]], axis=0
    )
    moved = modulate(block_in, modulation)
    if n == 4:
        me = lax.axis_index("face")
        core = me % 2

        def fetch(x, src_of):
            return lax.ppermute(x, "face", [(src_of(i), i) for i in range(n)])

        moved_chips = moved.reshape(tokens, 2, 2 * rows).transpose(1, 0, 2)

        def chip_weight(same_core, other_core):
            stack = jnp.zeros((2,) + w_qkv.shape, w_qkv.dtype)
            stack = lax.dynamic_update_index_in_dim(stack, same_core, core, 0)
            stack = lax.dynamic_update_index_in_dim(stack, other_core, 1 - core, 0)
            return stack.reshape(2 * rows, w_qkv.shape[1])

        def chip_part(chip, weight):
            return jnp.dot(
                lax.dynamic_index_in_dim(moved_chips, chip, 0, keepdims=False),
                weight,
                preferred_element_type=jnp.float32,
            )

        sib = fetch(w_qkv, lambda i: i ^ 1)
        far = fetch(w_qkv, lambda i: (i + 2) % n)
        local = chip_part(me // 2, chip_weight(w_qkv, sib))
        local, far = lax.optimization_barrier((local, far))
        fwd = fetch(far, lambda i: i ^ 1)
        qkv_sums = local + chip_part(1 - me // 2, chip_weight(far, fwd))
        w_out_late, _ = lax.optimization_barrier((w_out, (far, fwd)))
    else:
        qkv_pieces = face_pieces(w_qkv)
        w_out_late, _ = lax.optimization_barrier((w_out, [piece for piece, _ in qkv_pieces]))
        qkv_stack = jnp.zeros((n,) + w_qkv.shape, w_qkv.dtype)
        for piece, index in qkv_pieces:
            qkv_stack = lax.dynamic_update_index_in_dim(qkv_stack, piece, index, 0)
        w_qkv_full = qkv_stack.reshape(n * rows, w_qkv.shape[1])
        qkv_sums = jnp.dot(moved, w_qkv_full, preferred_element_type=jnp.float32)
    qkv_all = qkv_sums.astype(jnp.bfloat16)

    out_stack = jnp.zeros((n,) + w_out.shape, w_out.dtype)
    for piece, index in face_pieces(w_out_late):
        out_stack = lax.dynamic_update_index_in_dim(out_stack, piece, index, 0)
    w_out_full = out_stack.transpose(1, 0, 2).reshape(w_out.shape[0], n * w_out.shape[1])

    split = qkv_all.reshape(tokens, 3, HEADS, HD)
    queries = split[:, 0].transpose(1, 0, 2)
    keys = split[:, 1].transpose(1, 2, 0)
    values = split[:, 2].transpose(1, 0, 2)
    mid_a = 2 * rim + ((tokens - 2 * rim) // (2 * S * S)) * (S * S)
    gate = modulation[2]

    def tile_part(part_queries, part_in):
        return attend_project(part_queries, keys, values, w_out_full, part_in, gate)

    my_rows = lax.dynamic_index_in_dim(edge_table, lax.axis_index("face"), 0, keepdims=False)
    flips = my_rows[:, 2]
    routes = my_rows[:, 3]
    send_match = routes[None, :] == jnp.asarray(PARTNER_ROUTE, jnp.int32)[:, None]
    recv_match = routes[None, :] == jnp.arange(4, dtype=jnp.int32)[:, None]
    ramp = space_ramp.astype(jnp.float32)
    keep = ramp / (ramp + ramp[::-1])
    take = ramp[::-1] / (ramp + ramp[::-1])

    def strips_out(tile_out):
        part_tokens = tile_out.shape[0]
        part_frames = part_tokens // (S * S)
        _, send_table = strip_tables(part_frames)
        send_by_edge = jnp.where(flips[:, None] > 0, send_table[:, 1], send_table[:, 0])
        send_cells = jnp.sum(jnp.where(send_match[:, :, None], send_by_edge[None], 0), axis=1)
        send_cells = send_cells.reshape(-1)
        token_ids = jnp.arange(part_tokens, dtype=jnp.int32)
        pick = (send_cells[:, None] == token_ids[None, :]).astype(jnp.bfloat16)
        return jnp.dot(pick, tile_out, preferred_element_type=jnp.float32).astype(jnp.bfloat16)

    def strips_in(outgoing):
        strip_len = outgoing.shape[0] // 4
        arrived = []
        for route_id in range(4):
            sent = outgoing[route_id * strip_len : (route_id + 1) * strip_len]
            shift = -OFFSETS[route_id]
            arrived.append(
                lax.ppermute(sent, "face", [(i, (i + shift) % n) for i in range(n)])
            )
        return jnp.concatenate(arrived, axis=0)

    def space_blend(tile_out, arrived):
        part_tokens = tile_out.shape[0]
        part_frames = part_tokens // (S * S)
        recv_table, _ = strip_tables(part_frames)
        recv_cells = jnp.sum(jnp.where(recv_match[:, :, None], recv_table[None], 0), axis=1)
        recv_cells = recv_cells.reshape(-1)
        token_ids = jnp.arange(part_tokens, dtype=jnp.int32)
        place = (token_ids[:, None] == recv_cells[None, :]).astype(jnp.bfloat16)
        partner = jnp.dot(place, arrived, preferred_element_type=jnp.float32)
        dep = strip_depth(1)[:, None]
        w_keep = jnp.where(dep == 0, keep[0], keep[1])
        w_take = jnp.where(dep == 0, take[0], take[1])
        grid_shape = (part_frames, S * S, tile_out.shape[1])
        own = tile_out.astype(jnp.float32).reshape(grid_shape)
        partner = partner.reshape(grid_shape)
        mixed = jnp.where(dep >= 0, w_keep * own + w_take * partner, own)
        return mixed.reshape(tile_out.shape).astype(jnp.bfloat16)

    tile_rim = tile_part(queries[:, : 2 * rim], block_in[: 2 * rim])
    outgoing_rim = strips_out(tile_rim)
    arrived_rim = strips_in(outgoing_rim)
    first_queries, outgoing_rim = lax.optimization_barrier(
        (queries[:, 2 * rim : mid_a], outgoing_rim)
    )
    tile_first = tile_part(first_queries, block_in[2 * rim : mid_a])
    arrived_rim, tile_first = lax.optimization_barrier((arrived_rim, tile_first))
    spaced_rim = space_blend(tile_rim, arrived_rim)
    low, high = lax.optimization_barrier((spaced_rim[:rim], spaced_rim[rim:]))
    count = lax.axis_size("tm")
    lower = lax.ppermute(high, "tm", [(i, i + 1) for i in range(count - 1)])
    upper = lax.ppermute(low, "tm", [(i + 1, i) for i in range(count - 1)])
    outgoing_first = strips_out(tile_first)
    arrived_first = strips_in(outgoing_first)
    second_queries, low, high, outgoing_first = lax.optimization_barrier(
        (queries[:, mid_a:], low, high, outgoing_first)
    )
    tile_second = tile_part(second_queries, block_in[mid_a:])
    lower, upper, arrived_first, tile_second = lax.optimization_barrier(
        (lower, upper, arrived_first, tile_second)
    )
    spaced_mid = jnp.concatenate(
        [
            space_blend(tile_first, arrived_first),
            space_blend(tile_second, strips_in(strips_out(tile_second))),
        ],
        axis=0,
    )

    span_id = lax.axis_index("tm")
    has_lower = span_id > 0
    has_upper = span_id < count - 1
    tramp = time_ramp.astype(jnp.float32)
    hold = tramp / (tramp + tramp[::-1])
    pass_ = tramp[::-1] / (tramp + tramp[::-1])
    blocks = (OVT, S * S, D)
    low_f = low.astype(jnp.float32).reshape(blocks)
    high_f = high.astype(jnp.float32).reshape(blocks)
    hold_low = hold[:, None, None]
    pass_low = pass_[:, None, None]
    hold_high = hold[::-1][:, None, None]
    pass_high = pass_[::-1][:, None, None]
    low_mix = jnp.where(
        has_lower, hold_low * low_f + pass_low * lower.astype(jnp.float32).reshape(blocks), low_f
    ).reshape(rim, D)
    high_mix = jnp.where(
        has_upper, hold_high * high_f + pass_high * upper.astype(jnp.float32).reshape(blocks), high_f
    ).reshape(rim, D)
    result = jnp.concatenate(
        [low_mix.astype(jnp.bfloat16), spaced_mid, high_mix.astype(jnp.bfloat16)], axis=0
    )
    return result.reshape(1, 1, tokens, D)


def solution(mesh):
    return jax.shard_map(
        per_device,
        mesh=mesh,
        in_specs=(
            P(("groups", "tm"), "face", None, None),
            P("groups", None),
            P("face", None),
            P(None, "face"),
            P(),
            P(),
            P(),
        ),
        out_specs=P(("groups", "tm"), "face", None, None),
        check_vma=False,
    )
```

```python
import math

import jax
import jax.numpy as jnp
import numpy as np
from jax import lax
from jax.experimental import pallas as pl
from jax.experimental.pallas import tpu as pltpu
from jax.sharding import PartitionSpec as P

D = 1152
HD = 72
HEADS = 8
S = 8
OVS = 2
OVT = 4
MID = S - 2 * OVS


NORM_EPS = 1e-06
OFFSETS = (1, -1, 2, -2)
PARTNER_ROUTE = (1, 0, 3, 2)


def modulate(block_in, modulation):
    values = block_in.astype(jnp.float32)
    center = jnp.mean(values, axis=-1, keepdims=True)
    spread = jnp.mean(jnp.square(values - center), axis=-1, keepdims=True)
    normed = (values - center) * lax.rsqrt(spread + NORM_EPS)
    return (normed * (1.0 + modulation[1]) + modulation[0]).astype(jnp.bfloat16)


HEADS_PER_STEP = 2


def attention_kernel(*refs):
    x_ref, g_ref, o_ref, acc_ref = refs[-4:]
    per_head = refs[:-4]
    step = pl.program_id(1)

    @pl.when(step == 0)
    def _():
        acc_ref[...] = jnp.zeros_like(acc_ref)

    total = None
    for j in range(HEADS_PER_STEP):
        q_ref, k_ref, v_ref, w_ref = per_head[4 * j : 4 * j + 4]
        scores = jnp.dot(q_ref[0], k_ref[0], preferred_element_type=jnp.float32) * (
            1.0 / math.sqrt(HD)
        )
        row_max = jnp.max(scores, axis=-1, keepdims=True)
        weights = jnp.exp(scores - row_max)
        row_sum = jnp.sum(weights, axis=-1, keepdims=True)
        probabilities = (weights * (1.0 / row_sum)).astype(jnp.bfloat16)
        mixed = jnp.dot(probabilities, v_ref[0], preferred_element_type=jnp.float32).astype(
            jnp.bfloat16
        )
        part = jnp.dot(mixed, w_ref[...], preferred_element_type=jnp.float32)
        total = part if total is None else total + part
    acc_ref[...] += total

    @pl.when(step == pl.num_programs(1) - 1)
    def _():
        o_ref[...] = (x_ref[...].astype(jnp.float32) + g_ref[...] * acc_ref[...]).astype(
            o_ref.dtype
        )


def attend_project(queries, keys, values, w_out_full, block_in, gate):
    heads, size, tokens = keys.shape
    chunk = queries.shape[1]
    width = block_in.shape[1]
    hb = HEADS_PER_STEP
    in_specs = []
    operands = []
    for j in range(hb):
        in_specs += [
            pl.BlockSpec((1, chunk, size), lambda i, h, j=j: (hb * h + j, i, 0)),
            pl.BlockSpec((1, size, tokens), lambda i, h, j=j: (hb * h + j, 0, 0)),
            pl.BlockSpec((1, tokens, size), lambda i, h, j=j: (hb * h + j, 0, 0)),
            pl.BlockSpec((size, width), lambda i, h, j=j: (hb * h + j, 0)),
        ]
        operands += [queries, keys, values, w_out_full]
    in_specs += [
        pl.BlockSpec((chunk, width), lambda i, h: (i, 0)),
        pl.BlockSpec((1, width), lambda i, h: (0, 0)),
    ]
    return pl.pallas_call(
        attention_kernel,
        grid=(1, heads // hb),
        in_specs=in_specs,
        out_specs=pl.BlockSpec((chunk, width), lambda i, h: (i, 0)),
        out_shape=jax.ShapeDtypeStruct(block_in.shape, block_in.dtype),
        scratch_shapes=[pltpu.VMEM((chunk, width), jnp.float32)],
        compiler_params=pltpu.CompilerParams(dimension_semantics=("arbitrary", "arbitrary")),
    )(*operands, block_in, gate.reshape(1, width))


def face_pieces(shard):
    n = lax.axis_size("face")
    me = lax.axis_index("face")

    def fetch(x, src_of):
        return lax.ppermute(x, "face", [(src_of(i), i) for i in range(n)])

    pieces = [(shard, me), (fetch(shard, lambda i: i ^ 1), me ^ 1)]
    for j in range(1, n // 2):
        far = fetch(shard, lambda i: (i + 2 * j) % n)
        pieces.append((far, (me + 2 * j) % n))
        pieces.append((fetch(far, lambda i: i ^ 1), ((me ^ 1) + 2 * j) % n))
    return pieces


def strip_tables(frames):
    frame, depth, pos = np.meshgrid(
        np.arange(frames), np.arange(OVS), np.arange(MID), indexing="ij"
    )

    def token(edge, d, t):
        row = (d, S - 1 - d, OVS + t, OVS + t)[edge]
        col = (OVS + t, OVS + t, d, S - 1 - d)[edge]
        return (frame * (S * S) + row * S + col).reshape(-1)

    recv = np.stack([token(e, depth, pos) for e in range(4)])
    send = np.stack(
        [[token(e, OVS - 1 - depth, pos if flip == 0 else MID - 1 - pos) for flip in range(2)]
         for e in range(4)]
    )
    return recv.astype(np.int32), send.astype(np.int32)


def strip_depth(frames):
    grid = np.full((S, S), -1, np.int32)
    for d in range(OVS):
        grid[d, OVS : S - OVS] = d
        grid[S - 1 - d, OVS : S - OVS] = d
        grid[OVS : S - OVS, d] = d
        grid[OVS : S - OVS, S - 1 - d] = d
    return np.tile(grid.reshape(-1), frames)


def per_device(latents, modulation, w_qkv, w_out, edge_table, space_ramp, time_ramp):
    block_in = latents[0, 0]
    tokens = block_in.shape[0]
    frames = tokens // (S * S)
    n = lax.axis_size("face")
    rows = w_qkv.shape[0]
    rim = OVT * S * S
    block_in = jnp.concatenate(
        [block_in[:rim], block_in[tokens - rim :], block_in[rim : tokens - rim]], axis=0
    )
    moved = modulate(block_in, modulation)
    if n == 4:
        me = lax.axis_index("face")
        core = me % 2

        def fetch(x, src_of):
            return lax.ppermute(x, "face", [(src_of(i), i) for i in range(n)])

        moved_chips = moved.reshape(tokens, 2, 2 * rows).transpose(1, 0, 2)

        def chip_weight(same_core, other_core):
            tripled = jnp.concatenate([same_core, other_core, same_core], axis=0)
            return lax.dynamic_slice_in_dim(tripled, core * rows, 2 * rows, axis=0)

        def chip_part(chip, weight):
            return jnp.dot(
                lax.dynamic_index_in_dim(moved_chips, chip, 0, keepdims=False),
                weight,
                preferred_element_type=jnp.float32,
            )

        sib = fetch(w_qkv, lambda i: i ^ 1)
        far = fetch(w_qkv, lambda i: (i + 2) % n)
        local = chip_part(me // 2, chip_weight(w_qkv, sib))
        local, far = lax.optimization_barrier((local, far))
        fwd = fetch(far, lambda i: i ^ 1)
        qkv_sums = local + chip_part(1 - me // 2, chip_weight(far, fwd))
        w_out_late, _ = lax.optimization_barrier((w_out, (far, fwd)))
    else:
        qkv_pieces = face_pieces(w_qkv)
        w_out_late, _ = lax.optimization_barrier((w_out, [piece for piece, _ in qkv_pieces]))
        qkv_stack = jnp.zeros((n,) + w_qkv.shape, w_qkv.dtype)
        for piece, index in qkv_pieces:
            qkv_stack = lax.dynamic_update_index_in_dim(qkv_stack, piece, index, 0)
        w_qkv_full = qkv_stack.reshape(n * rows, w_qkv.shape[1])
        qkv_sums = jnp.dot(moved, w_qkv_full, preferred_element_type=jnp.float32)
    qkv_all = qkv_sums.astype(jnp.bfloat16)

    out_stack = jnp.zeros((n,) + w_out.shape, w_out.dtype)
    for piece, index in face_pieces(w_out_late):
        out_stack = lax.dynamic_update_index_in_dim(out_stack, piece, index, 0)
    w_out_full = out_stack.transpose(1, 0, 2).reshape(w_out.shape[0], n * w_out.shape[1])

    split = qkv_all.reshape(tokens, 3, HEADS, HD)
    queries = split[:, 0].transpose(1, 0, 2)
    keys = split[:, 1].transpose(1, 2, 0)
    values = split[:, 2].transpose(1, 0, 2)
    mid_a = 2 * rim + ((tokens - 2 * rim) // (2 * S * S)) * (S * S)
    gate = modulation[2]

    def tile_part(part_queries, part_in):
        return attend_project(part_queries, keys, values, w_out_full, part_in, gate)

    my_rows = lax.dynamic_index_in_dim(edge_table, lax.axis_index("face"), 0, keepdims=False)
    flips = my_rows[:, 2]
    routes = my_rows[:, 3]
    send_match = routes[None, :] == jnp.asarray(PARTNER_ROUTE, jnp.int32)[:, None]
    recv_match = routes[None, :] == jnp.arange(4, dtype=jnp.int32)[:, None]
    ramp = space_ramp.astype(jnp.float32)
    keep = ramp / (ramp + ramp[::-1])
    take = ramp[::-1] / (ramp + ramp[::-1])

    def strips_out(tile_out):
        part_tokens = tile_out.shape[0]
        part_frames = part_tokens // (S * S)
        _, send_table = strip_tables(part_frames)
        send_by_edge = jnp.where(flips[:, None] > 0, send_table[:, 1], send_table[:, 0])
        send_cells = jnp.sum(jnp.where(send_match[:, :, None], send_by_edge[None], 0), axis=1)
        send_cells = send_cells.reshape(-1)
        token_ids = jnp.arange(part_tokens, dtype=jnp.int32)
        pick = (send_cells[:, None] == token_ids[None, :]).astype(jnp.bfloat16)
        return jnp.dot(pick, tile_out, preferred_element_type=jnp.float32).astype(jnp.bfloat16)

    def strips_in(outgoing):
        strip_len = outgoing.shape[0] // 4
        arrived = []
        for route_id in range(4):
            sent = outgoing[route_id * strip_len : (route_id + 1) * strip_len]
            shift = -OFFSETS[route_id]
            arrived.append(
                lax.ppermute(sent, "face", [(i, (i + shift) % n) for i in range(n)])
            )
        return jnp.concatenate(arrived, axis=0)

    def space_blend(tile_out, arrived):
        part_tokens = tile_out.shape[0]
        part_frames = part_tokens // (S * S)
        recv_table, _ = strip_tables(part_frames)
        recv_cells = jnp.sum(jnp.where(recv_match[:, :, None], recv_table[None], 0), axis=1)
        recv_cells = recv_cells.reshape(-1)
        token_ids = jnp.arange(part_tokens, dtype=jnp.int32)
        place = (token_ids[:, None] == recv_cells[None, :]).astype(jnp.bfloat16)
        partner = jnp.dot(place, arrived, preferred_element_type=jnp.float32)
        dep = strip_depth(1)[:, None]
        w_keep = jnp.where(dep == 0, keep[0], keep[1])
        w_take = jnp.where(dep == 0, take[0], take[1])
        grid_shape = (part_frames, S * S, tile_out.shape[1])
        own = tile_out.astype(jnp.float32).reshape(grid_shape)
        partner = partner.reshape(grid_shape)
        mixed = jnp.where(dep >= 0, w_keep * own + w_take * partner, own)
        return mixed.reshape(tile_out.shape).astype(jnp.bfloat16)

    tile_rim = tile_part(queries[:, : 2 * rim], block_in[: 2 * rim])
    outgoing_rim = strips_out(tile_rim)
    arrived_rim = strips_in(outgoing_rim)
    first_queries, outgoing_rim = lax.optimization_barrier(
        (queries[:, 2 * rim : mid_a], outgoing_rim)
    )
    tile_first = tile_part(first_queries, block_in[2 * rim : mid_a])
    arrived_rim, tile_first = lax.optimization_barrier((arrived_rim, tile_first))
    spaced_rim = space_blend(tile_rim, arrived_rim)
    low, high = lax.optimization_barrier((spaced_rim[:rim], spaced_rim[rim:]))
    count = lax.axis_size("tm")
    lower = lax.ppermute(high, "tm", [(i, i + 1) for i in range(count - 1)])
    upper = lax.ppermute(low, "tm", [(i + 1, i) for i in range(count - 1)])
    outgoing_first = strips_out(tile_first)
    arrived_first = strips_in(outgoing_first)
    second_queries, low, high, outgoing_first = lax.optimization_barrier(
        (queries[:, mid_a:], low, high, outgoing_first)
    )
    tile_second = tile_part(second_queries, block_in[mid_a:])
    lower, upper, arrived_first, tile_second = lax.optimization_barrier(
        (lower, upper, arrived_first, tile_second)
    )
    spaced_mid = jnp.concatenate(
        [
            space_blend(tile_first, arrived_first),
            space_blend(tile_second, strips_in(strips_out(tile_second))),
        ],
        axis=0,
    )

    span_id = lax.axis_index("tm")
    has_lower = span_id > 0
    has_upper = span_id < count - 1
    tramp = time_ramp.astype(jnp.float32)
    hold = tramp / (tramp + tramp[::-1])
    pass_ = tramp[::-1] / (tramp + tramp[::-1])
    blocks = (OVT, S * S, D)
    low_f = low.astype(jnp.float32).reshape(blocks)
    high_f = high.astype(jnp.float32).reshape(blocks)
    hold_low = hold[:, None, None]
    pass_low = pass_[:, None, None]
    hold_high = hold[::-1][:, None, None]
    pass_high = pass_[::-1][:, None, None]
    low_mix = jnp.where(
        has_lower, hold_low * low_f + pass_low * lower.astype(jnp.float32).reshape(blocks), low_f
    ).reshape(rim, D)
    high_mix = jnp.where(
        has_upper, hold_high * high_f + pass_high * upper.astype(jnp.float32).reshape(blocks), high_f
    ).reshape(rim, D)
    result = jnp.concatenate(
        [low_mix.astype(jnp.bfloat16), spaced_mid, high_mix.astype(jnp.bfloat16)], axis=0
    )
    return result.reshape(1, 1, tokens, D)


def solution(mesh):
    return jax.shard_map(
        per_device,
        mesh=mesh,
        in_specs=(
            P(("groups", "tm"), "face", None, None),
            P("groups", None),
            P("face", None),
            P(None, "face"),
            P(),
            P(),
            P(),
        ),
        out_specs=P(("groups", "tm"), "face", None, None),
        check_vma=False,
    )
```

```python
import math

import jax
import jax.numpy as jnp
import numpy as np
from jax import lax
from jax.experimental import pallas as pl
from jax.experimental.pallas import tpu as pltpu
from jax.sharding import PartitionSpec as P

D = 1152
HD = 72
HEADS = 8
S = 8
OVS = 2
OVT = 4
MID = S - 2 * OVS


NORM_EPS = 1e-06
OFFSETS = (1, -1, 2, -2)
PARTNER_ROUTE = (1, 0, 3, 2)


def modulate(block_in, modulation):
    values = block_in.astype(jnp.float32)
    center = jnp.mean(values, axis=-1, keepdims=True)
    spread = jnp.mean(jnp.square(values - center), axis=-1, keepdims=True)
    normed = (values - center) * lax.rsqrt(spread + NORM_EPS)
    return (normed * (1.0 + modulation[1]) + modulation[0]).astype(jnp.bfloat16)


HEADS_PER_STEP = 4


def attention_kernel(*refs):
    x_ref, g_ref, o_ref, acc_ref = refs[-4:]
    per_head = refs[:-4]
    step = pl.program_id(1)

    @pl.when(step == 0)
    def _():
        acc_ref[...] = jnp.zeros_like(acc_ref)

    total = None
    for j in range(HEADS_PER_STEP):
        q_ref, k_ref, v_ref, w_ref = per_head[4 * j : 4 * j + 4]
        scores = jnp.dot(q_ref[0], k_ref[0], preferred_element_type=jnp.float32) * (
            1.0 / math.sqrt(HD)
        )
        row_max = jnp.max(scores, axis=-1, keepdims=True)
        weights = jnp.exp(scores - row_max)
        row_sum = jnp.sum(weights, axis=-1, keepdims=True)
        probabilities = (weights * (1.0 / row_sum)).astype(jnp.bfloat16)
        mixed = jnp.dot(probabilities, v_ref[0], preferred_element_type=jnp.float32).astype(
            jnp.bfloat16
        )
        part = jnp.dot(mixed, w_ref[...], preferred_element_type=jnp.float32)
        total = part if total is None else total + part
    acc_ref[...] += total

    @pl.when(step == pl.num_programs(1) - 1)
    def _():
        o_ref[...] = (x_ref[...].astype(jnp.float32) + g_ref[...] * acc_ref[...]).astype(
            o_ref.dtype
        )


def attend_project(queries, keys, values, w_out_full, block_in, gate):
    heads, size, tokens = keys.shape
    chunk = queries.shape[1]
    width = block_in.shape[1]
    hb = HEADS_PER_STEP
    in_specs = []
    operands = []
    for j in range(hb):
        in_specs += [
            pl.BlockSpec((1, chunk, size), lambda i, h, j=j: (hb * h + j, i, 0)),
            pl.BlockSpec((1, size, tokens), lambda i, h, j=j: (hb * h + j, 0, 0)),
            pl.BlockSpec((1, tokens, size), lambda i, h, j=j: (hb * h + j, 0, 0)),
            pl.BlockSpec((size, width), lambda i, h, j=j: (hb * h + j, 0)),
        ]
        operands += [queries, keys, values, w_out_full]
    in_specs += [
        pl.BlockSpec((chunk, width), lambda i, h: (i, 0)),
        pl.BlockSpec((1, width), lambda i, h: (0, 0)),
    ]
    return pl.pallas_call(
        attention_kernel,
        grid=(1, heads // hb),
        in_specs=in_specs,
        out_specs=pl.BlockSpec((chunk, width), lambda i, h: (i, 0)),
        out_shape=jax.ShapeDtypeStruct(block_in.shape, block_in.dtype),
        scratch_shapes=[pltpu.VMEM((chunk, width), jnp.float32)],
        compiler_params=pltpu.CompilerParams(dimension_semantics=("arbitrary", "arbitrary")),
    )(*operands, block_in, gate.reshape(1, width))


def face_pieces(shard):
    n = lax.axis_size("face")
    me = lax.axis_index("face")

    def fetch(x, src_of):
        return lax.ppermute(x, "face", [(src_of(i), i) for i in range(n)])

    pieces = [(shard, me), (fetch(shard, lambda i: i ^ 1), me ^ 1)]
    for j in range(1, n // 2):
        far = fetch(shard, lambda i: (i + 2 * j) % n)
        pieces.append((far, (me + 2 * j) % n))
        pieces.append((fetch(far, lambda i: i ^ 1), ((me ^ 1) + 2 * j) % n))
    return pieces


def strip_tables(frames):
    frame, depth, pos = np.meshgrid(
        np.arange(frames), np.arange(OVS), np.arange(MID), indexing="ij"
    )

    def token(edge, d, t):
        row = (d, S - 1 - d, OVS + t, OVS + t)[edge]
        col = (OVS + t, OVS + t, d, S - 1 - d)[edge]
        return (frame * (S * S) + row * S + col).reshape(-1)

    recv = np.stack([token(e, depth, pos) for e in range(4)])
    send = np.stack(
        [[token(e, OVS - 1 - depth, pos if flip == 0 else MID - 1 - pos) for flip in range(2)]
         for e in range(4)]
    )
    return recv.astype(np.int32), send.astype(np.int32)


def strip_depth(frames):
    grid = np.full((S, S), -1, np.int32)
    for d in range(OVS):
        grid[d, OVS : S - OVS] = d
        grid[S - 1 - d, OVS : S - OVS] = d
        grid[OVS : S - OVS, d] = d
        grid[OVS : S - OVS, S - 1 - d] = d
    return np.tile(grid.reshape(-1), frames)


def per_device(latents, modulation, w_qkv, w_out, edge_table, space_ramp, time_ramp):
    block_in = latents[0, 0]
    tokens = block_in.shape[0]
    frames = tokens // (S * S)
    n = lax.axis_size("face")
    rows = w_qkv.shape[0]
    rim = OVT * S * S
    block_in = jnp.concatenate(
        [block_in[:rim], block_in[tokens - rim :], block_in[rim : tokens - rim]], axis=0
    )
    moved = modulate(block_in, modulation)
    if n == 4:
        me = lax.axis_index("face")
        core = me % 2

        def fetch(x, src_of):
            return lax.ppermute(x, "face", [(src_of(i), i) for i in range(n)])

        moved_chips = moved.reshape(tokens, 2, 2 * rows).transpose(1, 0, 2)

        def chip_weight(same_core, other_core):
            stack = jnp.zeros((2,) + w_qkv.shape, w_qkv.dtype)
            stack = lax.dynamic_update_index_in_dim(stack, same_core, core, 0)
            stack = lax.dynamic_update_index_in_dim(stack, other_core, 1 - core, 0)
            return stack.reshape(2 * rows, w_qkv.shape[1])

        def chip_part(chip, weight):
            return jnp.dot(
                lax.dynamic_index_in_dim(moved_chips, chip, 0, keepdims=False),
                weight,
                preferred_element_type=jnp.float32,
            )

        sib = fetch(w_qkv, lambda i: i ^ 1)
        far = fetch(w_qkv, lambda i: (i + 2) % n)
        local = chip_part(me // 2, chip_weight(w_qkv, sib))
        local, far = lax.optimization_barrier((local, far))
        fwd = fetch(far, lambda i: i ^ 1)
        qkv_sums = local + chip_part(1 - me // 2, chip_weight(far, fwd))
        w_out_late, _ = lax.optimization_barrier((w_out, (far, fwd)))
    else:
        qkv_pieces = face_pieces(w_qkv)
        w_out_late, _ = lax.optimization_barrier((w_out, [piece for piece, _ in qkv_pieces]))
        qkv_stack = jnp.zeros((n,) + w_qkv.shape, w_qkv.dtype)
        for piece, index in qkv_pieces:
            qkv_stack = lax.dynamic_update_index_in_dim(qkv_stack, piece, index, 0)
        w_qkv_full = qkv_stack.reshape(n * rows, w_qkv.shape[1])
        qkv_sums = jnp.dot(moved, w_qkv_full, preferred_element_type=jnp.float32)
    qkv_all = qkv_sums.astype(jnp.bfloat16)

    out_stack = jnp.zeros((n,) + w_out.shape, w_out.dtype)
    for piece, index in face_pieces(w_out_late):
        out_stack = lax.dynamic_update_index_in_dim(out_stack, piece, index, 0)
    w_out_full = out_stack.transpose(1, 0, 2).reshape(w_out.shape[0], n * w_out.shape[1])

    split = qkv_all.reshape(tokens, 3, HEADS, HD)
    queries = split[:, 0].transpose(1, 0, 2)
    keys = split[:, 1].transpose(1, 2, 0)
    values = split[:, 2].transpose(1, 0, 2)
    mid_a = 2 * rim + ((tokens - 2 * rim) // (2 * S * S)) * (S * S)
    gate = modulation[2]

    def tile_part(part_queries, part_in):
        return attend_project(part_queries, keys, values, w_out_full, part_in, gate)

    my_rows = lax.dynamic_index_in_dim(edge_table, lax.axis_index("face"), 0, keepdims=False)
    flips = my_rows[:, 2]
    routes = my_rows[:, 3]
    send_match = routes[None, :] == jnp.asarray(PARTNER_ROUTE, jnp.int32)[:, None]
    recv_match = routes[None, :] == jnp.arange(4, dtype=jnp.int32)[:, None]
    ramp = space_ramp.astype(jnp.float32)
    keep = ramp / (ramp + ramp[::-1])
    take = ramp[::-1] / (ramp + ramp[::-1])

    def strips_out(tile_out):
        part_tokens = tile_out.shape[0]
        part_frames = part_tokens // (S * S)
        _, send_table = strip_tables(part_frames)
        send_by_edge = jnp.where(flips[:, None] > 0, send_table[:, 1], send_table[:, 0])
        send_cells = jnp.sum(jnp.where(send_match[:, :, None], send_by_edge[None], 0), axis=1)
        send_cells = send_cells.reshape(-1)
        token_ids = jnp.arange(part_tokens, dtype=jnp.int32)
        pick = (send_cells[:, None] == token_ids[None, :]).astype(jnp.bfloat16)
        return jnp.dot(pick, tile_out, preferred_element_type=jnp.float32).astype(jnp.bfloat16)

    def strips_in(outgoing):
        strip_len = outgoing.shape[0] // 4
        arrived = []
        for route_id in range(4):
            sent = outgoing[route_id * strip_len : (route_id + 1) * strip_len]
            shift = -OFFSETS[route_id]
            arrived.append(
                lax.ppermute(sent, "face", [(i, (i + shift) % n) for i in range(n)])
            )
        return jnp.concatenate(arrived, axis=0)

    def space_blend(tile_out, arrived):
        part_tokens = tile_out.shape[0]
        part_frames = part_tokens // (S * S)
        recv_table, _ = strip_tables(part_frames)
        recv_cells = jnp.sum(jnp.where(recv_match[:, :, None], recv_table[None], 0), axis=1)
        recv_cells = recv_cells.reshape(-1)
        token_ids = jnp.arange(part_tokens, dtype=jnp.int32)
        place = (token_ids[:, None] == recv_cells[None, :]).astype(jnp.bfloat16)
        partner = jnp.dot(place, arrived, preferred_element_type=jnp.float32)
        dep = strip_depth(1)[:, None]
        w_keep = jnp.where(dep == 0, keep[0], keep[1])
        w_take = jnp.where(dep == 0, take[0], take[1])
        grid_shape = (part_frames, S * S, tile_out.shape[1])
        own = tile_out.astype(jnp.float32).reshape(grid_shape)
        partner = partner.reshape(grid_shape)
        mixed = jnp.where(dep >= 0, w_keep * own + w_take * partner, own)
        return mixed.reshape(tile_out.shape).astype(jnp.bfloat16)

    tile_rim = tile_part(queries[:, : 2 * rim], block_in[: 2 * rim])
    outgoing_rim = strips_out(tile_rim)
    arrived_rim = strips_in(outgoing_rim)
    first_queries, outgoing_rim = lax.optimization_barrier(
        (queries[:, 2 * rim : mid_a], outgoing_rim)
    )
    tile_first = tile_part(first_queries, block_in[2 * rim : mid_a])
    arrived_rim, tile_first = lax.optimization_barrier((arrived_rim, tile_first))
    spaced_rim = space_blend(tile_rim, arrived_rim)
    low, high = lax.optimization_barrier((spaced_rim[:rim], spaced_rim[rim:]))
    count = lax.axis_size("tm")
    lower = lax.ppermute(high, "tm", [(i, i + 1) for i in range(count - 1)])
    upper = lax.ppermute(low, "tm", [(i + 1, i) for i in range(count - 1)])
    outgoing_first = strips_out(tile_first)
    arrived_first = strips_in(outgoing_first)
    second_queries, low, high, outgoing_first = lax.optimization_barrier(
        (queries[:, mid_a:], low, high, outgoing_first)
    )
    tile_second = tile_part(second_queries, block_in[mid_a:])
    lower, upper, arrived_first, tile_second = lax.optimization_barrier(
        (lower, upper, arrived_first, tile_second)
    )
    spaced_mid = jnp.concatenate(
        [
            space_blend(tile_first, arrived_first),
            space_blend(tile_second, strips_in(strips_out(tile_second))),
        ],
        axis=0,
    )

    span_id = lax.axis_index("tm")
    has_lower = span_id > 0
    has_upper = span_id < count - 1
    tramp = time_ramp.astype(jnp.float32)
    hold = tramp / (tramp + tramp[::-1])
    pass_ = tramp[::-1] / (tramp + tramp[::-1])
    blocks = (OVT, S * S, D)
    low_f = low.astype(jnp.float32).reshape(blocks)
    high_f = high.astype(jnp.float32).reshape(blocks)
    hold_low = hold[:, None, None]
    pass_low = pass_[:, None, None]
    hold_high = hold[::-1][:, None, None]
    pass_high = pass_[::-1][:, None, None]
    low_mix = jnp.where(
        has_lower, hold_low * low_f + pass_low * lower.astype(jnp.float32).reshape(blocks), low_f
    ).reshape(rim, D)
    high_mix = jnp.where(
        has_upper, hold_high * high_f + pass_high * upper.astype(jnp.float32).reshape(blocks), high_f
    ).reshape(rim, D)
    result = jnp.concatenate(
        [low_mix.astype(jnp.bfloat16), spaced_mid, high_mix.astype(jnp.bfloat16)], axis=0
    )
    return result.reshape(1, 1, tokens, D)


def solution(mesh):
    return jax.shard_map(
        per_device,
        mesh=mesh,
        in_specs=(
            P(("groups", "tm"), "face", None, None),
            P("groups", None),
            P("face", None),
            P(None, "face"),
            P(),
            P(),
            P(),
        ),
        out_specs=P(("groups", "tm"), "face", None, None),
        check_vma=False,
    )
```

```python
import math

import jax
import jax.numpy as jnp
import numpy as np
from jax import lax
from jax.experimental import pallas as pl
from jax.experimental.pallas import tpu as pltpu
from jax.sharding import PartitionSpec as P

D = 1152
HD = 72
HEADS = 8
S = 8
OVS = 2
OVT = 4
MID = S - 2 * OVS


NORM_EPS = 1e-06
OFFSETS = (1, -1, 2, -2)
PARTNER_ROUTE = (1, 0, 3, 2)


def modulate(block_in, modulation):
    values = block_in.astype(jnp.float32)
    center = jnp.mean(values, axis=-1, keepdims=True)
    spread = jnp.mean(jnp.square(values - center), axis=-1, keepdims=True)
    normed = (values - center) * lax.rsqrt(spread + NORM_EPS)
    return (normed * (1.0 + modulation[1]) + modulation[0]).astype(jnp.bfloat16)


HEADS_PER_STEP = 4


def attention_kernel(*refs):
    x_ref, g_ref, o_ref, acc_ref = refs[-4:]
    per_head = refs[:-4]
    step = pl.program_id(1)

    @pl.when(step == 0)
    def _():
        acc_ref[...] = jnp.zeros_like(acc_ref)

    total = None
    for j in range(HEADS_PER_STEP):
        q_ref, k_ref, v_ref, w_ref = per_head[4 * j : 4 * j + 4]
        scores = jnp.dot(q_ref[0], k_ref[0], preferred_element_type=jnp.float32) * (
            1.0 / math.sqrt(HD)
        )
        row_max = jnp.max(scores, axis=-1, keepdims=True)
        weights = jnp.exp(scores - row_max)
        row_sum = jnp.sum(weights, axis=-1, keepdims=True)
        probabilities = (weights * (1.0 / row_sum)).astype(jnp.bfloat16)
        mixed = jnp.dot(probabilities, v_ref[0], preferred_element_type=jnp.float32).astype(
            jnp.bfloat16
        )
        part = jnp.dot(mixed, w_ref[...], preferred_element_type=jnp.float32)
        total = part if total is None else total + part
    acc_ref[...] += total

    @pl.when(step == pl.num_programs(1) - 1)
    def _():
        o_ref[...] = (x_ref[...].astype(jnp.float32) + g_ref[...] * acc_ref[...]).astype(
            o_ref.dtype
        )


def attend_project(queries, keys, values, w_out_full, block_in, gate):
    heads, size, tokens = keys.shape
    chunk = queries.shape[1]
    width = block_in.shape[1]
    hb = HEADS_PER_STEP
    in_specs = []
    operands = []
    for j in range(hb):
        in_specs += [
            pl.BlockSpec((1, chunk, size), lambda i, h, j=j: (hb * h + j, i, 0)),
            pl.BlockSpec((1, size, tokens), lambda i, h, j=j: (hb * h + j, 0, 0)),
            pl.BlockSpec((1, tokens, size), lambda i, h, j=j: (hb * h + j, 0, 0)),
            pl.BlockSpec((size, width), lambda i, h, j=j: (hb * h + j, 0)),
        ]
        operands += [queries, keys, values, w_out_full]
    in_specs += [
        pl.BlockSpec((chunk, width), lambda i, h: (i, 0)),
        pl.BlockSpec((1, width), lambda i, h: (0, 0)),
    ]
    return pl.pallas_call(
        attention_kernel,
        grid=(1, heads // hb),
        in_specs=in_specs,
        out_specs=pl.BlockSpec((chunk, width), lambda i, h: (i, 0)),
        out_shape=jax.ShapeDtypeStruct(block_in.shape, block_in.dtype),
        scratch_shapes=[pltpu.VMEM((chunk, width), jnp.float32)],
        compiler_params=pltpu.CompilerParams(dimension_semantics=("arbitrary", "arbitrary")),
    )(*operands, block_in, gate.reshape(1, width))


def face_pieces(shard):
    n = lax.axis_size("face")
    me = lax.axis_index("face")

    def fetch(x, src_of):
        return lax.ppermute(x, "face", [(src_of(i), i) for i in range(n)])

    pieces = [(shard, me), (fetch(shard, lambda i: i ^ 1), me ^ 1)]
    for j in range(1, n // 2):
        far = fetch(shard, lambda i: (i + 2 * j) % n)
        pieces.append((far, (me + 2 * j) % n))
        pieces.append((fetch(far, lambda i: i ^ 1), ((me ^ 1) + 2 * j) % n))
    return pieces


def strip_tables(frames):
    frame, depth, pos = np.meshgrid(
        np.arange(frames), np.arange(OVS), np.arange(MID), indexing="ij"
    )

    def token(edge, d, t):
        row = (d, S - 1 - d, OVS + t, OVS + t)[edge]
        col = (OVS + t, OVS + t, d, S - 1 - d)[edge]
        return (frame * (S * S) + row * S + col).reshape(-1)

    recv = np.stack([token(e, depth, pos) for e in range(4)])
    send = np.stack(
        [[token(e, OVS - 1 - depth, pos if flip == 0 else MID - 1 - pos) for flip in range(2)]
         for e in range(4)]
    )
    return recv.astype(np.int32), send.astype(np.int32)


def strip_depth(frames):
    grid = np.full((S, S), -1, np.int32)
    for d in range(OVS):
        grid[d, OVS : S - OVS] = d
        grid[S - 1 - d, OVS : S - OVS] = d
        grid[OVS : S - OVS, d] = d
        grid[OVS : S - OVS, S - 1 - d] = d
    return np.tile(grid.reshape(-1), frames)


def per_device(latents, modulation, w_qkv, w_out, edge_table, space_ramp, time_ramp):
    block_in = latents[0, 0]
    tokens = block_in.shape[0]
    frames = tokens // (S * S)
    n = lax.axis_size("face")
    rows = w_qkv.shape[0]
    rim = OVT * S * S
    block_in = jnp.concatenate(
        [block_in[:rim], block_in[tokens - rim :], block_in[rim : tokens - rim]], axis=0
    )
    moved = modulate(block_in, modulation)
    if n == 4:
        me = lax.axis_index("face")
        core = me % 2

        def fetch(x, src_of):
            return lax.ppermute(x, "face", [(src_of(i), i) for i in range(n)])

        moved_chips = moved.reshape(tokens, 2, 2 * rows).transpose(1, 0, 2)

        def chip_weight(same_core, other_core):
            stack = jnp.zeros((2,) + w_qkv.shape, w_qkv.dtype)
            stack = lax.dynamic_update_index_in_dim(stack, same_core, core, 0)
            stack = lax.dynamic_update_index_in_dim(stack, other_core, 1 - core, 0)
            return stack.reshape(2 * rows, w_qkv.shape[1])

        def chip_part(chip, weight):
            return jnp.dot(
                lax.dynamic_index_in_dim(moved_chips, chip, 0, keepdims=False),
                weight,
                preferred_element_type=jnp.float32,
            )

        sib = fetch(w_qkv, lambda i: i ^ 1)
        far = fetch(w_qkv, lambda i: (i + 2) % n)
        local = chip_part(me // 2, chip_weight(w_qkv, sib))
        local, far = lax.optimization_barrier((local, far))
        fwd = fetch(far, lambda i: i ^ 1)
        qkv_sums = local + chip_part(1 - me // 2, chip_weight(far, fwd))
        w_out_late, _ = lax.optimization_barrier((w_out, (far, fwd)))
    else:
        qkv_pieces = face_pieces(w_qkv)
        w_out_late, _ = lax.optimization_barrier((w_out, [piece for piece, _ in qkv_pieces]))
        qkv_stack = jnp.zeros((n,) + w_qkv.shape, w_qkv.dtype)
        for piece, index in qkv_pieces:
            qkv_stack = lax.dynamic_update_index_in_dim(qkv_stack, piece, index, 0)
        w_qkv_full = qkv_stack.reshape(n * rows, w_qkv.shape[1])
        qkv_sums = jnp.dot(moved, w_qkv_full, preferred_element_type=jnp.float32)
    qkv_all = qkv_sums.astype(jnp.bfloat16)

    out_stack = jnp.zeros((n,) + w_out.shape, w_out.dtype)
    for piece, index in face_pieces(w_out_late):
        out_stack = lax.dynamic_update_index_in_dim(out_stack, piece, index, 0)
    w_out_full = out_stack.transpose(1, 0, 2).reshape(w_out.shape[0], n * w_out.shape[1])

    split = qkv_all.reshape(tokens, 3, HEADS, HD)
    queries = split[:, 0].transpose(1, 0, 2)
    keys = split[:, 1].transpose(1, 2, 0)
    values = split[:, 2].transpose(1, 0, 2)
    mid_a = 2 * rim + ((tokens - 2 * rim) // (2 * S * S)) * (S * S)
    gate = modulation[2]

    def tile_part(part_queries, part_in):
        return attend_project(part_queries, keys, values, w_out_full, part_in, gate)

    my_rows = lax.dynamic_index_in_dim(edge_table, lax.axis_index("face"), 0, keepdims=False)
    flips = my_rows[:, 2]
    routes = my_rows[:, 3]
    send_match = routes[None, :] == jnp.asarray(PARTNER_ROUTE, jnp.int32)[:, None]
    recv_match = routes[None, :] == jnp.arange(4, dtype=jnp.int32)[:, None]
    ramp = space_ramp.astype(jnp.float32)
    keep = ramp / (ramp + ramp[::-1])
    take = ramp[::-1] / (ramp + ramp[::-1])

    def strips_out(tile_out):
        part_tokens = tile_out.shape[0]
        part_frames = part_tokens // (S * S)
        _, send_table = strip_tables(part_frames)
        send_by_edge = jnp.where(flips[:, None] > 0, send_table[:, 1], send_table[:, 0])
        send_cells = jnp.sum(jnp.where(send_match[:, :, None], send_by_edge[None], 0), axis=1)
        send_cells = send_cells.reshape(-1)
        token_ids = jnp.arange(part_tokens, dtype=jnp.int32)
        pick = (send_cells[:, None] == token_ids[None, :]).astype(jnp.bfloat16)
        return jnp.dot(pick, tile_out, preferred_element_type=jnp.float32).astype(jnp.bfloat16)

    def strips_in(outgoing):
        strip_len = outgoing.shape[0] // 4
        arrived = []
        for route_id in range(4):
            sent = outgoing[route_id * strip_len : (route_id + 1) * strip_len]
            shift = -OFFSETS[route_id]
            arrived.append(
                lax.ppermute(sent, "face", [(i, (i + shift) % n) for i in range(n)])
            )
        return jnp.concatenate(arrived, axis=0)

    def space_blend(tile_out, arrived):
        part_tokens = tile_out.shape[0]
        part_frames = part_tokens // (S * S)
        recv_table, _ = strip_tables(part_frames)
        recv_cells = jnp.sum(jnp.where(recv_match[:, :, None], recv_table[None], 0), axis=1)
        recv_cells = recv_cells.reshape(-1)
        token_ids = jnp.arange(part_tokens, dtype=jnp.int32)
        place = (token_ids[:, None] == recv_cells[None, :]).astype(jnp.bfloat16)
        partner = jnp.dot(place, arrived, preferred_element_type=jnp.float32)
        dep = strip_depth(1)[:, None]
        cell = lax.broadcasted_iota(jnp.int32, (S * S, 1), 0)
        row, col = cell // S, cell % S
        near = (row == 0) | (row == S - 1) | (col == 0) | (col == S - 1)
        w_keep = jnp.where(near, keep[0], keep[1])
        w_take = jnp.where(near, take[0], take[1])
        grid_shape = (part_frames, S * S, tile_out.shape[1])
        own = tile_out.astype(jnp.float32).reshape(grid_shape)
        partner = partner.reshape(grid_shape)
        mixed = jnp.where(dep >= 0, w_keep * own + w_take * partner, own)
        return mixed.reshape(tile_out.shape).astype(jnp.bfloat16)

    tile_rim = tile_part(queries[:, : 2 * rim], block_in[: 2 * rim])
    outgoing_rim = strips_out(tile_rim)
    arrived_rim = strips_in(outgoing_rim)
    first_queries, outgoing_rim = lax.optimization_barrier(
        (queries[:, 2 * rim : mid_a], outgoing_rim)
    )
    tile_first = tile_part(first_queries, block_in[2 * rim : mid_a])
    arrived_rim, tile_first = lax.optimization_barrier((arrived_rim, tile_first))
    spaced_rim = space_blend(tile_rim, arrived_rim)
    low, high = lax.optimization_barrier((spaced_rim[:rim], spaced_rim[rim:]))
    count = lax.axis_size("tm")
    lower = lax.ppermute(high, "tm", [(i, i + 1) for i in range(count - 1)])
    upper = lax.ppermute(low, "tm", [(i + 1, i) for i in range(count - 1)])
    outgoing_first = strips_out(tile_first)
    arrived_first = strips_in(outgoing_first)
    second_queries, low, high, outgoing_first = lax.optimization_barrier(
        (queries[:, mid_a:], low, high, outgoing_first)
    )
    tile_second = tile_part(second_queries, block_in[mid_a:])
    lower, upper, arrived_first, tile_second = lax.optimization_barrier(
        (lower, upper, arrived_first, tile_second)
    )
    spaced_mid = jnp.concatenate(
        [
            space_blend(tile_first, arrived_first),
            space_blend(tile_second, strips_in(strips_out(tile_second))),
        ],
        axis=0,
    )

    span_id = lax.axis_index("tm")
    has_lower = span_id > 0
    has_upper = span_id < count - 1
    tramp = time_ramp.astype(jnp.float32)
    hold = tramp / (tramp + tramp[::-1])
    pass_ = tramp[::-1] / (tramp + tramp[::-1])
    blocks = (OVT, S * S, D)
    low_f = low.astype(jnp.float32).reshape(blocks)
    high_f = high.astype(jnp.float32).reshape(blocks)
    hold_low = hold[:, None, None]
    pass_low = pass_[:, None, None]
    hold_high = hold[::-1][:, None, None]
    pass_high = pass_[::-1][:, None, None]
    low_mix = jnp.where(
        has_lower, hold_low * low_f + pass_low * lower.astype(jnp.float32).reshape(blocks), low_f
    ).reshape(rim, D)
    high_mix = jnp.where(
        has_upper, hold_high * high_f + pass_high * upper.astype(jnp.float32).reshape(blocks), high_f
    ).reshape(rim, D)
    result = jnp.concatenate(
        [low_mix.astype(jnp.bfloat16), spaced_mid, high_mix.astype(jnp.bfloat16)], axis=0
    )
    return result.reshape(1, 1, tokens, D)


def solution(mesh):
    return jax.shard_map(
        per_device,
        mesh=mesh,
        in_specs=(
            P(("groups", "tm"), "face", None, None),
            P("groups", None),
            P("face", None),
            P(None, "face"),
            P(),
            P(),
            P(),
        ),
        out_specs=P(("groups", "tm"), "face", None, None),
        check_vma=False,
    )
```

```python
import math

import jax
import jax.numpy as jnp
import numpy as np
from jax import lax
from jax.experimental import pallas as pl
from jax.experimental.pallas import tpu as pltpu
from jax.sharding import PartitionSpec as P

D = 1152
HD = 72
HEADS = 8
S = 8
OVS = 2
OVT = 4
MID = S - 2 * OVS


NORM_EPS = 1e-06
OFFSETS = (1, -1, 2, -2)
PARTNER_ROUTE = (1, 0, 3, 2)


def modulate(block_in, modulation):
    values = block_in.astype(jnp.float32)
    center = jnp.mean(values, axis=-1, keepdims=True)
    spread = jnp.mean(jnp.square(values - center), axis=-1, keepdims=True)
    normed = (values - center) * lax.rsqrt(spread + NORM_EPS)
    return (normed * (1.0 + modulation[1]) + modulation[0]).astype(jnp.bfloat16)


HEADS_PER_STEP = 4


def attention_kernel(*refs):
    x_ref, g_ref, o_ref, acc_ref = refs[-4:]
    per_head = refs[:-4]
    step = pl.program_id(1)

    @pl.when(step == 0)
    def _():
        acc_ref[...] = jnp.zeros_like(acc_ref)

    total = None
    for j in range(HEADS_PER_STEP):
        q_ref, k_ref, v_ref, w_ref = per_head[4 * j : 4 * j + 4]
        scores = jnp.dot(q_ref[0], k_ref[0], preferred_element_type=jnp.float32) * (
            1.0 / math.sqrt(HD)
        )
        row_max = jnp.max(scores, axis=-1, keepdims=True)
        weights = jnp.exp(scores - row_max)
        row_sum = jnp.sum(weights, axis=-1, keepdims=True)
        probabilities = (weights * (1.0 / row_sum)).astype(jnp.bfloat16)
        mixed = jnp.dot(probabilities, v_ref[0], preferred_element_type=jnp.float32).astype(
            jnp.bfloat16
        )
        part = jnp.dot(mixed, w_ref[...], preferred_element_type=jnp.float32)
        total = part if total is None else total + part
    acc_ref[...] += total

    @pl.when(step == pl.num_programs(1) - 1)
    def _():
        o_ref[...] = (x_ref[...].astype(jnp.float32) + g_ref[...] * acc_ref[...]).astype(
            o_ref.dtype
        )


def attend_project(queries, keys, values, w_out_full, block_in, gate):
    heads, size, tokens = keys.shape
    chunk = queries.shape[1]
    width = block_in.shape[1]
    hb = HEADS_PER_STEP
    in_specs = []
    operands = []
    for j in range(hb):
        in_specs += [
            pl.BlockSpec((1, chunk, size), lambda i, h, j=j: (hb * h + j, i, 0)),
            pl.BlockSpec((1, size, tokens), lambda i, h, j=j: (hb * h + j, 0, 0)),
            pl.BlockSpec((1, tokens, size), lambda i, h, j=j: (hb * h + j, 0, 0)),
            pl.BlockSpec((size, width), lambda i, h, j=j: (hb * h + j, 0)),
        ]
        operands += [queries, keys, values, w_out_full]
    in_specs += [
        pl.BlockSpec((chunk, width), lambda i, h: (i, 0)),
        pl.BlockSpec((1, width), lambda i, h: (0, 0)),
    ]
    return pl.pallas_call(
        attention_kernel,
        grid=(1, heads // hb),
        in_specs=in_specs,
        out_specs=pl.BlockSpec((chunk, width), lambda i, h: (i, 0)),
        out_shape=jax.ShapeDtypeStruct(block_in.shape, block_in.dtype),
        scratch_shapes=[pltpu.VMEM((chunk, width), jnp.float32)],
        compiler_params=pltpu.CompilerParams(dimension_semantics=("arbitrary", "arbitrary")),
    )(*operands, block_in, gate.reshape(1, width))


def face_pieces(shard):
    n = lax.axis_size("face")
    me = lax.axis_index("face")

    def fetch(x, src_of):
        return lax.ppermute(x, "face", [(src_of(i), i) for i in range(n)])

    pieces = [(shard, me), (fetch(shard, lambda i: i ^ 1), me ^ 1)]
    for j in range(1, n // 2):
        far = fetch(shard, lambda i: (i + 2 * j) % n)
        pieces.append((far, (me + 2 * j) % n))
        pieces.append((fetch(far, lambda i: i ^ 1), ((me ^ 1) + 2 * j) % n))
    return pieces


def strip_tables(frames):
    frame, depth, pos = np.meshgrid(
        np.arange(frames), np.arange(OVS), np.arange(MID), indexing="ij"
    )

    def token(edge, d, t):
        row = (d, S - 1 - d, OVS + t, OVS + t)[edge]
        col = (OVS + t, OVS + t, d, S - 1 - d)[edge]
        return (frame * (S * S) + row * S + col).reshape(-1)

    recv = np.stack([token(e, depth, pos) for e in range(4)])
    send = np.stack(
        [[token(e, OVS - 1 - depth, pos if flip == 0 else MID - 1 - pos) for flip in range(2)]
         for e in range(4)]
    )
    return recv.astype(np.int32), send.astype(np.int32)


def strip_depth(frames):
    grid = np.full((S, S), -1, np.int32)
    for d in range(OVS):
        grid[d, OVS : S - OVS] = d
        grid[S - 1 - d, OVS : S - OVS] = d
        grid[OVS : S - OVS, d] = d
        grid[OVS : S - OVS, S - 1 - d] = d
    return np.tile(grid.reshape(-1), frames)


def per_device(latents, modulation, w_qkv, w_out, edge_table, space_ramp, time_ramp):
    block_in = latents[0, 0]
    tokens = block_in.shape[0]
    frames = tokens // (S * S)
    n = lax.axis_size("face")
    rows = w_qkv.shape[0]
    rim = OVT * S * S
    block_in = jnp.concatenate(
        [block_in[:rim], block_in[tokens - rim :], block_in[rim : tokens - rim]], axis=0
    )
    moved = modulate(block_in, modulation)
    if n == 4:
        me = lax.axis_index("face")
        core = me % 2

        def fetch(x, src_of):
            return lax.ppermute(x, "face", [(src_of(i), i) for i in range(n)])

        moved_chips = moved.reshape(tokens, 2, 2 * rows).transpose(1, 0, 2)

        def chip_weight(same_core, other_core):
            first = jnp.where(core == 0, same_core, other_core)
            second = jnp.where(core == 0, other_core, same_core)
            return jnp.concatenate([first, second], axis=0)

        def chip_part(chip, weight):
            return jnp.dot(
                lax.dynamic_index_in_dim(moved_chips, chip, 0, keepdims=False),
                weight,
                preferred_element_type=jnp.float32,
            )

        sib = fetch(w_qkv, lambda i: i ^ 1)
        far = fetch(w_qkv, lambda i: (i + 2) % n)
        local = chip_part(me // 2, chip_weight(w_qkv, sib))
        local, far = lax.optimization_barrier((local, far))
        fwd = fetch(far, lambda i: i ^ 1)
        qkv_sums = local + chip_part(1 - me // 2, chip_weight(far, fwd))
        w_out_late, _ = lax.optimization_barrier((w_out, (far, fwd)))
    else:
        qkv_pieces = face_pieces(w_qkv)
        w_out_late, _ = lax.optimization_barrier((w_out, [piece for piece, _ in qkv_pieces]))
        qkv_stack = jnp.zeros((n,) + w_qkv.shape, w_qkv.dtype)
        for piece, index in qkv_pieces:
            qkv_stack = lax.dynamic_update_index_in_dim(qkv_stack, piece, index, 0)
        w_qkv_full = qkv_stack.reshape(n * rows, w_qkv.shape[1])
        qkv_sums = jnp.dot(moved, w_qkv_full, preferred_element_type=jnp.float32)
    qkv_all = qkv_sums.astype(jnp.bfloat16)

    out_stack = jnp.zeros((n,) + w_out.shape, w_out.dtype)
    for piece, index in face_pieces(w_out_late):
        out_stack = lax.dynamic_update_index_in_dim(out_stack, piece, index, 0)
    w_out_full = out_stack.transpose(1, 0, 2).reshape(w_out.shape[0], n * w_out.shape[1])

    split = qkv_all.reshape(tokens, 3, HEADS, HD)
    queries = split[:, 0].transpose(1, 0, 2)
    keys = split[:, 1].transpose(1, 2, 0)
    values = split[:, 2].transpose(1, 0, 2)
    mid_a = 2 * rim + ((tokens - 2 * rim) // (2 * S * S)) * (S * S)
    gate = modulation[2]

    def tile_part(part_queries, part_in):
        return attend_project(part_queries, keys, values, w_out_full, part_in, gate)

    my_rows = lax.dynamic_index_in_dim(edge_table, lax.axis_index("face"), 0, keepdims=False)
    flips = my_rows[:, 2]
    routes = my_rows[:, 3]
    send_match = routes[None, :] == jnp.asarray(PARTNER_ROUTE, jnp.int32)[:, None]
    recv_match = routes[None, :] == jnp.arange(4, dtype=jnp.int32)[:, None]
    ramp = space_ramp.astype(jnp.float32)
    keep = ramp / (ramp + ramp[::-1])
    take = ramp[::-1] / (ramp + ramp[::-1])

    def strips_out(tile_out):
        part_tokens = tile_out.shape[0]
        part_frames = part_tokens // (S * S)
        _, send_table = strip_tables(part_frames)
        send_by_edge = jnp.where(flips[:, None] > 0, send_table[:, 1], send_table[:, 0])
        send_cells = jnp.sum(jnp.where(send_match[:, :, None], send_by_edge[None], 0), axis=1)
        send_cells = send_cells.reshape(-1)
        token_ids = jnp.arange(part_tokens, dtype=jnp.int32)
        pick = (send_cells[:, None] == token_ids[None, :]).astype(jnp.bfloat16)
        return jnp.dot(pick, tile_out, preferred_element_type=jnp.float32).astype(jnp.bfloat16)

    def strips_in(outgoing):
        strip_len = outgoing.shape[0] // 4
        arrived = []
        for route_id in range(4):
            sent = outgoing[route_id * strip_len : (route_id + 1) * strip_len]
            shift = -OFFSETS[route_id]
            arrived.append(
                lax.ppermute(sent, "face", [(i, (i + shift) % n) for i in range(n)])
            )
        return jnp.concatenate(arrived, axis=0)

    def space_blend(tile_out, arrived):
        part_tokens = tile_out.shape[0]
        part_frames = part_tokens // (S * S)
        recv_table, _ = strip_tables(part_frames)
        recv_cells = jnp.sum(jnp.where(recv_match[:, :, None], recv_table[None], 0), axis=1)
        recv_cells = recv_cells.reshape(-1)
        token_ids = jnp.arange(part_tokens, dtype=jnp.int32)
        place = (token_ids[:, None] == recv_cells[None, :]).astype(jnp.bfloat16)
        partner = jnp.dot(place, arrived, preferred_element_type=jnp.float32)
        dep = strip_depth(1)[:, None]
        cell = lax.broadcasted_iota(jnp.int32, (S * S, 1), 0)
        row, col = cell // S, cell % S
        near = (row == 0) | (row == S - 1) | (col == 0) | (col == S - 1)
        w_keep = jnp.where(near, keep[0], keep[1])
        w_take = jnp.where(near, take[0], take[1])
        grid_shape = (part_frames, S * S, tile_out.shape[1])
        own = tile_out.astype(jnp.float32).reshape(grid_shape)
        partner = partner.reshape(grid_shape)
        mixed = jnp.where(dep >= 0, w_keep * own + w_take * partner, own)
        return mixed.reshape(tile_out.shape).astype(jnp.bfloat16)

    tile_rim = tile_part(queries[:, : 2 * rim], block_in[: 2 * rim])
    outgoing_rim = strips_out(tile_rim)
    arrived_rim = strips_in(outgoing_rim)
    first_queries, outgoing_rim = lax.optimization_barrier(
        (queries[:, 2 * rim : mid_a], outgoing_rim)
    )
    tile_first = tile_part(first_queries, block_in[2 * rim : mid_a])
    arrived_rim, tile_first = lax.optimization_barrier((arrived_rim, tile_first))
    spaced_rim = space_blend(tile_rim, arrived_rim)
    low, high = lax.optimization_barrier((spaced_rim[:rim], spaced_rim[rim:]))
    count = lax.axis_size("tm")
    lower = lax.ppermute(high, "tm", [(i, i + 1) for i in range(count - 1)])
    upper = lax.ppermute(low, "tm", [(i + 1, i) for i in range(count - 1)])
    outgoing_first = strips_out(tile_first)
    arrived_first = strips_in(outgoing_first)
    second_queries, low, high, outgoing_first = lax.optimization_barrier(
        (queries[:, mid_a:], low, high, outgoing_first)
    )
    tile_second = tile_part(second_queries, block_in[mid_a:])
    lower, upper, arrived_first, tile_second = lax.optimization_barrier(
        (lower, upper, arrived_first, tile_second)
    )
    spaced_mid = jnp.concatenate(
        [
            space_blend(tile_first, arrived_first),
            space_blend(tile_second, strips_in(strips_out(tile_second))),
        ],
        axis=0,
    )

    span_id = lax.axis_index("tm")
    has_lower = span_id > 0
    has_upper = span_id < count - 1
    tramp = time_ramp.astype(jnp.float32)
    hold = tramp / (tramp + tramp[::-1])
    pass_ = tramp[::-1] / (tramp + tramp[::-1])
    blocks = (OVT, S * S, D)
    low_f = low.astype(jnp.float32).reshape(blocks)
    high_f = high.astype(jnp.float32).reshape(blocks)
    hold_low = hold[:, None, None]
    pass_low = pass_[:, None, None]
    hold_high = hold[::-1][:, None, None]
    pass_high = pass_[::-1][:, None, None]
    low_mix = jnp.where(
        has_lower, hold_low * low_f + pass_low * lower.astype(jnp.float32).reshape(blocks), low_f
    ).reshape(rim, D)
    high_mix = jnp.where(
        has_upper, hold_high * high_f + pass_high * upper.astype(jnp.float32).reshape(blocks), high_f
    ).reshape(rim, D)
    result = jnp.concatenate(
        [low_mix.astype(jnp.bfloat16), spaced_mid, high_mix.astype(jnp.bfloat16)], axis=0
    )
    return result.reshape(1, 1, tokens, D)


def solution(mesh):
    return jax.shard_map(
        per_device,
        mesh=mesh,
        in_specs=(
            P(("groups", "tm"), "face", None, None),
            P("groups", None),
            P("face", None),
            P(None, "face"),
            P(),
            P(),
            P(),
        ),
        out_specs=P(("groups", "tm"), "face", None, None),
        check_vma=False,
    )
```

```python
import math

import jax
import jax.numpy as jnp
import numpy as np
from jax import lax
from jax.experimental import pallas as pl
from jax.experimental.pallas import tpu as pltpu
from jax.sharding import PartitionSpec as P

D = 1152
HD = 72
HEADS = 8
S = 8
OVS = 2
OVT = 4
MID = S - 2 * OVS


NORM_EPS = 1e-06
OFFSETS = (1, -1, 2, -2)
PARTNER_ROUTE = (1, 0, 3, 2)


def modulate(block_in, modulation):
    values = block_in.astype(jnp.float32)
    center = jnp.mean(values, axis=-1, keepdims=True)
    spread = jnp.mean(jnp.square(values - center), axis=-1, keepdims=True)
    normed = (values - center) * lax.rsqrt(spread + NORM_EPS)
    return (normed * (1.0 + modulation[1]) + modulation[0]).astype(jnp.bfloat16)


HEADS_PER_STEP = 4


def attention_kernel(*refs):
    x_ref, g_ref, o_ref, acc_ref = refs[-4:]
    per_head = refs[:-4]
    step = pl.program_id(1)

    @pl.when(step == 0)
    def _():
        acc_ref[...] = jnp.zeros_like(acc_ref)

    total = None
    for j in range(HEADS_PER_STEP):
        q_ref, k_ref, v_ref, w_ref = per_head[4 * j : 4 * j + 4]
        scores = jnp.dot(q_ref[0], k_ref[0], preferred_element_type=jnp.float32) * (
            1.0 / math.sqrt(HD)
        )
        row_max = jnp.max(scores, axis=-1, keepdims=True)
        weights = jnp.exp(scores - row_max)
        row_sum = jnp.sum(weights, axis=-1, keepdims=True)
        probabilities = (weights * (1.0 / row_sum)).astype(jnp.bfloat16)
        mixed = jnp.dot(probabilities, v_ref[0], preferred_element_type=jnp.float32).astype(
            jnp.bfloat16
        )
        part = jnp.dot(mixed, w_ref[...], preferred_element_type=jnp.float32)
        total = part if total is None else total + part
    acc_ref[...] += total

    @pl.when(step == pl.num_programs(1) - 1)
    def _():
        o_ref[...] = (x_ref[...].astype(jnp.float32) + g_ref[...] * acc_ref[...]).astype(
            o_ref.dtype
        )


def attend_project(queries, keys, values, w_out_full, block_in, gate, chunk=None):
    heads, size, tokens = keys.shape
    chunk = queries.shape[1] if chunk is None else chunk
    width = block_in.shape[1]
    hb = HEADS_PER_STEP
    in_specs = []
    operands = []
    for j in range(hb):
        in_specs += [
            pl.BlockSpec((1, chunk, size), lambda i, h, j=j: (hb * h + j, i, 0)),
            pl.BlockSpec((1, size, tokens), lambda i, h, j=j: (hb * h + j, 0, 0)),
            pl.BlockSpec((1, tokens, size), lambda i, h, j=j: (hb * h + j, 0, 0)),
            pl.BlockSpec((size, width), lambda i, h, j=j: (hb * h + j, 0)),
        ]
        operands += [queries, keys, values, w_out_full]
    in_specs += [
        pl.BlockSpec((chunk, width), lambda i, h: (i, 0)),
        pl.BlockSpec((1, width), lambda i, h: (0, 0)),
    ]
    return pl.pallas_call(
        attention_kernel,
        grid=(1, heads // hb),
        in_specs=in_specs,
        out_specs=pl.BlockSpec((chunk, width), lambda i, h: (i, 0)),
        out_shape=jax.ShapeDtypeStruct((chunk, width), block_in.dtype),
        scratch_shapes=[pltpu.VMEM((chunk, width), jnp.float32)],
        compiler_params=pltpu.CompilerParams(dimension_semantics=("arbitrary", "arbitrary")),
    )(*operands, block_in, gate.reshape(1, width))


def face_pieces(shard):
    n = lax.axis_size("face")
    me = lax.axis_index("face")

    def fetch(x, src_of):
        return lax.ppermute(x, "face", [(src_of(i), i) for i in range(n)])

    pieces = [(shard, me), (fetch(shard, lambda i: i ^ 1), me ^ 1)]
    for j in range(1, n // 2):
        far = fetch(shard, lambda i: (i + 2 * j) % n)
        pieces.append((far, (me + 2 * j) % n))
        pieces.append((fetch(far, lambda i: i ^ 1), ((me ^ 1) + 2 * j) % n))
    return pieces


def strip_tables(frames):
    frame, depth, pos = np.meshgrid(
        np.arange(frames), np.arange(OVS), np.arange(MID), indexing="ij"
    )

    def token(edge, d, t):
        row = (d, S - 1 - d, OVS + t, OVS + t)[edge]
        col = (OVS + t, OVS + t, d, S - 1 - d)[edge]
        return (frame * (S * S) + row * S + col).reshape(-1)

    recv = np.stack([token(e, depth, pos) for e in range(4)])
    send = np.stack(
        [[token(e, OVS - 1 - depth, pos if flip == 0 else MID - 1 - pos) for flip in range(2)]
         for e in range(4)]
    )
    return recv.astype(np.int32), send.astype(np.int32)


def strip_depth(frames):
    grid = np.full((S, S), -1, np.int32)
    for d in range(OVS):
        grid[d, OVS : S - OVS] = d
        grid[S - 1 - d, OVS : S - OVS] = d
        grid[OVS : S - OVS, d] = d
        grid[OVS : S - OVS, S - 1 - d] = d
    return np.tile(grid.reshape(-1), frames)


def per_device(latents, modulation, w_qkv, w_out, edge_table, space_ramp, time_ramp):
    block_in = latents[0, 0]
    tokens = block_in.shape[0]
    frames = tokens // (S * S)
    n = lax.axis_size("face")
    rows = w_qkv.shape[0]
    rim = OVT * S * S
    block_in = jnp.concatenate(
        [block_in[:rim], block_in[tokens - rim :], block_in[rim : tokens - rim]], axis=0
    )
    moved = modulate(block_in, modulation)
    if n == 4:
        me = lax.axis_index("face")
        core = me % 2

        def fetch(x, src_of):
            return lax.ppermute(x, "face", [(src_of(i), i) for i in range(n)])

        moved_chips = moved.reshape(tokens, 2, 2 * rows).transpose(1, 0, 2)

        def chip_weight(same_core, other_core):
            stack = jnp.zeros((2,) + w_qkv.shape, w_qkv.dtype)
            stack = lax.dynamic_update_index_in_dim(stack, same_core, core, 0)
            stack = lax.dynamic_update_index_in_dim(stack, other_core, 1 - core, 0)
            return stack.reshape(2 * rows, w_qkv.shape[1])

        def chip_part(chip, weight):
            return jnp.dot(
                lax.dynamic_index_in_dim(moved_chips, chip, 0, keepdims=False),
                weight,
                preferred_element_type=jnp.float32,
            )

        sib = fetch(w_qkv, lambda i: i ^ 1)
        far = fetch(w_qkv, lambda i: (i + 2) % n)
        local = chip_part(me // 2, chip_weight(w_qkv, sib))
        local, far = lax.optimization_barrier((local, far))
        fwd = fetch(far, lambda i: i ^ 1)
        qkv_sums = local + chip_part(1 - me // 2, chip_weight(far, fwd))
        w_out_late, _ = lax.optimization_barrier((w_out, (far, fwd)))
    else:
        qkv_pieces = face_pieces(w_qkv)
        w_out_late, _ = lax.optimization_barrier((w_out, [piece for piece, _ in qkv_pieces]))
        qkv_stack = jnp.zeros((n,) + w_qkv.shape, w_qkv.dtype)
        for piece, index in qkv_pieces:
            qkv_stack = lax.dynamic_update_index_in_dim(qkv_stack, piece, index, 0)
        w_qkv_full = qkv_stack.reshape(n * rows, w_qkv.shape[1])
        qkv_sums = jnp.dot(moved, w_qkv_full, preferred_element_type=jnp.float32)
    qkv_all = qkv_sums.astype(jnp.bfloat16)

    out_stack = jnp.zeros((n,) + w_out.shape, w_out.dtype)
    for piece, index in face_pieces(w_out_late):
        out_stack = lax.dynamic_update_index_in_dim(out_stack, piece, index, 0)
    w_out_full = out_stack.transpose(1, 0, 2).reshape(w_out.shape[0], n * w_out.shape[1])

    split = qkv_all.reshape(tokens, 3, HEADS, HD)
    queries = split[:, 0].transpose(1, 0, 2)
    keys = split[:, 1].transpose(1, 2, 0)
    values = split[:, 2].transpose(1, 0, 2)
    mid_a = 2 * rim + ((tokens - 2 * rim) // (2 * S * S)) * (S * S)
    gate = modulation[2]

    def tile_part(part_queries, part_in):
        return attend_project(part_queries, keys, values, w_out_full, part_in, gate)

    my_rows = lax.dynamic_index_in_dim(edge_table, lax.axis_index("face"), 0, keepdims=False)
    flips = my_rows[:, 2]
    routes = my_rows[:, 3]
    send_match = routes[None, :] == jnp.asarray(PARTNER_ROUTE, jnp.int32)[:, None]
    recv_match = routes[None, :] == jnp.arange(4, dtype=jnp.int32)[:, None]
    ramp = space_ramp.astype(jnp.float32)
    keep = ramp / (ramp + ramp[::-1])
    take = ramp[::-1] / (ramp + ramp[::-1])

    def strips_out(tile_out):
        part_tokens = tile_out.shape[0]
        part_frames = part_tokens // (S * S)
        _, send_table = strip_tables(part_frames)
        send_by_edge = jnp.where(flips[:, None] > 0, send_table[:, 1], send_table[:, 0])
        send_cells = jnp.sum(jnp.where(send_match[:, :, None], send_by_edge[None], 0), axis=1)
        send_cells = send_cells.reshape(-1)
        token_ids = jnp.arange(part_tokens, dtype=jnp.int32)
        pick = (send_cells[:, None] == token_ids[None, :]).astype(jnp.bfloat16)
        return jnp.dot(pick, tile_out, preferred_element_type=jnp.float32).astype(jnp.bfloat16)

    def strips_in(outgoing):
        strip_len = outgoing.shape[0] // 4
        arrived = []
        for route_id in range(4):
            sent = outgoing[route_id * strip_len : (route_id + 1) * strip_len]
            shift = -OFFSETS[route_id]
            arrived.append(
                lax.ppermute(sent, "face", [(i, (i + shift) % n) for i in range(n)])
            )
        return jnp.concatenate(arrived, axis=0)

    def space_blend(tile_out, arrived):
        part_tokens = tile_out.shape[0]
        part_frames = part_tokens // (S * S)
        recv_table, _ = strip_tables(part_frames)
        recv_cells = jnp.sum(jnp.where(recv_match[:, :, None], recv_table[None], 0), axis=1)
        recv_cells = recv_cells.reshape(-1)
        token_ids = jnp.arange(part_tokens, dtype=jnp.int32)
        place = (token_ids[:, None] == recv_cells[None, :]).astype(jnp.bfloat16)
        partner = jnp.dot(place, arrived, preferred_element_type=jnp.float32)
        dep = strip_depth(1)[:, None]
        cell = lax.broadcasted_iota(jnp.int32, (S * S, 1), 0)
        row, col = cell // S, cell % S
        near = (row == 0) | (row == S - 1) | (col == 0) | (col == S - 1)
        w_keep = jnp.where(near, keep[0], keep[1])
        w_take = jnp.where(near, take[0], take[1])
        grid_shape = (part_frames, S * S, tile_out.shape[1])
        own = tile_out.astype(jnp.float32).reshape(grid_shape)
        partner = partner.reshape(grid_shape)
        mixed = jnp.where(dep >= 0, w_keep * own + w_take * partner, own)
        return mixed.reshape(tile_out.shape).astype(jnp.bfloat16)

    tile_rim = attend_project(queries, keys, values, w_out_full, block_in, gate, 2 * rim)
    outgoing_rim = strips_out(tile_rim)
    arrived_rim = strips_in(outgoing_rim)
    first_queries, outgoing_rim = lax.optimization_barrier(
        (queries[:, 2 * rim : mid_a], outgoing_rim)
    )
    tile_first = tile_part(first_queries, block_in[2 * rim : mid_a])
    arrived_rim, tile_first = lax.optimization_barrier((arrived_rim, tile_first))
    spaced_rim = space_blend(tile_rim, arrived_rim)
    low, high = lax.optimization_barrier((spaced_rim[:rim], spaced_rim[rim:]))
    count = lax.axis_size("tm")
    lower = lax.ppermute(high, "tm", [(i, i + 1) for i in range(count - 1)])
    upper = lax.ppermute(low, "tm", [(i + 1, i) for i in range(count - 1)])
    outgoing_first = strips_out(tile_first)
    arrived_first = strips_in(outgoing_first)
    second_queries, low, high, outgoing_first = lax.optimization_barrier(
        (queries[:, mid_a:], low, high, outgoing_first)
    )
    tile_second = tile_part(second_queries, block_in[mid_a:])
    lower, upper, arrived_first, tile_second = lax.optimization_barrier(
        (lower, upper, arrived_first, tile_second)
    )
    spaced_mid = jnp.concatenate(
        [
            space_blend(tile_first, arrived_first),
            space_blend(tile_second, strips_in(strips_out(tile_second))),
        ],
        axis=0,
    )

    span_id = lax.axis_index("tm")
    has_lower = span_id > 0
    has_upper = span_id < count - 1
    tramp = time_ramp.astype(jnp.float32)
    hold = tramp / (tramp + tramp[::-1])
    pass_ = tramp[::-1] / (tramp + tramp[::-1])
    blocks = (OVT, S * S, D)
    low_f = low.astype(jnp.float32).reshape(blocks)
    high_f = high.astype(jnp.float32).reshape(blocks)
    hold_low = hold[:, None, None]
    pass_low = pass_[:, None, None]
    hold_high = hold[::-1][:, None, None]
    pass_high = pass_[::-1][:, None, None]
    low_mix = jnp.where(
        has_lower, hold_low * low_f + pass_low * lower.astype(jnp.float32).reshape(blocks), low_f
    ).reshape(rim, D)
    high_mix = jnp.where(
        has_upper, hold_high * high_f + pass_high * upper.astype(jnp.float32).reshape(blocks), high_f
    ).reshape(rim, D)
    result = jnp.concatenate(
        [low_mix.astype(jnp.bfloat16), spaced_mid, high_mix.astype(jnp.bfloat16)], axis=0
    )
    return result.reshape(1, 1, tokens, D)


def solution(mesh):
    return jax.shard_map(
        per_device,
        mesh=mesh,
        in_specs=(
            P(("groups", "tm"), "face", None, None),
            P("groups", None),
            P("face", None),
            P(None, "face"),
            P(),
            P(),
            P(),
        ),
        out_specs=P(("groups", "tm"), "face", None, None),
        check_vma=False,
    )
```
